32 devices in a mesh: layer: 4 (over x, core), row: 4 (over z), col: 2 (over y).
Axes of the slice: x: 2, y: 2, z: 4, core: 2. Of those that a mesh axis runs over, the one named last changes fastest.
Arguments:
- tensor: bfloat16 [512, 16, 12288], P('row', 'col', 'layer'), may hold values from -6 to 6
- tensor_pattern: int32 [16, 192], P('col', 'layer'), may hold values 0 or 1
- green: bfloat16 [12288, 12288], P(('layer', 'col'), 'row'), may hold values from -0.15625 to 0.15625
- green_pattern: int32 [192, 192], P(('layer', 'col'), 'row'), may hold values from 0 to 1, as said below
Outputs:
- product: bfloat16 [512, 16, 12288], P('layer', 'col', 'row')
The draws below stay inside these ranges and needn't reach their ends.
Inputs may be any that keep to these rules, and one draw needn't show every extreme that they name: `green_pattern`: in every aligned tile of 24 block rows by 48 block columns at most 48 entries are 1, and in every aligned band of 24 block rows some tile holds exactly 48.
All inputs are finite; a program needn't handle non-finite values. No bound on the sum of `tensor_pattern` on one device may be relied on, other than what follows from the above.
Results may differ from the reference program's by a relative error of at most 0.001.
Values may be sent and summed in bfloat16 or wider, within the bound.
No kernel may reach another device: no remote copies, remote signals or barrier semaphores. Data moves between devices by JAX's collectives and lax.ppermute only.
A program may use at most 320 MiB of HBM per device.

```python
import jax
import jax.numpy as jnp
from jax import lax

NAO = 12288
BLK = 64
RIB = 512
MU_W = 16
CAP = 48
NBLK = 192
TILE_ROWS = 24
TILE_COLS = 48


def draw_green_pattern(key, part):
    tile_area = TILE_ROWS * TILE_COLS
    band_rows = NBLK // TILE_ROWS
    band_cols = NBLK // TILE_COLS
    count_key, score_key = jax.random.split(key)
    counts = jax.random.randint(count_key, (band_rows, band_cols), 1, CAP // 2 + 1)
    first_col = jnp.arange(band_rows) * TILE_ROWS // TILE_COLS
    on_diagonal = jnp.arange(band_cols)[None, :] == first_col[:, None]
    counts = jnp.where(on_diagonal, CAP, counts)
    scores = jax.random.randint(score_key, (band_rows, band_cols, tile_area), 0, 2 ** 20) * tile_area + jnp.arange(tile_area)
    rank_order = jnp.argsort(jnp.argsort(scores, axis=2), axis=2)
    pattern_ones = (rank_order < counts[:, :, None]).astype(jnp.int32)
    return pattern_ones.reshape(band_rows, band_cols, TILE_ROWS, TILE_COLS).transpose(0, 2, 1, 3).reshape(NBLK, NBLK)


def set_ends(array, rng, smallest, high):
    shape = array.shape
    spot = [jax.random.randint(jax.random.fold_in(rng, axis), (), 0, shape[axis]) for axis in range(len(shape))]
    array = array.at[tuple(spot)].set(smallest)
    longest = shape.index(max(shape))
    spot[longest] = (spot[longest] + 1) % shape[longest]
    return array.at[tuple(spot)].set(high)


def shard_levels(stream_key, dims, cuts, low, largest):
    def one(dim, shards_of):
        draws = jax.random.uniform(jax.random.fold_in(jax.random.fold_in(stream_key, 6), dim), (shards_of,), jnp.float32, low / len(cuts), largest / len(cuts))
        return jnp.repeat(jnp.exp(draws), dims[dim] // shards_of).reshape((-1,) + (1,) * (len(dims) - dim - 1))

    gain = one(*cuts[0])
    for cut in cuts[1:]:
        gain = gain * one(*cut)
    return gain


def scatter_about(own_key, shape, spread, bound, cuts=(), held_as=jnp.bfloat16):
    gain = shard_levels(own_key, shape, cuts, -0.22, 0.18) if cuts else 1.0
    entries = jax.random.normal(own_key, shape, jnp.float32) * spread * gain
    return jnp.minimum(jnp.maximum(entries, -bound), bound).astype(held_as)


def setup_inputs(seed: int = 0) -> dict:
    keys = jax.random.split(jax.random.key(seed), 5)
    tensor = scatter_about(keys[0], (RIB, MU_W, NAO), 1.0, 6.0, ((0, 4), (1, 2), (2, 4)))
    tensor_pattern = set_ends((jax.random.randint(keys[1], (MU_W, NBLK), 0, 2) < 1).astype(jnp.int32), jax.random.fold_in(keys[1], 1), 0, 1)
    green = scatter_about(keys[2], (NAO, NAO), (NAO // 10) ** -0.5, 0.15625, ((0, 8), (1, 4)))
    green_pattern = draw_green_pattern(jax.random.fold_in(keys[4], 71), 0)
    return dict(tensor=tensor, tensor_pattern=tensor_pattern, green=green, green_pattern=green_pattern)


def reference(tensor, tensor_pattern, green, green_pattern):
    tensor_mask = jnp.repeat(tensor_pattern, BLK, axis=1).astype(tensor.dtype)
    masked = (tensor * tensor_mask[None, :, :]).reshape(RIB * MU_W, NAO)
    green_mask = green_pattern.astype(green.dtype)[:, None, :, None]
    green_masked = (green.reshape(NBLK, BLK, NBLK, BLK) * green_mask).reshape(NAO, NAO)
    product = jnp.dot(masked.astype(jnp.float32), green_masked.astype(jnp.float32), precision=lax.Precision.HIGHEST, preferred_element_type=jnp.float32)
    return product.astype(jnp.bfloat16).reshape(RIB, MU_W, NAO)
```

```python
import jax
import jax.numpy as jnp
from jax import lax
from jax.sharding import PartitionSpec as P

BLK = 64
CAP = 48


def passed_along(value, axis, by):
    length = lax.axis_size(axis)
    return lax.ppermute(value, axis, [(i, (i + by) % length) for i in range(length)])


def cannon_per_device(tensor, tensor_pattern, green, green_pattern):
    row_count = lax.axis_size("row")
    col_count = lax.axis_size("col")
    col_bits = col_count.bit_length() - 1
    row_index = lax.axis_index("row")
    col_index = lax.axis_index("col")
    odd_row = row_index % 2 == 1
    half_row = row_index // 2
    ri_local, mu_local, nu_local = tensor.shape
    width = nu_local // row_count
    tensor_mask = jnp.repeat(tensor_pattern, BLK, axis=1).astype(jnp.bfloat16)
    masked = tensor * tensor_mask[None, :, :]
    left_block = lax.all_to_all(masked, "row", split_axis=2, concat_axis=0, tiled=True)
    for bit_number in range(col_bits):
        arrived = passed_along(left_block, "row", -(2 << bit_number))
        left_block = jnp.where(col_index >> bit_number & 1 == 1, arrived, left_block)
    ri_total = left_block.shape[0]
    all_rows = ri_total * mu_local
    left_block = left_block.reshape(all_rows, width)
    tile_rows, tile_cols = green_pattern.shape
    green_mask = green_pattern.astype(jnp.bfloat16)[:, None, :, None]
    green_tile = (green.reshape(tile_rows, BLK, tile_cols, BLK) * green_mask).reshape(
        tile_rows * BLK, tile_cols * BLK
    )
    green_state = green_tile
    for bit_number in range(col_bits):
        arrived = passed_along(green_state, "col", -(1 << bit_number))
        green_state = jnp.where(half_row >> bit_number & 1 == 1, arrived, green_state)

    def advance(current_state):
        arrived_state = passed_along(current_state, "col", -1)
        return (arrived_state, arrived_state)

    def shift_left(block_now):
        return passed_along(block_now, "row", -1)

    def pair_turn(state_now, shift_last):
        product_sum, block_now, current_state, current = state_now
        green_half = jnp.where(odd_row, current[width:], current[:width])
        product_sum = product_sum + jnp.dot(
            block_now, green_half, preferred_element_type=jnp.float32
        )
        block_now = shift_left(block_now)
        previous = current
        current_state, current = advance(current_state)
        green_half = jnp.where(odd_row, current[:width], previous[width:])
        product_sum = product_sum + jnp.dot(
            block_now, green_half, preferred_element_type=jnp.float32
        )
        if shift_last:
            block_now = shift_left(block_now)
        return (product_sum, block_now, current_state, current)

    start = (
        jnp.zeros((all_rows, tile_cols * BLK), jnp.float32),
        left_block,
        green_state,
        green_state,
    )
    state_now = lax.fori_loop(
        0, col_count - 1, lambda turn_index, state_before: pair_turn(state_before, True), start
    )
    state_now = pair_turn(state_now, False)
    layer_terms = state_now[0].reshape(ri_total, mu_local, tile_cols * BLK)
    return lax.psum_scatter(layer_terms, "layer", scatter_dimension=0, tiled=True).astype(
        jnp.bfloat16
    )


def transposed(value, size):
    return lax.ppermute(
        value,
        ("layer", "row"),
        [(a * size + b, b * size + a) for a in range(size) for b in range(size)],
    )


def compressed_tile(green, green_pattern):
    tile_rows, tile_cols = green_pattern.shape
    cap = min(CAP, tile_rows * tile_cols)
    flat = green_pattern.reshape(-1)
    (spots,) = jnp.nonzero(flat != 0, size=cap, fill_value=0)
    valid = jnp.arange(cap) < jnp.sum(flat != 0)
    block_row = spots // tile_cols
    block_col = spots % tile_cols
    blocks = green.reshape(tile_rows, BLK, tile_cols, BLK)[block_row, :, block_col, :]
    scale = jnp.where(valid, flat[spots], 0).astype(jnp.bfloat16)
    blocks = blocks * scale[:, None, None]
    return blocks, block_row, block_col


def per_device(tensor, tensor_pattern, green, green_pattern):
    layer_count = lax.axis_size("layer")
    row_count = lax.axis_size("row")
    if layer_count != row_count:
        return cannon_per_device(tensor, tensor_pattern, green, green_pattern)
    ri_local, mu_local, nu_local = tensor.shape
    tile_rows, tile_cols = green_pattern.shape
    tensor_mask = jnp.repeat(tensor_pattern, BLK, axis=1).astype(jnp.bfloat16)
    masked = tensor * tensor_mask[None, :, :]
    full_rows = lax.all_gather(masked, "layer", axis=2, tiled=True)
    nao = full_rows.shape[2]
    blocks, block_row, block_col = compressed_tile(green, green_pattern)
    band_blocks = transposed(lax.all_gather(blocks, ("layer", "col"), axis=0), row_count)
    band_rows = transposed(lax.all_gather(block_row, ("layer", "col"), axis=0), row_count)
    band_cols = transposed(lax.all_gather(block_col, ("layer", "col"), axis=0), row_count)
    band_count = band_blocks.shape[0]
    band_width = tile_rows * BLK
    rows_all = full_rows.reshape(ri_local * mu_local, nao)

    def add_band(band, total):
        dense = jnp.zeros((tile_rows, BLK, tile_cols, BLK), jnp.bfloat16)
        dense = dense.at[band_rows[band], :, band_cols[band], :].add(band_blocks[band])
        dense = dense.reshape(band_width, tile_cols * BLK)
        rows = lax.dynamic_slice_in_dim(rows_all, band * band_width, band_width, axis=1)
        return total + jnp.dot(rows, dense, preferred_element_type=jnp.float32)

    total = jnp.zeros((ri_local * mu_local, tile_cols * BLK), jnp.float32)
    total = lax.fori_loop(0, band_count, add_band, total)
    product = total.astype(jnp.bfloat16)
    product = product.reshape(ri_local, mu_local, tile_cols * BLK)
    return transposed(product, row_count)


def solution(mesh):
    in_specs = (
        P("row", "col", "layer"),
        P("col", "layer"),
        P(("layer", "col"), "row"),
        P(("layer", "col"), "row"),
    )
    out_specs = P("layer", "col", "row")
    return jax.shard_map(
        per_device, mesh=mesh, in_specs=in_specs, out_specs=out_specs, check_vma=False
    )
```

```python
import jax
import jax.numpy as jnp
from jax import lax
from jax.experimental import pallas as pl
from jax.experimental.pallas import tpu as pltpu
from jax.sharding import PartitionSpec as P

BLK = 64
CAP = 48
LANE = 128
ROW_CHUNK = 256


def passed_along(value, axis, by):
    length = lax.axis_size(axis)
    return lax.ppermute(value, axis, [(i, (i + by) % length) for i in range(length)])


def cannon_per_device(tensor, tensor_pattern, green, green_pattern):
    row_count = lax.axis_size("row")
    col_count = lax.axis_size("col")
    col_bits = col_count.bit_length() - 1
    row_index = lax.axis_index("row")
    col_index = lax.axis_index("col")
    odd_row = row_index % 2 == 1
    half_row = row_index // 2
    ri_local, mu_local, nu_local = tensor.shape
    width = nu_local // row_count
    tensor_mask = jnp.repeat(tensor_pattern, BLK, axis=1).astype(jnp.bfloat16)
    masked = tensor * tensor_mask[None, :, :]
    left_block = lax.all_to_all(masked, "row", split_axis=2, concat_axis=0, tiled=True)
    for bit_number in range(col_bits):
        arrived = passed_along(left_block, "row", -(2 << bit_number))
        left_block = jnp.where(col_index >> bit_number & 1 == 1, arrived, left_block)
    ri_total = left_block.shape[0]
    all_rows = ri_total * mu_local
    left_block = left_block.reshape(all_rows, width)
    tile_rows, tile_cols = green_pattern.shape
    green_mask = green_pattern.astype(jnp.bfloat16)[:, None, :, None]
    green_tile = (green.reshape(tile_rows, BLK, tile_cols, BLK) * green_mask).reshape(
        tile_rows * BLK, tile_cols * BLK
    )
    green_state = green_tile
    for bit_number in range(col_bits):
        arrived = passed_along(green_state, "col", -(1 << bit_number))
        green_state = jnp.where(half_row >> bit_number & 1 == 1, arrived, green_state)

    def advance(current_state):
        arrived_state = passed_along(current_state, "col", -1)
        return (arrived_state, arrived_state)

    def shift_left(block_now):
        return passed_along(block_now, "row", -1)

    def pair_turn(state_now, shift_last):
        product_sum, block_now, current_state, current = state_now
        green_half = jnp.where(odd_row, current[width:], current[:width])
        product_sum = product_sum + jnp.dot(
            block_now, green_half, preferred_element_type=jnp.float32
        )
        block_now = shift_left(block_now)
        previous = current
        current_state, current = advance(current_state)
        green_half = jnp.where(odd_row, current[:width], previous[width:])
        product_sum = product_sum + jnp.dot(
            block_now, green_half, preferred_element_type=jnp.float32
        )
        if shift_last:
            block_now = shift_left(block_now)
        return (product_sum, block_now, current_state, current)

    start = (
        jnp.zeros((all_rows, tile_cols * BLK), jnp.float32),
        left_block,
        green_state,
        green_state,
    )
    state_now = lax.fori_loop(
        0, col_count - 1, lambda turn_index, state_before: pair_turn(state_before, True), start
    )
    state_now = pair_turn(state_now, False)
    layer_terms = state_now[0].reshape(ri_total, mu_local, tile_cols * BLK)
    return lax.psum_scatter(layer_terms, "layer", scatter_dimension=0, tiled=True).astype(
        jnp.bfloat16
    )


def transposed(value, size):
    return lax.ppermute(
        value,
        ("layer", "row"),
        [(a * size + b, b * size + a) for a in range(size) for b in range(size)],
    )


def compressed_tile(green, green_pattern):
    tile_rows, tile_cols = green_pattern.shape
    cap = min(CAP, tile_rows * tile_cols)
    flat = green_pattern.reshape(-1)
    (spots,) = jnp.nonzero(flat != 0, size=cap, fill_value=0)
    valid = jnp.arange(cap) < jnp.sum(flat != 0)
    block_row = spots // tile_cols
    block_col = spots % tile_cols
    blocks = green.reshape(tile_rows, BLK, tile_cols, BLK)[block_row, :, block_col, :]
    scale = jnp.where(valid, flat[spots], 0).astype(jnp.bfloat16)
    blocks = blocks * scale[:, None, None]
    return blocks, block_row, block_col


def padded_blocks(blocks, block_rows, block_cols):
    empty = jnp.zeros_like(blocks)
    left = (block_cols % 2 == 0)[:, None, None]
    top = (block_rows % 2 == 0)[:, None, None]
    half = jnp.concatenate([jnp.where(left, blocks, empty), jnp.where(left, empty, blocks)], axis=2)
    empty = jnp.zeros_like(half)
    return jnp.concatenate([jnp.where(top, half, empty), jnp.where(top, empty, half)], axis=1)


def block_sparse_product(rows_all, blocks, block_rows, block_cols, width):
    row_total, nao = rows_all.shape
    entries = blocks.shape[0]
    chunks = width // LANE
    chunk_of = block_cols // 2
    order = jnp.argsort(chunk_of)
    chunk_sorted = chunk_of[order]
    starts = jnp.searchsorted(chunk_sorted, jnp.arange(chunks + 1), side="left").astype(jnp.int32)
    k_sorted = (block_rows[order] // 2).astype(jnp.int32)
    padded = padded_blocks(blocks, block_rows, block_cols)[order]
    row_chunk = min(ROW_CHUNK, row_total)

    def kernel(starts_ref, k_ref, t_ref, g_ref, o_ref):
        for chunk in range(chunks):
            def body(entry, acc):
                k = pl.multiple_of(k_ref[entry] * LANE, LANE)
                return acc + jnp.dot(
                    t_ref[:, pl.ds(k, LANE)], g_ref[entry], preferred_element_type=jnp.float32
                )

            acc = lax.fori_loop(
                starts_ref[chunk],
                starts_ref[chunk + 1],
                body,
                jnp.zeros((row_chunk, LANE), jnp.float32),
            )
            o_ref[:, chunk * LANE : (chunk + 1) * LANE] = acc.astype(o_ref.dtype)

    grid_spec = pltpu.PrefetchScalarGridSpec(
        num_scalar_prefetch=2,
        grid=(row_total // row_chunk,),
        in_specs=[
            pl.BlockSpec((row_chunk, nao), lambda i, s, k: (i, 0)),
            pl.BlockSpec((entries, LANE, LANE), lambda i, s, k: (0, 0, 0)),
        ],
        out_specs=pl.BlockSpec((row_chunk, width), lambda i, s, k: (i, 0)),
    )
    return pl.pallas_call(
        kernel,
        grid_spec=grid_spec,
        out_shape=jax.ShapeDtypeStruct((row_total, width), jnp.bfloat16),
        compiler_params=pltpu.CompilerParams(vmem_limit_bytes=56 * 1024 * 1024),
    )(starts, k_sorted, rows_all, padded)


def per_device(tensor, tensor_pattern, green, green_pattern):
    layer_count = lax.axis_size("layer")
    row_count = lax.axis_size("row")
    if layer_count != row_count:
        return cannon_per_device(tensor, tensor_pattern, green, green_pattern)
    ri_local, mu_local, nu_local = tensor.shape
    tile_rows, tile_cols = green_pattern.shape
    tensor_mask = jnp.repeat(tensor_pattern, BLK, axis=1).astype(jnp.bfloat16)
    masked = tensor * tensor_mask[None, :, :]
    full_rows = lax.all_gather(masked, "layer", axis=2, tiled=True)
    nao = full_rows.shape[2]
    blocks, block_row, block_col = compressed_tile(green, green_pattern)
    band_blocks = transposed(lax.all_gather(blocks, ("layer", "col"), axis=0), row_count)
    band_rows = transposed(lax.all_gather(block_row, ("layer", "col"), axis=0), row_count)
    band_cols = transposed(lax.all_gather(block_col, ("layer", "col"), axis=0), row_count)
    rows_all = full_rows.reshape(ri_local * mu_local, nao)
    band_count = band_blocks.shape[0]
    entry_rows = (band_rows + jnp.arange(band_count)[:, None] * tile_rows).reshape(-1)
    entry_cols = band_cols.reshape(-1)
    entry_blocks = band_blocks.reshape(-1, BLK, BLK)
    product = block_sparse_product(rows_all, entry_blocks, entry_rows, entry_cols, tile_cols * BLK)
    product = product.reshape(ri_local, mu_local, tile_cols * BLK)
    return transposed(product, row_count)


def solution(mesh):
    in_specs = (
        P("row", "col", "layer"),
        P("col", "layer"),
        P(("layer", "col"), "row"),
        P(("layer", "col"), "row"),
    )
    out_specs = P("layer", "col", "row")
    return jax.shard_map(
        per_device, mesh=mesh, in_specs=in_specs, out_specs=out_specs, check_vma=False
    )
```

```python
import jax
import jax.numpy as jnp
from jax import lax
from jax.experimental import pallas as pl
from jax.experimental.pallas import tpu as pltpu
from jax.sharding import PartitionSpec as P

BLK = 64
CAP = 48
LANE = 128
ROW_CHUNK = 512


def passed_along(value, axis, by):
    length = lax.axis_size(axis)
    return lax.ppermute(value, axis, [(i, (i + by) % length) for i in range(length)])


def cannon_per_device(tensor, tensor_pattern, green, green_pattern):
    row_count = lax.axis_size("row")
    col_count = lax.axis_size("col")
    col_bits = col_count.bit_length() - 1
    row_index = lax.axis_index("row")
    col_index = lax.axis_index("col")
    odd_row = row_index % 2 == 1
    half_row = row_index // 2
    ri_local, mu_local, nu_local = tensor.shape
    width = nu_local // row_count
    tensor_mask = jnp.repeat(tensor_pattern, BLK, axis=1).astype(jnp.bfloat16)
    masked = tensor * tensor_mask[None, :, :]
    left_block = lax.all_to_all(masked, "row", split_axis=2, concat_axis=0, tiled=True)
    for bit_number in range(col_bits):
        arrived = passed_along(left_block, "row", -(2 << bit_number))
        left_block = jnp.where(col_index >> bit_number & 1 == 1, arrived, left_block)
    ri_total = left_block.shape[0]
    all_rows = ri_total * mu_local
    left_block = left_block.reshape(all_rows, width)
    tile_rows, tile_cols = green_pattern.shape
    green_mask = green_pattern.astype(jnp.bfloat16)[:, None, :, None]
    green_tile = (green.reshape(tile_rows, BLK, tile_cols, BLK) * green_mask).reshape(
        tile_rows * BLK, tile_cols * BLK
    )
    green_state = green_tile
    for bit_number in range(col_bits):
        arrived = passed_along(green_state, "col", -(1 << bit_number))
        green_state = jnp.where(half_row >> bit_number & 1 == 1, arrived, green_state)

    def advance(current_state):
        arrived_state = passed_along(current_state, "col", -1)
        return (arrived_state, arrived_state)

    def shift_left(block_now):
        return passed_along(block_now, "row", -1)

    def pair_turn(state_now, shift_last):
        product_sum, block_now, current_state, current = state_now
        green_half = jnp.where(odd_row, current[width:], current[:width])
        product_sum = product_sum + jnp.dot(
            block_now, green_half, preferred_element_type=jnp.float32
        )
        block_now = shift_left(block_now)
        previous = current
        current_state, current = advance(current_state)
        green_half = jnp.where(odd_row, current[:width], previous[width:])
        product_sum = product_sum + jnp.dot(
            block_now, green_half, preferred_element_type=jnp.float32
        )
        if shift_last:
            block_now = shift_left(block_now)
        return (product_sum, block_now, current_state, current)

    start = (
        jnp.zeros((all_rows, tile_cols * BLK), jnp.float32),
        left_block,
        green_state,
        green_state,
    )
    state_now = lax.fori_loop(
        0, col_count - 1, lambda turn_index, state_before: pair_turn(state_before, True), start
    )
    state_now = pair_turn(state_now, False)
    layer_terms = state_now[0].reshape(ri_total, mu_local, tile_cols * BLK)
    return lax.psum_scatter(layer_terms, "layer", scatter_dimension=0, tiled=True).astype(
        jnp.bfloat16
    )


def transposed(value, size):
    return lax.ppermute(
        value,
        ("layer", "row"),
        [(a * size + b, b * size + a) for a in range(size) for b in range(size)],
    )


def compressed_tile(green, green_pattern):
    tile_rows, tile_cols = green_pattern.shape
    cap = min(CAP, tile_rows * tile_cols)
    flat = green_pattern.reshape(-1)
    (spots,) = jnp.nonzero(flat != 0, size=cap, fill_value=0)
    valid = jnp.arange(cap) < jnp.sum(flat != 0)
    block_row = spots // tile_cols
    block_col = spots % tile_cols
    blocks = green.reshape(tile_rows, BLK, tile_cols, BLK)[block_row, :, block_col, :]
    scale = jnp.where(valid, flat[spots], 0).astype(jnp.bfloat16)
    blocks = blocks * scale[:, None, None]
    return blocks, block_row, block_col


def padded_blocks(blocks, block_rows, block_cols):
    empty = jnp.zeros_like(blocks)
    left = (block_cols % 2 == 0)[:, None, None]
    top = (block_rows % 2 == 0)[:, None, None]
    half = jnp.concatenate([jnp.where(left, blocks, empty), jnp.where(left, empty, blocks)], axis=2)
    empty = jnp.zeros_like(half)
    return jnp.concatenate([jnp.where(top, half, empty), jnp.where(top, empty, half)], axis=1)


def block_sparse_product(rows_all, blocks, block_rows, block_cols, width):
    row_total, nao = rows_all.shape
    entries = blocks.shape[0]
    chunks = width // LANE
    chunk_of = block_cols // 2
    order = jnp.argsort(chunk_of)
    chunk_sorted = chunk_of[order]
    starts = jnp.searchsorted(chunk_sorted, jnp.arange(chunks + 1), side="left").astype(jnp.int32)
    k_sorted = (block_rows[order] // 2).astype(jnp.int32)
    padded = padded_blocks(blocks, block_rows, block_cols)[order]
    row_chunk = min(ROW_CHUNK, row_total)

    def kernel(starts_ref, k_ref, t_ref, g_ref, o_ref):
        for chunk in range(chunks):
            def body(entry, acc):
                k = pl.multiple_of(k_ref[entry] * LANE, LANE)
                return acc + jnp.dot(
                    t_ref[:, pl.ds(k, LANE)], g_ref[entry], preferred_element_type=jnp.float32
                )

            acc = lax.fori_loop(
                starts_ref[chunk],
                starts_ref[chunk + 1],
                body,
                jnp.zeros((row_chunk, LANE), jnp.float32),
            )
            o_ref[:, chunk * LANE : (chunk + 1) * LANE] = acc.astype(o_ref.dtype)

    grid_spec = pltpu.PrefetchScalarGridSpec(
        num_scalar_prefetch=2,
        grid=(row_total // row_chunk,),
        in_specs=[
            pl.BlockSpec((row_chunk, nao), lambda i, s, k: (i, 0)),
            pl.BlockSpec(
                (entries, LANE, LANE), lambda i, s, k: (0, 0, 0), pipeline_mode=pl.Buffered(1)
            ),
        ],
        out_specs=pl.BlockSpec((row_chunk, width), lambda i, s, k: (i, 0)),
    )
    return pl.pallas_call(
        kernel,
        grid_spec=grid_spec,
        out_shape=jax.ShapeDtypeStruct((row_total, width), jnp.bfloat16),
        compiler_params=pltpu.CompilerParams(vmem_limit_bytes=56 * 1024 * 1024),
    )(starts, k_sorted, rows_all, padded)


def per_device(tensor, tensor_pattern, green, green_pattern):
    layer_count = lax.axis_size("layer")
    row_count = lax.axis_size("row")
    if layer_count != row_count:
        return cannon_per_device(tensor, tensor_pattern, green, green_pattern)
    ri_local, mu_local, nu_local = tensor.shape
    tile_rows, tile_cols = green_pattern.shape
    tensor_mask = jnp.repeat(tensor_pattern, BLK, axis=1).astype(jnp.bfloat16)
    masked = tensor * tensor_mask[None, :, :]
    full_rows = lax.all_gather(masked, "layer", axis=2, tiled=True)
    nao = full_rows.shape[2]
    blocks, block_row, block_col = compressed_tile(green, green_pattern)
    band_blocks = transposed(lax.all_gather(blocks, ("layer", "col"), axis=0), row_count)
    band_rows = transposed(lax.all_gather(block_row, ("layer", "col"), axis=0), row_count)
    band_cols = transposed(lax.all_gather(block_col, ("layer", "col"), axis=0), row_count)
    rows_all = full_rows.reshape(ri_local * mu_local, nao)
    band_count = band_blocks.shape[0]
    entry_rows = (band_rows + jnp.arange(band_count)[:, None] * tile_rows).reshape(-1)
    entry_cols = band_cols.reshape(-1)
    entry_blocks = band_blocks.reshape(-1, BLK, BLK)
    pieces = []
    for start in range(0, ri_local * mu_local, ROW_CHUNK):
        piece = block_sparse_product(
            rows_all[start : start + ROW_CHUNK], entry_blocks, entry_rows, entry_cols, tile_cols * BLK
        )
        pieces.append(transposed(piece, row_count))
    product = jnp.concatenate(pieces, axis=0)
    return product.reshape(ri_local, mu_local, tile_cols * BLK)


def solution(mesh):
    in_specs = (
        P("row", "col", "layer"),
        P("col", "layer"),
        P(("layer", "col"), "row"),
        P(("layer", "col"), "row"),
    )
    out_specs = P("layer", "col", "row")
    return jax.shard_map(
        per_device, mesh=mesh, in_specs=in_specs, out_specs=out_specs, check_vma=False
    )
```

```python
import jax
import jax.numpy as jnp
from jax import lax
from jax.experimental import pallas as pl
from jax.experimental.pallas import tpu as pltpu
from jax.sharding import PartitionSpec as P

BLK = 64
CAP = 48
LANE = 128
ROW_CHUNK = 512


def passed_along(value, axis, by):
    length = lax.axis_size(axis)
    return lax.ppermute(value, axis, [(i, (i + by) % length) for i in range(length)])


def cannon_per_device(tensor, tensor_pattern, green, green_pattern):
    row_count = lax.axis_size("row")
    col_count = lax.axis_size("col")
    col_bits = col_count.bit_length() - 1
    row_index = lax.axis_index("row")
    col_index = lax.axis_index("col")
    odd_row = row_index % 2 == 1
    half_row = row_index // 2
    ri_local, mu_local, nu_local = tensor.shape
    width = nu_local // row_count
    tensor_mask = jnp.repeat(tensor_pattern, BLK, axis=1).astype(jnp.bfloat16)
    masked = tensor * tensor_mask[None, :, :]
    left_block = lax.all_to_all(masked, "row", split_axis=2, concat_axis=0, tiled=True)
    for bit_number in range(col_bits):
        arrived = passed_along(left_block, "row", -(2 << bit_number))
        left_block = jnp.where(col_index >> bit_number & 1 == 1, arrived, left_block)
    ri_total = left_block.shape[0]
    all_rows = ri_total * mu_local
    left_block = left_block.reshape(all_rows, width)
    tile_rows, tile_cols = green_pattern.shape
    green_mask = green_pattern.astype(jnp.bfloat16)[:, None, :, None]
    green_tile = (green.reshape(tile_rows, BLK, tile_cols, BLK) * green_mask).reshape(
        tile_rows * BLK, tile_cols * BLK
    )
    green_state = green_tile
    for bit_number in range(col_bits):
        arrived = passed_along(green_state, "col", -(1 << bit_number))
        green_state = jnp.where(half_row >> bit_number & 1 == 1, arrived, green_state)

    def advance(current_state):
        arrived_state = passed_along(current_state, "col", -1)
        return (arrived_state, arrived_state)

    def shift_left(block_now):
        return passed_along(block_now, "row", -1)

    def pair_turn(state_now, shift_last):
        product_sum, block_now, current_state, current = state_now
        green_half = jnp.where(odd_row, current[width:], current[:width])
        product_sum = product_sum + jnp.dot(
            block_now, green_half, preferred_element_type=jnp.float32
        )
        block_now = shift_left(block_now)
        previous = current
        current_state, current = advance(current_state)
        green_half = jnp.where(odd_row, current[:width], previous[width:])
        product_sum = product_sum + jnp.dot(
            block_now, green_half, preferred_element_type=jnp.float32
        )
        if shift_last:
            block_now = shift_left(block_now)
        return (product_sum, block_now, current_state, current)

    start = (
        jnp.zeros((all_rows, tile_cols * BLK), jnp.float32),
        left_block,
        green_state,
        green_state,
    )
    state_now = lax.fori_loop(
        0, col_count - 1, lambda turn_index, state_before: pair_turn(state_before, True), start
    )
    state_now = pair_turn(state_now, False)
    layer_terms = state_now[0].reshape(ri_total, mu_local, tile_cols * BLK)
    return lax.psum_scatter(layer_terms, "layer", scatter_dimension=0, tiled=True).astype(
        jnp.bfloat16
    )


def transposed(value, size):
    return lax.ppermute(
        value,
        ("layer", "row"),
        [(a * size + b, b * size + a) for a in range(size) for b in range(size)],
    )


def compressed_tile(green, green_pattern):
    tile_rows, tile_cols = green_pattern.shape
    cap = min(CAP, tile_rows * tile_cols)
    flat = green_pattern.reshape(-1)
    (spots,) = jnp.nonzero(flat != 0, size=cap, fill_value=0)
    valid = jnp.arange(cap) < jnp.sum(flat != 0)
    block_row = spots // tile_cols
    block_col = spots % tile_cols
    windows = jax.vmap(
        lambda r, c: lax.dynamic_slice(green, (r * BLK, c * LANE), (BLK, LANE))
    )(block_row, block_col // 2)
    left = (block_col % 2 == 0)[:, None, None]
    blocks = jnp.where(left, windows[:, :, :BLK], windows[:, :, BLK:])
    scale = jnp.where(valid, flat[spots], 0).astype(jnp.bfloat16)
    blocks = blocks * scale[:, None, None]
    return blocks, block_row, block_col


def padded_blocks(blocks, block_rows, block_cols):
    empty = jnp.zeros_like(blocks)
    left = (block_cols % 2 == 0)[:, None, None]
    top = (block_rows % 2 == 0)[:, None, None]
    half = jnp.concatenate([jnp.where(left, blocks, empty), jnp.where(left, empty, blocks)], axis=2)
    empty = jnp.zeros_like(half)
    return jnp.concatenate([jnp.where(top, half, empty), jnp.where(top, empty, half)], axis=1)


def block_sparse_product(rows_all, blocks, block_rows, block_cols, width):
    row_total, nao = rows_all.shape
    entries = blocks.shape[0]
    chunks = width // LANE
    chunk_of = block_cols // 2
    order = jnp.argsort(chunk_of)
    chunk_sorted = chunk_of[order]
    starts = jnp.searchsorted(chunk_sorted, jnp.arange(chunks + 1), side="left").astype(jnp.int32)
    k_sorted = (block_rows[order] // 2).astype(jnp.int32)
    padded = padded_blocks(blocks, block_rows, block_cols)[order]
    row_chunk = min(ROW_CHUNK, row_total)

    def kernel(starts_ref, k_ref, t_ref, g_ref, o_ref):
        for chunk in range(chunks):
            def body(entry, acc):
                k = pl.multiple_of(k_ref[entry] * LANE, LANE)
                return acc + jnp.dot(
                    t_ref[:, pl.ds(k, LANE)], g_ref[entry], preferred_element_type=jnp.float32
                )

            acc = lax.fori_loop(
                starts_ref[chunk],
                starts_ref[chunk + 1],
                body,
                jnp.zeros((row_chunk, LANE), jnp.float32),
            )
            o_ref[:, chunk * LANE : (chunk + 1) * LANE] = acc.astype(o_ref.dtype)

    grid_spec = pltpu.PrefetchScalarGridSpec(
        num_scalar_prefetch=2,
        grid=(row_total // row_chunk,),
        in_specs=[
            pl.BlockSpec((row_chunk, nao), lambda i, s, k: (i, 0)),
            pl.BlockSpec(
                (entries, LANE, LANE), lambda i, s, k: (0, 0, 0), pipeline_mode=pl.Buffered(1)
            ),
        ],
        out_specs=pl.BlockSpec((row_chunk, width), lambda i, s, k: (i, 0)),
    )
    return pl.pallas_call(
        kernel,
        grid_spec=grid_spec,
        out_shape=jax.ShapeDtypeStruct((row_total, width), jnp.bfloat16),
        compiler_params=pltpu.CompilerParams(vmem_limit_bytes=56 * 1024 * 1024),
    )(starts, k_sorted, rows_all, padded)


def per_device(tensor, tensor_pattern, green, green_pattern):
    layer_count = lax.axis_size("layer")
    row_count = lax.axis_size("row")
    if layer_count != row_count:
        return cannon_per_device(tensor, tensor_pattern, green, green_pattern)
    ri_local, mu_local, nu_local = tensor.shape
    tile_rows, tile_cols = green_pattern.shape
    tensor_mask = jnp.repeat(tensor_pattern, BLK, axis=1).astype(jnp.bfloat16)
    masked = tensor * tensor_mask[None, :, :]
    own = masked.reshape(ri_local * mu_local, nu_local)
    layer_index = lax.axis_index("layer")
    col_count = lax.axis_size("col")
    blocks, block_row, block_col = compressed_tile(green, green_pattern)
    blocks, block_row, block_col = (
        lax.all_gather(transposed(part, row_count), ("row", "col"), axis=0)
        for part in (blocks, block_row, block_col)
    )
    band_count = blocks.shape[0]
    band = jnp.arange(band_count)[:, None]
    if layer_count == 4:
        across = lax.ppermute(own, "layer", [(i, i ^ 2) for i in range(4)])
        pair = jnp.concatenate([own, across], axis=1)
        partner = lax.ppermute(pair, "layer", [(i, i ^ 1) for i in range(4)])
        rows_all = jnp.concatenate([pair, partner], axis=1)
        source = (band // col_count) ^ layer_index
        position = jnp.array([0, 2, 1, 3], jnp.int32)[source]
    else:
        rows_all = lax.all_gather(own, "layer", axis=1, tiled=True)
        position = band // col_count
    entry_rows = (position * col_count + band % col_count) * tile_rows + block_row
    entry_rows = entry_rows.reshape(-1)
    entry_cols = block_col.reshape(-1)
    entry_blocks = blocks.reshape(-1, BLK, BLK)
    pieces = []
    for start in range(0, ri_local * mu_local, ROW_CHUNK):
        piece = block_sparse_product(
            rows_all[start : start + ROW_CHUNK], entry_blocks, entry_rows, entry_cols, tile_cols * BLK
        )
        pieces.append(transposed(piece, row_count))
    product = jnp.concatenate(pieces, axis=0)
    return product.reshape(ri_local, mu_local, tile_cols * BLK)


def solution(mesh):
    in_specs = (
        P("row", "col", "layer"),
        P("col", "layer"),
        P(("layer", "col"), "row"),
        P(("layer", "col"), "row"),
    )
    out_specs = P("layer", "col", "row")
    return jax.shard_map(
        per_device, mesh=mesh, in_specs=in_specs, out_specs=out_specs, check_vma=False
    )
```

```python
import jax
import jax.numpy as jnp
from jax import lax
from jax.experimental import pallas as pl
from jax.experimental.pallas import tpu as pltpu
from jax.sharding import PartitionSpec as P

BLK = 64
CAP = 48
LANE = 128
COL_PIECES = 2


def passed_along(value, axis, by):
    length = lax.axis_size(axis)
    return lax.ppermute(value, axis, [(i, (i + by) % length) for i in range(length)])


def cannon_per_device(tensor, tensor_pattern, green, green_pattern):
    row_count = lax.axis_size("row")
    col_count = lax.axis_size("col")
    col_bits = col_count.bit_length() - 1
    row_index = lax.axis_index("row")
    col_index = lax.axis_index("col")
    odd_row = row_index % 2 == 1
    half_row = row_index // 2
    ri_local, mu_local, nu_local = tensor.shape
    width = nu_local // row_count
    tensor_mask = jnp.repeat(tensor_pattern, BLK, axis=1).astype(jnp.bfloat16)
    masked = tensor * tensor_mask[None, :, :]
    left_block = lax.all_to_all(masked, "row", split_axis=2, concat_axis=0, tiled=True)
    for bit_number in range(col_bits):
        arrived = passed_along(left_block, "row", -(2 << bit_number))
        left_block = jnp.where(col_index >> bit_number & 1 == 1, arrived, left_block)
    ri_total = left_block.shape[0]
    all_rows = ri_total * mu_local
    left_block = left_block.reshape(all_rows, width)
    tile_rows, tile_cols = green_pattern.shape
    green_mask = green_pattern.astype(jnp.bfloat16)[:, None, :, None]
    green_tile = (green.reshape(tile_rows, BLK, tile_cols, BLK) * green_mask).reshape(
        tile_rows * BLK, tile_cols * BLK
    )
    green_state = green_tile
    for bit_number in range(col_bits):
        arrived = passed_along(green_state, "col", -(1 << bit_number))
        green_state = jnp.where(half_row >> bit_number & 1 == 1, arrived, green_state)

    def advance(current_state):
        arrived_state = passed_along(current_state, "col", -1)
        return (arrived_state, arrived_state)

    def shift_left(block_now):
        return passed_along(block_now, "row", -1)

    def pair_turn(state_now, shift_last):
        product_sum, block_now, current_state, current = state_now
        green_half = jnp.where(odd_row, current[width:], current[:width])
        product_sum = product_sum + jnp.dot(
            block_now, green_half, preferred_element_type=jnp.float32
        )
        block_now = shift_left(block_now)
        previous = current
        current_state, current = advance(current_state)
        green_half = jnp.where(odd_row, current[:width], previous[width:])
        product_sum = product_sum + jnp.dot(
            block_now, green_half, preferred_element_type=jnp.float32
        )
        if shift_last:
            block_now = shift_left(block_now)
        return (product_sum, block_now, current_state, current)

    start = (
        jnp.zeros((all_rows, tile_cols * BLK), jnp.float32),
        left_block,
        green_state,
        green_state,
    )
    state_now = lax.fori_loop(
        0, col_count - 1, lambda turn_index, state_before: pair_turn(state_before, True), start
    )
    state_now = pair_turn(state_now, False)
    layer_terms = state_now[0].reshape(ri_total, mu_local, tile_cols * BLK)
    return lax.psum_scatter(layer_terms, "layer", scatter_dimension=0, tiled=True).astype(
        jnp.bfloat16
    )


def transposed(value, size):
    return lax.ppermute(
        value,
        ("layer", "row"),
        [(a * size + b, b * size + a) for a in range(size) for b in range(size)],
    )


def compressed_tile(green, green_pattern):
    tile_rows, tile_cols = green_pattern.shape
    cap = min(CAP, tile_rows * tile_cols)
    flat = green_pattern.reshape(-1)
    (spots,) = jnp.nonzero(flat != 0, size=cap, fill_value=0)
    valid = jnp.arange(cap) < jnp.sum(flat != 0)
    block_row = spots // tile_cols
    block_col = spots % tile_cols
    blocks = green.reshape(tile_rows, BLK, tile_cols, BLK)[block_row, :, block_col, :]
    scale = jnp.where(valid, flat[spots], 0).astype(jnp.bfloat16)
    blocks = blocks * scale[:, None, None]
    return blocks, block_row, block_col


def padded_blocks(blocks, block_rows, block_cols):
    empty = jnp.zeros_like(blocks)
    left = (block_cols % 2 == 0)[:, None, None]
    top = (block_rows % 2 == 0)[:, None, None]
    half = jnp.concatenate([jnp.where(left, blocks, empty), jnp.where(left, empty, blocks)], axis=2)
    empty = jnp.zeros_like(half)
    return jnp.concatenate([jnp.where(top, half, empty), jnp.where(top, empty, half)], axis=1)


def block_sparse_product(rows_all, blocks, block_rows, block_cols, width, pieces):
    row_total, nao = rows_all.shape
    entries = blocks.shape[0]
    chunks = width // LANE
    piece_chunks = chunks // pieces
    chunk_of = block_cols // 2
    order = jnp.argsort(chunk_of)
    chunk_sorted = chunk_of[order]
    starts = jnp.searchsorted(chunk_sorted, jnp.arange(chunks + 1), side="left").astype(jnp.int32)
    k_sorted = (block_rows[order] // 2).astype(jnp.int32)
    padded = padded_blocks(blocks, block_rows, block_cols)[order]
    results = []
    for piece in range(pieces):
        first = piece * piece_chunks

        def kernel(starts_ref, k_ref, t_ref, g_ref, o_ref, first=first):
            for chunk in range(piece_chunks):
                def body(entry, acc):
                    k = pl.multiple_of(k_ref[entry] * LANE, LANE)
                    return acc + jnp.dot(
                        t_ref[:, pl.ds(k, LANE)], g_ref[entry], preferred_element_type=jnp.float32
                    )

                acc = lax.fori_loop(
                    starts_ref[first + chunk],
                    starts_ref[first + chunk + 1],
                    body,
                    jnp.zeros((row_total, LANE), jnp.float32),
                )
                o_ref[:, chunk * LANE : (chunk + 1) * LANE] = acc.astype(o_ref.dtype)

        grid_spec = pltpu.PrefetchScalarGridSpec(
            num_scalar_prefetch=2,
            grid=(1,),
            in_specs=[
                pl.BlockSpec(
                    (row_total, nao), lambda i, s, k: (0, 0), pipeline_mode=pl.Buffered(1)
                ),
                pl.BlockSpec(
                    (entries, LANE, LANE), lambda i, s, k: (0, 0, 0), pipeline_mode=pl.Buffered(1)
                ),
            ],
            out_specs=pl.BlockSpec((row_total, piece_chunks * LANE), lambda i, s, k: (0, 0)),
        )
        results.append(
            pl.pallas_call(
                kernel,
                grid_spec=grid_spec,
                out_shape=jax.ShapeDtypeStruct((row_total, piece_chunks * LANE), jnp.bfloat16),
                compiler_params=pltpu.CompilerParams(vmem_limit_bytes=60 * 1024 * 1024),
            )(starts, k_sorted, rows_all, padded)
        )
    return results

def per_device(tensor, tensor_pattern, green, green_pattern):
    layer_count = lax.axis_size("layer")
    row_count = lax.axis_size("row")
    if layer_count != row_count:
        return cannon_per_device(tensor, tensor_pattern, green, green_pattern)
    ri_local, mu_local, nu_local = tensor.shape
    tile_rows, tile_cols = green_pattern.shape
    tensor_mask = jnp.repeat(tensor_pattern, BLK, axis=1).astype(jnp.bfloat16)
    masked = tensor * tensor_mask[None, :, :]
    own = masked.reshape(ri_local * mu_local, nu_local)
    layer_index = lax.axis_index("layer")
    col_count = lax.axis_size("col")
    blocks, block_row, block_col = compressed_tile(green, green_pattern)
    blocks, block_row, block_col = (
        lax.all_gather(transposed(part, row_count), ("row", "col"), axis=0)
        for part in (blocks, block_row, block_col)
    )
    band_count = blocks.shape[0]
    band = jnp.arange(band_count)[:, None]
    if layer_count == 4:
        across = lax.ppermute(own, "layer", [(i, i ^ 2) for i in range(4)])
        pair = jnp.concatenate([own, across], axis=1)
        partner = lax.ppermute(pair, "layer", [(i, i ^ 1) for i in range(4)])
        rows_all = jnp.concatenate([pair, partner], axis=1)
        source = (band // col_count) ^ layer_index
        position = jnp.array([0, 2, 1, 3], jnp.int32)[source]
    else:
        rows_all = lax.all_gather(own, "layer", axis=1, tiled=True)
        position = band // col_count
    entry_rows = (position * col_count + band % col_count) * tile_rows + block_row
    entry_rows = entry_rows.reshape(-1)
    entry_cols = block_col.reshape(-1)
    entry_blocks = blocks.reshape(-1, BLK, BLK)
    pieces = block_sparse_product(
        rows_all, entry_blocks, entry_rows, entry_cols, tile_cols * BLK, COL_PIECES
    )
    product = jnp.concatenate([transposed(piece, row_count) for piece in pieces], axis=1)
    return product.reshape(ri_local, mu_local, tile_cols * BLK)

def solution(mesh):
    in_specs = (
        P("row", "col", "layer"),
        P("col", "layer"),
        P(("layer", "col"), "row"),
        P(("layer", "col"), "row"),
    )
    out_specs = P("layer", "col", "row")
    return jax.shard_map(
        per_device, mesh=mesh, in_specs=in_specs, out_specs=out_specs, check_vma=False
    )
```

```python
import jax
import jax.numpy as jnp
from jax import lax
from jax.experimental import pallas as pl
from jax.experimental.pallas import tpu as pltpu
from jax.sharding import PartitionSpec as P

BLK = 64
CAP = 48
LANE = 128
ROW_CHUNK = 512


def passed_along(value, axis, by):
    length = lax.axis_size(axis)
    return lax.ppermute(value, axis, [(i, (i + by) % length) for i in range(length)])


def cannon_per_device(tensor, tensor_pattern, green, green_pattern):
    row_count = lax.axis_size("row")
    col_count = lax.axis_size("col")
    col_bits = col_count.bit_length() - 1
    row_index = lax.axis_index("row")
    col_index = lax.axis_index("col")
    odd_row = row_index % 2 == 1
    half_row = row_index // 2
    ri_local, mu_local, nu_local = tensor.shape
    width = nu_local // row_count
    tensor_mask = jnp.repeat(tensor_pattern, BLK, axis=1).astype(jnp.bfloat16)
    masked = tensor * tensor_mask[None, :, :]
    left_block = lax.all_to_all(masked, "row", split_axis=2, concat_axis=0, tiled=True)
    for bit_number in range(col_bits):
        arrived = passed_along(left_block, "row", -(2 << bit_number))
        left_block = jnp.where(col_index >> bit_number & 1 == 1, arrived, left_block)
    ri_total = left_block.shape[0]
    all_rows = ri_total * mu_local
    left_block = left_block.reshape(all_rows, width)
    tile_rows, tile_cols = green_pattern.shape
    green_mask = green_pattern.astype(jnp.bfloat16)[:, None, :, None]
    green_tile = (green.reshape(tile_rows, BLK, tile_cols, BLK) * green_mask).reshape(
        tile_rows * BLK, tile_cols * BLK
    )
    green_state = green_tile
    for bit_number in range(col_bits):
        arrived = passed_along(green_state, "col", -(1 << bit_number))
        green_state = jnp.where(half_row >> bit_number & 1 == 1, arrived, green_state)

    def advance(current_state):
        arrived_state = passed_along(current_state, "col", -1)
        return (arrived_state, arrived_state)

    def shift_left(block_now):
        return passed_along(block_now, "row", -1)

    def pair_turn(state_now, shift_last):
        product_sum, block_now, current_state, current = state_now
        green_half = jnp.where(odd_row, current[width:], current[:width])
        product_sum = product_sum + jnp.dot(
            block_now, green_half, preferred_element_type=jnp.float32
        )
        block_now = shift_left(block_now)
        previous = current
        current_state, current = advance(current_state)
        green_half = jnp.where(odd_row, current[:width], previous[width:])
        product_sum = product_sum + jnp.dot(
            block_now, green_half, preferred_element_type=jnp.float32
        )
        if shift_last:
            block_now = shift_left(block_now)
        return (product_sum, block_now, current_state, current)

    start = (
        jnp.zeros((all_rows, tile_cols * BLK), jnp.float32),
        left_block,
        green_state,
        green_state,
    )
    state_now = lax.fori_loop(
        0, col_count - 1, lambda turn_index, state_before: pair_turn(state_before, True), start
    )
    state_now = pair_turn(state_now, False)
    layer_terms = state_now[0].reshape(ri_total, mu_local, tile_cols * BLK)
    return lax.psum_scatter(layer_terms, "layer", scatter_dimension=0, tiled=True).astype(
        jnp.bfloat16
    )


def transposed(value, size):
    return lax.ppermute(
        value,
        ("layer", "row"),
        [(a * size + b, b * size + a) for a in range(size) for b in range(size)],
    )


def compressed_tile(green, green_pattern):
    tile_rows, tile_cols = green_pattern.shape
    cap = min(CAP, tile_rows * tile_cols)
    flat = green_pattern.reshape(-1)
    (spots,) = jnp.nonzero(flat != 0, size=cap, fill_value=0)
    valid = jnp.arange(cap) < jnp.sum(flat != 0)
    block_row = spots // tile_cols
    block_col = spots % tile_cols
    blocks = green.reshape(tile_rows, BLK, tile_cols, BLK)[block_row, :, block_col, :]
    scale = jnp.where(valid, flat[spots], 0).astype(jnp.bfloat16)
    blocks = blocks * scale[:, None, None]
    return blocks, block_row, block_col


def padded_blocks(blocks, block_rows, block_cols):
    empty = jnp.zeros_like(blocks)
    left = (block_cols % 2 == 0)[:, None, None]
    top = (block_rows % 2 == 0)[:, None, None]
    half = jnp.concatenate([jnp.where(left, blocks, empty), jnp.where(left, empty, blocks)], axis=2)
    empty = jnp.zeros_like(half)
    return jnp.concatenate([jnp.where(top, half, empty), jnp.where(top, empty, half)], axis=1)


def block_sparse_product(rows_all, blocks, block_rows, block_cols, width, pieces):
    row_total, nao = rows_all.shape
    entries = blocks.shape[0]
    chunks = width // LANE
    piece_chunks = chunks // pieces
    chunk_of = block_cols // 2
    order = jnp.argsort(chunk_of)
    chunk_sorted = chunk_of[order]
    starts = jnp.searchsorted(chunk_sorted, jnp.arange(chunks + 1), side="left").astype(jnp.int32)
    k_sorted = (block_rows[order] // 2).astype(jnp.int32)
    padded = padded_blocks(blocks, block_rows, block_cols)[order]
    results = []
    for piece in range(pieces):
        first = piece * piece_chunks

        def kernel(starts_ref, k_ref, t_ref, g_ref, o_ref, first=first):
            for chunk in range(piece_chunks):
                def body(entry, acc):
                    k = pl.multiple_of(k_ref[entry] * LANE, LANE)
                    return acc + jnp.dot(
                        t_ref[:, pl.ds(k, LANE)], g_ref[entry], preferred_element_type=jnp.float32
                    )

                acc = lax.fori_loop(
                    starts_ref[first + chunk],
                    starts_ref[first + chunk + 1],
                    body,
                    jnp.zeros((row_total, LANE), jnp.float32),
                )
                o_ref[:, chunk * LANE : (chunk + 1) * LANE] = acc.astype(o_ref.dtype)

        grid_spec = pltpu.PrefetchScalarGridSpec(
            num_scalar_prefetch=2,
            grid=(1,),
            in_specs=[
                pl.BlockSpec(
                    (row_total, nao), lambda i, s, k: (0, 0), pipeline_mode=pl.Buffered(1)
                ),
                pl.BlockSpec(
                    (entries, LANE, LANE), lambda i, s, k: (0, 0, 0), pipeline_mode=pl.Buffered(1)
                ),
            ],
            out_specs=pl.BlockSpec((row_total, piece_chunks * LANE), lambda i, s, k: (0, 0)),
        )
        results.append(
            pl.pallas_call(
                kernel,
                grid_spec=grid_spec,
                out_shape=jax.ShapeDtypeStruct((row_total, piece_chunks * LANE), jnp.bfloat16),
                compiler_params=pltpu.CompilerParams(vmem_limit_bytes=60 * 1024 * 1024),
            )(starts, k_sorted, rows_all, padded)
        )
    return results

def per_device(tensor, tensor_pattern, green, green_pattern):
    layer_count = lax.axis_size("layer")
    row_count = lax.axis_size("row")
    if layer_count != row_count:
        return cannon_per_device(tensor, tensor_pattern, green, green_pattern)
    ri_local, mu_local, nu_local = tensor.shape
    tile_rows, tile_cols = green_pattern.shape
    tensor_mask = jnp.repeat(tensor_pattern, BLK, axis=1).astype(jnp.bfloat16)
    masked = tensor * tensor_mask[None, :, :]
    own = masked.reshape(ri_local * mu_local, nu_local)
    layer_index = lax.axis_index("layer")
    col_count = lax.axis_size("col")
    blocks, block_row, block_col = compressed_tile(green, green_pattern)
    blocks, block_row, block_col = (
        lax.all_gather(transposed(part, row_count), ("row", "col"), axis=0)
        for part in (blocks, block_row, block_col)
    )
    band_count = blocks.shape[0]
    band = jnp.arange(band_count)[:, None]
    rows_all = lax.all_gather(own, "layer", axis=1, tiled=True)
    position = band // col_count
    entry_rows = (position * col_count + band % col_count) * tile_rows + block_row
    entry_rows = entry_rows.reshape(-1)
    entry_cols = block_col.reshape(-1)
    entry_blocks = blocks.reshape(-1, BLK, BLK)
    pieces = []
    for start in range(0, ri_local * mu_local, ROW_CHUNK):
        (piece,) = block_sparse_product(
            rows_all[start : start + ROW_CHUNK], entry_blocks, entry_rows, entry_cols, tile_cols * BLK, 1
        )
        pieces.append(transposed(piece, row_count))
    product = jnp.concatenate(pieces, axis=0)
    return product.reshape(ri_local, mu_local, tile_cols * BLK)

def solution(mesh):
    in_specs = (
        P("row", "col", "layer"),
        P("col", "layer"),
        P(("layer", "col"), "row"),
        P(("layer", "col"), "row"),
    )
    out_specs = P("layer", "col", "row")
    return jax.shard_map(
        per_device, mesh=mesh, in_specs=in_specs, out_specs=out_specs, check_vma=False
    )
```

```python
import jax
import jax.numpy as jnp
from jax import lax
from jax.experimental import pallas as pl
from jax.experimental.pallas import tpu as pltpu
from jax.sharding import PartitionSpec as P

BLK = 64
CAP = 48
LANE = 128
ROW_CHUNK = 512


def passed_along(value, axis, by):
    length = lax.axis_size(axis)
    return lax.ppermute(value, axis, [(i, (i + by) % length) for i in range(length)])


def cannon_per_device(tensor, tensor_pattern, green, green_pattern):
    row_count = lax.axis_size("row")
    col_count = lax.axis_size("col")
    col_bits = col_count.bit_length() - 1
    row_index = lax.axis_index("row")
    col_index = lax.axis_index("col")
    odd_row = row_index % 2 == 1
    half_row = row_index // 2
    ri_local, mu_local, nu_local = tensor.shape
    width = nu_local // row_count
    tensor_mask = jnp.repeat(tensor_pattern, BLK, axis=1).astype(jnp.bfloat16)
    masked = tensor * tensor_mask[None, :, :]
    left_block = lax.all_to_all(masked, "row", split_axis=2, concat_axis=0, tiled=True)
    for bit_number in range(col_bits):
        arrived = passed_along(left_block, "row", -(2 << bit_number))
        left_block = jnp.where(col_index >> bit_number & 1 == 1, arrived, left_block)
    ri_total = left_block.shape[0]
    all_rows = ri_total * mu_local
    left_block = left_block.reshape(all_rows, width)
    tile_rows, tile_cols = green_pattern.shape
    green_mask = green_pattern.astype(jnp.bfloat16)[:, None, :, None]
    green_tile = (green.reshape(tile_rows, BLK, tile_cols, BLK) * green_mask).reshape(
        tile_rows * BLK, tile_cols * BLK
    )
    green_state = green_tile
    for bit_number in range(col_bits):
        arrived = passed_along(green_state, "col", -(1 << bit_number))
        green_state = jnp.where(half_row >> bit_number & 1 == 1, arrived, green_state)

    def advance(current_state):
        arrived_state = passed_along(current_state, "col", -1)
        return (arrived_state, arrived_state)

    def shift_left(block_now):
        return passed_along(block_now, "row", -1)

    def pair_turn(state_now, shift_last):
        product_sum, block_now, current_state, current = state_now
        green_half = jnp.where(odd_row, current[width:], current[:width])
        product_sum = product_sum + jnp.dot(
            block_now, green_half, preferred_element_type=jnp.float32
        )
        block_now = shift_left(block_now)
        previous = current
        current_state, current = advance(current_state)
        green_half = jnp.where(odd_row, current[:width], previous[width:])
        product_sum = product_sum + jnp.dot(
            block_now, green_half, preferred_element_type=jnp.float32
        )
        if shift_last:
            block_now = shift_left(block_now)
        return (product_sum, block_now, current_state, current)

    start = (
        jnp.zeros((all_rows, tile_cols * BLK), jnp.float32),
        left_block,
        green_state,
        green_state,
    )
    state_now = lax.fori_loop(
        0, col_count - 1, lambda turn_index, state_before: pair_turn(state_before, True), start
    )
    state_now = pair_turn(state_now, False)
    layer_terms = state_now[0].reshape(ri_total, mu_local, tile_cols * BLK)
    return lax.psum_scatter(layer_terms, "layer", scatter_dimension=0, tiled=True).astype(
        jnp.bfloat16
    )


def transposed(value, size, flip=0):
    return lax.ppermute(
        value,
        ("layer", "row"),
        [(a * size + b, (b ^ flip) * size + (a ^ flip)) for a in range(size) for b in range(size)],
    )


def split_transposed(value, size):
    if size != 4:
        return transposed(value, size)
    half = value.shape[0] // 2
    direct = transposed(value[:half], size)
    across = [(i, i ^ 2) for i in range(4)]
    detour = lax.ppermute(value[half:], "layer", across)
    detour = lax.ppermute(transposed(detour, size, 2), "layer", across)
    return jnp.concatenate([direct, detour], axis=0)


def compressed_tile(green, green_pattern):
    tile_rows, tile_cols = green_pattern.shape
    cap = min(CAP, tile_rows * tile_cols)
    flat = green_pattern.reshape(-1)
    (spots,) = jnp.nonzero(flat != 0, size=cap, fill_value=0)
    valid = jnp.arange(cap) < jnp.sum(flat != 0)
    block_row = spots // tile_cols
    block_col = spots % tile_cols
    blocks = green.reshape(tile_rows, BLK, tile_cols, BLK)[block_row, :, block_col, :]
    scale = jnp.where(valid, flat[spots], 0).astype(jnp.bfloat16)
    blocks = blocks * scale[:, None, None]
    return blocks, block_row, block_col


def padded_blocks(blocks, block_rows, block_cols):
    empty = jnp.zeros_like(blocks)
    left = (block_cols % 2 == 0)[:, None, None]
    top = (block_rows % 2 == 0)[:, None, None]
    half = jnp.concatenate([jnp.where(left, blocks, empty), jnp.where(left, empty, blocks)], axis=2)
    empty = jnp.zeros_like(half)
    return jnp.concatenate([jnp.where(top, half, empty), jnp.where(top, empty, half)], axis=1)


def block_sparse_product(rows_all, blocks, block_rows, block_cols, width, pieces):
    row_total, nao = rows_all.shape
    entries = blocks.shape[0]
    chunks = width // LANE
    piece_chunks = chunks // pieces
    chunk_of = block_cols // 2
    order = jnp.argsort(chunk_of)
    chunk_sorted = chunk_of[order]
    starts = jnp.searchsorted(chunk_sorted, jnp.arange(chunks + 1), side="left").astype(jnp.int32)
    k_sorted = (block_rows[order] // 2).astype(jnp.int32)
    padded = padded_blocks(blocks, block_rows, block_cols)[order]
    results = []
    for piece in range(pieces):
        first = piece * piece_chunks

        def kernel(starts_ref, k_ref, t_ref, g_ref, o_ref, first=first):
            for chunk in range(piece_chunks):
                def body(entry, acc):
                    k = pl.multiple_of(k_ref[entry] * LANE, LANE)
                    return acc + jnp.dot(
                        t_ref[:, pl.ds(k, LANE)], g_ref[entry], preferred_element_type=jnp.float32
                    )

                acc = lax.fori_loop(
                    starts_ref[first + chunk],
                    starts_ref[first + chunk + 1],
                    body,
                    jnp.zeros((row_total, LANE), jnp.float32),
                )
                o_ref[:, chunk * LANE : (chunk + 1) * LANE] = acc.astype(o_ref.dtype)

        grid_spec = pltpu.PrefetchScalarGridSpec(
            num_scalar_prefetch=2,
            grid=(1,),
            in_specs=[
                pl.BlockSpec(
                    (row_total, nao), lambda i, s, k: (0, 0), pipeline_mode=pl.Buffered(1)
                ),
                pl.BlockSpec(
                    (entries, LANE, LANE), lambda i, s, k: (0, 0, 0), pipeline_mode=pl.Buffered(1)
                ),
            ],
            out_specs=pl.BlockSpec((row_total, piece_chunks * LANE), lambda i, s, k: (0, 0)),
        )
        results.append(
            pl.pallas_call(
                kernel,
                grid_spec=grid_spec,
                out_shape=jax.ShapeDtypeStruct((row_total, piece_chunks * LANE), jnp.bfloat16),
                compiler_params=pltpu.CompilerParams(vmem_limit_bytes=60 * 1024 * 1024),
            )(starts, k_sorted, rows_all, padded)
        )
    return results

def per_device(tensor, tensor_pattern, green, green_pattern):
    layer_count = lax.axis_size("layer")
    row_count = lax.axis_size("row")
    if layer_count != row_count:
        return cannon_per_device(tensor, tensor_pattern, green, green_pattern)
    ri_local, mu_local, nu_local = tensor.shape
    tile_rows, tile_cols = green_pattern.shape
    tensor_mask = jnp.repeat(tensor_pattern, BLK, axis=1).astype(jnp.bfloat16)
    masked = tensor * tensor_mask[None, :, :]
    own = masked.reshape(ri_local * mu_local, nu_local)
    layer_index = lax.axis_index("layer")
    col_count = lax.axis_size("col")
    blocks, block_row, block_col = compressed_tile(green, green_pattern)
    blocks, block_row, block_col = (
        lax.all_gather(transposed(part, row_count), ("row", "col"), axis=0)
        for part in (blocks, block_row, block_col)
    )
    band_count = blocks.shape[0]
    band = jnp.arange(band_count)[:, None]
    rows_all = lax.all_gather(own, "layer", axis=1, tiled=True)
    position = band // col_count
    entry_rows = (position * col_count + band % col_count) * tile_rows + block_row
    entry_rows = entry_rows.reshape(-1)
    entry_cols = block_col.reshape(-1)
    entry_blocks = blocks.reshape(-1, BLK, BLK)
    pieces = []
    for start in range(0, ri_local * mu_local, ROW_CHUNK):
        (piece,) = block_sparse_product(
            rows_all[start : start + ROW_CHUNK], entry_blocks, entry_rows, entry_cols, tile_cols * BLK, 1
        )
        pieces.append(split_transposed(piece, row_count))
    product = jnp.concatenate(pieces, axis=0)
    return product.reshape(ri_local, mu_local, tile_cols * BLK)

def solution(mesh):
    in_specs = (
        P("row", "col", "layer"),
        P("col", "layer"),
        P(("layer", "col"), "row"),
        P(("layer", "col"), "row"),
    )
    out_specs = P("layer", "col", "row")
    return jax.shard_map(
        per_device, mesh=mesh, in_specs=in_specs, out_specs=out_specs, check_vma=False
    )
```

```python
import jax
import jax.numpy as jnp
from jax import lax
from jax.experimental import pallas as pl
from jax.experimental.pallas import tpu as pltpu
from jax.sharding import PartitionSpec as P

BLK = 64
CAP = 48
LANE = 128
ROW_CHUNK = 512


def passed_along(value, axis, by):
    length = lax.axis_size(axis)
    return lax.ppermute(value, axis, [(i, (i + by) % length) for i in range(length)])


def cannon_per_device(tensor, tensor_pattern, green, green_pattern):
    row_count = lax.axis_size("row")
    col_count = lax.axis_size("col")
    col_bits = col_count.bit_length() - 1
    row_index = lax.axis_index("row")
    col_index = lax.axis_index("col")
    odd_row = row_index % 2 == 1
    half_row = row_index // 2
    ri_local, mu_local, nu_local = tensor.shape
    width = nu_local // row_count
    tensor_mask = jnp.repeat(tensor_pattern, BLK, axis=1).astype(jnp.bfloat16)
    masked = tensor * tensor_mask[None, :, :]
    left_block = lax.all_to_all(masked, "row", split_axis=2, concat_axis=0, tiled=True)
    for bit_number in range(col_bits):
        arrived = passed_along(left_block, "row", -(2 << bit_number))
        left_block = jnp.where(col_index >> bit_number & 1 == 1, arrived, left_block)
    ri_total = left_block.shape[0]
    all_rows = ri_total * mu_local
    left_block = left_block.reshape(all_rows, width)
    tile_rows, tile_cols = green_pattern.shape
    green_mask = green_pattern.astype(jnp.bfloat16)[:, None, :, None]
    green_tile = (green.reshape(tile_rows, BLK, tile_cols, BLK) * green_mask).reshape(
        tile_rows * BLK, tile_cols * BLK
    )
    green_state = green_tile
    for bit_number in range(col_bits):
        arrived = passed_along(green_state, "col", -(1 << bit_number))
        green_state = jnp.where(half_row >> bit_number & 1 == 1, arrived, green_state)

    def advance(current_state):
        arrived_state = passed_along(current_state, "col", -1)
        return (arrived_state, arrived_state)

    def shift_left(block_now):
        return passed_along(block_now, "row", -1)

    def pair_turn(state_now, shift_last):
        product_sum, block_now, current_state, current = state_now
        green_half = jnp.where(odd_row, current[width:], current[:width])
        product_sum = product_sum + jnp.dot(
            block_now, green_half, preferred_element_type=jnp.float32
        )
        block_now = shift_left(block_now)
        previous = current
        current_state, current = advance(current_state)
        green_half = jnp.where(odd_row, current[:width], previous[width:])
        product_sum = product_sum + jnp.dot(
            block_now, green_half, preferred_element_type=jnp.float32
        )
        if shift_last:
            block_now = shift_left(block_now)
        return (product_sum, block_now, current_state, current)

    start = (
        jnp.zeros((all_rows, tile_cols * BLK), jnp.float32),
        left_block,
        green_state,
        green_state,
    )
    state_now = lax.fori_loop(
        0, col_count - 1, lambda turn_index, state_before: pair_turn(state_before, True), start
    )
    state_now = pair_turn(state_now, False)
    layer_terms = state_now[0].reshape(ri_total, mu_local, tile_cols * BLK)
    return lax.psum_scatter(layer_terms, "layer", scatter_dimension=0, tiled=True).astype(
        jnp.bfloat16
    )


def transposed(value, size):
    return lax.ppermute(
        value,
        ("layer", "row"),
        [(a * size + b, b * size + a) for a in range(size) for b in range(size)],
    )


def gathered_windows(green, window_rows, window_cols):
    count = window_rows.shape[0]

    def kernel(rows_ref, cols_ref, green_ref, out_ref):
        out_ref[0] = green_ref[...]

    grid_spec = pltpu.PrefetchScalarGridSpec(
        num_scalar_prefetch=2,
        grid=(count,),
        in_specs=[pl.BlockSpec((BLK, LANE), lambda e, r, c: (r[e], c[e]))],
        out_specs=pl.BlockSpec((1, BLK, LANE), lambda e, r, c: (e, 0, 0)),
    )
    return pl.pallas_call(
        kernel,
        grid_spec=grid_spec,
        out_shape=jax.ShapeDtypeStruct((count, BLK, LANE), green.dtype),
    )(window_rows.astype(jnp.int32), window_cols.astype(jnp.int32), green)


def compressed_tile(green, green_pattern):
    tile_rows, tile_cols = green_pattern.shape
    cap = min(CAP, tile_rows * tile_cols)
    flat = green_pattern.reshape(-1)
    (spots,) = jnp.nonzero(flat != 0, size=cap, fill_value=0)
    valid = jnp.arange(cap) < jnp.sum(flat != 0)
    block_row = spots // tile_cols
    block_col = spots % tile_cols
    windows = gathered_windows(green, block_row, block_col // 2)
    left = (block_col % 2 == 0)[:, None, None]
    blocks = jnp.where(left, windows[:, :, :BLK], windows[:, :, BLK:])
    scale = jnp.where(valid, flat[spots], 0).astype(jnp.bfloat16)
    blocks = blocks * scale[:, None, None]
    return blocks, block_row, block_col


def padded_blocks(blocks, block_rows, block_cols):
    empty = jnp.zeros_like(blocks)
    left = (block_cols % 2 == 0)[:, None, None]
    top = (block_rows % 2 == 0)[:, None, None]
    half = jnp.concatenate([jnp.where(left, blocks, empty), jnp.where(left, empty, blocks)], axis=2)
    empty = jnp.zeros_like(half)
    return jnp.concatenate([jnp.where(top, half, empty), jnp.where(top, empty, half)], axis=1)


def block_sparse_product(rows_all, blocks, block_rows, block_cols, width, pieces):
    row_total, nao = rows_all.shape
    entries = blocks.shape[0]
    chunks = width // LANE
    piece_chunks = chunks // pieces
    chunk_of = block_cols // 2
    order = jnp.argsort(chunk_of)
    chunk_sorted = chunk_of[order]
    starts = jnp.searchsorted(chunk_sorted, jnp.arange(chunks + 1), side="left").astype(jnp.int32)
    k_sorted = (block_rows[order] // 2).astype(jnp.int32)
    padded = padded_blocks(blocks, block_rows, block_cols)[order]
    results = []
    for piece in range(pieces):
        first = piece * piece_chunks

        def kernel(starts_ref, k_ref, t_ref, g_ref, o_ref, first=first):
            for chunk in range(piece_chunks):
                def body(entry, acc):
                    k = pl.multiple_of(k_ref[entry] * LANE, LANE)
                    return acc + jnp.dot(
                        t_ref[:, pl.ds(k, LANE)], g_ref[entry], preferred_element_type=jnp.float32
                    )

                acc = lax.fori_loop(
                    starts_ref[first + chunk],
                    starts_ref[first + chunk + 1],
                    body,
                    jnp.zeros((row_total, LANE), jnp.float32),
                )
                o_ref[:, chunk * LANE : (chunk + 1) * LANE] = acc.astype(o_ref.dtype)

        grid_spec = pltpu.PrefetchScalarGridSpec(
            num_scalar_prefetch=2,
            grid=(1,),
            in_specs=[
                pl.BlockSpec(
                    (row_total, nao), lambda i, s, k: (0, 0), pipeline_mode=pl.Buffered(1)
                ),
                pl.BlockSpec(
                    (entries, LANE, LANE), lambda i, s, k: (0, 0, 0), pipeline_mode=pl.Buffered(1)
                ),
            ],
            out_specs=pl.BlockSpec((row_total, piece_chunks * LANE), lambda i, s, k: (0, 0)),
        )
        results.append(
            pl.pallas_call(
                kernel,
                grid_spec=grid_spec,
                out_shape=jax.ShapeDtypeStruct((row_total, piece_chunks * LANE), jnp.bfloat16),
                compiler_params=pltpu.CompilerParams(vmem_limit_bytes=60 * 1024 * 1024),
            )(starts, k_sorted, rows_all, padded)
        )
    return results

def per_device(tensor, tensor_pattern, green, green_pattern):
    layer_count = lax.axis_size("layer")
    row_count = lax.axis_size("row")
    if layer_count != row_count:
        return cannon_per_device(tensor, tensor_pattern, green, green_pattern)
    ri_local, mu_local, nu_local = tensor.shape
    tile_rows, tile_cols = green_pattern.shape
    tensor_mask = jnp.repeat(tensor_pattern, BLK, axis=1).astype(jnp.bfloat16)
    masked = tensor * tensor_mask[None, :, :]
    own = masked.reshape(ri_local * mu_local, nu_local)
    layer_index = lax.axis_index("layer")
    col_count = lax.axis_size("col")
    blocks, block_row, block_col = compressed_tile(green, green_pattern)
    blocks, block_row, block_col = (
        lax.all_gather(transposed(part, row_count), ("row", "col"), axis=0)
        for part in (blocks, block_row, block_col)
    )
    band_count = blocks.shape[0]
    band = jnp.arange(band_count)[:, None]
    rows_all = lax.all_gather(own, "layer", axis=1, tiled=True)
    position = band // col_count
    entry_rows = (position * col_count + band % col_count) * tile_rows + block_row
    entry_rows = entry_rows.reshape(-1)
    entry_cols = block_col.reshape(-1)
    entry_blocks = blocks.reshape(-1, BLK, BLK)
    pieces = []
    for start in range(0, ri_local * mu_local, ROW_CHUNK):
        (piece,) = block_sparse_product(
            rows_all[start : start + ROW_CHUNK], entry_blocks, entry_rows, entry_cols, tile_cols * BLK, 1
        )
        pieces.append(transposed(piece, row_count))
    product = jnp.concatenate(pieces, axis=0)
    return product.reshape(ri_local, mu_local, tile_cols * BLK)

def solution(mesh):
    in_specs = (
        P("row", "col", "layer"),
        P("col", "layer"),
        P(("layer", "col"), "row"),
        P(("layer", "col"), "row"),
    )
    out_specs = P("layer", "col", "row")
    return jax.shard_map(
        per_device, mesh=mesh, in_specs=in_specs, out_specs=out_specs, check_vma=False
    )
```

```python
import jax
import jax.numpy as jnp
from jax import lax
from jax.experimental import pallas as pl
from jax.experimental.pallas import tpu as pltpu
from jax.sharding import PartitionSpec as P

BLK = 64
CAP = 48
LANE = 128
ROW_CHUNK = 512


def passed_along(value, axis, by):
    length = lax.axis_size(axis)
    return lax.ppermute(value, axis, [(i, (i + by) % length) for i in range(length)])


def cannon_per_device(tensor, tensor_pattern, green, green_pattern):
    row_count = lax.axis_size("row")
    col_count = lax.axis_size("col")
    col_bits = col_count.bit_length() - 1
    row_index = lax.axis_index("row")
    col_index = lax.axis_index("col")
    odd_row = row_index % 2 == 1
    half_row = row_index // 2
    ri_local, mu_local, nu_local = tensor.shape
    width = nu_local // row_count
    tensor_mask = jnp.repeat(tensor_pattern, BLK, axis=1).astype(jnp.bfloat16)
    masked = tensor * tensor_mask[None, :, :]
    left_block = lax.all_to_all(masked, "row", split_axis=2, concat_axis=0, tiled=True)
    for bit_number in range(col_bits):
        arrived = passed_along(left_block, "row", -(2 << bit_number))
        left_block = jnp.where(col_index >> bit_number & 1 == 1, arrived, left_block)
    ri_total = left_block.shape[0]
    all_rows = ri_total * mu_local
    left_block = left_block.reshape(all_rows, width)
    tile_rows, tile_cols = green_pattern.shape
    green_mask = green_pattern.astype(jnp.bfloat16)[:, None, :, None]
    green_tile = (green.reshape(tile_rows, BLK, tile_cols, BLK) * green_mask).reshape(
        tile_rows * BLK, tile_cols * BLK
    )
    green_state = green_tile
    for bit_number in range(col_bits):
        arrived = passed_along(green_state, "col", -(1 << bit_number))
        green_state = jnp.where(half_row >> bit_number & 1 == 1, arrived, green_state)

    def advance(current_state):
        arrived_state = passed_along(current_state, "col", -1)
        return (arrived_state, arrived_state)

    def shift_left(block_now):
        return passed_along(block_now, "row", -1)

    def pair_turn(state_now, shift_last):
        product_sum, block_now, current_state, current = state_now
        green_half = jnp.where(odd_row, current[width:], current[:width])
        product_sum = product_sum + jnp.dot(
            block_now, green_half, preferred_element_type=jnp.float32
        )
        block_now = shift_left(block_now)
        previous = current
        current_state, current = advance(current_state)
        green_half = jnp.where(odd_row, current[:width], previous[width:])
        product_sum = product_sum + jnp.dot(
            block_now, green_half, preferred_element_type=jnp.float32
        )
        if shift_last:
            block_now = shift_left(block_now)
        return (product_sum, block_now, current_state, current)

    start = (
        jnp.zeros((all_rows, tile_cols * BLK), jnp.float32),
        left_block,
        green_state,
        green_state,
    )
    state_now = lax.fori_loop(
        0, col_count - 1, lambda turn_index, state_before: pair_turn(state_before, True), start
    )
    state_now = pair_turn(state_now, False)
    layer_terms = state_now[0].reshape(ri_total, mu_local, tile_cols * BLK)
    return lax.psum_scatter(layer_terms, "layer", scatter_dimension=0, tiled=True).astype(
        jnp.bfloat16
    )


def transposed(value, size):
    return lax.ppermute(
        value,
        ("layer", "row"),
        [(a * size + b, b * size + a) for a in range(size) for b in range(size)],
    )


def gathered_windows(green, window_rows, window_cols):
    count = window_rows.shape[0]

    def kernel(rows_ref, cols_ref, green_ref, out_ref):
        out_ref[0] = green_ref[...]

    grid_spec = pltpu.PrefetchScalarGridSpec(
        num_scalar_prefetch=2,
        grid=(count,),
        in_specs=[pl.BlockSpec((BLK, LANE), lambda e, r, c: (r[e], c[e]))],
        out_specs=pl.BlockSpec((1, BLK, LANE), lambda e, r, c: (e, 0, 0)),
    )
    return pl.pallas_call(
        kernel,
        grid_spec=grid_spec,
        out_shape=jax.ShapeDtypeStruct((count, BLK, LANE), green.dtype),
    )(window_rows.astype(jnp.int32), window_cols.astype(jnp.int32), green)


def compressed_tile(green, green_pattern):
    tile_rows, tile_cols = green_pattern.shape
    cap = min(CAP, tile_rows * tile_cols)
    flat = green_pattern.reshape(-1)
    (spots,) = jnp.nonzero(flat != 0, size=cap, fill_value=0)
    valid = jnp.arange(cap) < jnp.sum(flat != 0)
    block_row = spots // tile_cols
    block_col = spots % tile_cols
    windows = gathered_windows(green, block_row, block_col // 2)
    left = (block_col % 2 == 0)[:, None, None]
    blocks = jnp.where(left, windows[:, :, :BLK], windows[:, :, BLK:])
    scale = jnp.where(valid, flat[spots], 0).astype(jnp.bfloat16)
    blocks = blocks * scale[:, None, None]
    return blocks, block_row, block_col


def padded_blocks(blocks, block_rows, block_cols):
    empty = jnp.zeros_like(blocks)
    left = (block_cols % 2 == 0)[:, None, None]
    top = (block_rows % 2 == 0)[:, None, None]
    half = jnp.concatenate([jnp.where(left, blocks, empty), jnp.where(left, empty, blocks)], axis=2)
    empty = jnp.zeros_like(half)
    return jnp.concatenate([jnp.where(top, half, empty), jnp.where(top, empty, half)], axis=1)


def block_sparse_product(rows_all, blocks, block_rows, block_cols, width, pieces):
    row_total, nao = rows_all.shape
    entries = blocks.shape[0]
    chunks = width // LANE
    piece_chunks = chunks // pieces
    chunk_of = block_cols // 2
    order = jnp.argsort(chunk_of)
    chunk_sorted = chunk_of[order]
    starts = jnp.searchsorted(chunk_sorted, jnp.arange(chunks + 1), side="left").astype(jnp.int32)
    k_sorted = (block_rows[order] // 2).astype(jnp.int32)
    padded = padded_blocks(blocks, block_rows, block_cols)[order]
    results = []
    for piece in range(pieces):
        first = piece * piece_chunks

        def kernel(starts_ref, k_ref, t_ref, g_ref, o_ref, first=first):
            def window(entry):
                return t_ref[:, pl.ds(pl.multiple_of(k_ref[entry] * LANE, LANE), LANE)]

            def one(entry, acc):
                return acc + jnp.dot(window(entry), g_ref[entry], preferred_element_type=jnp.float32)

            for chunk in range(piece_chunks):
                begin = starts_ref[first + chunk]
                end = starts_ref[first + chunk + 1]
                pairs = (end - begin) // 2

                def two(pair, acc, begin=begin):
                    entry = begin + 2 * pair
                    lhs = jnp.concatenate([window(entry), window(entry + 1)], axis=1)
                    rhs = jnp.concatenate([g_ref[entry], g_ref[entry + 1]], axis=0)
                    return acc + jnp.dot(lhs, rhs, preferred_element_type=jnp.float32)

                acc = lax.fori_loop(0, pairs, two, jnp.zeros((row_total, LANE), jnp.float32))
                acc = lax.fori_loop(begin + 2 * pairs, end, one, acc)
                o_ref[:, chunk * LANE : (chunk + 1) * LANE] = acc.astype(o_ref.dtype)

        grid_spec = pltpu.PrefetchScalarGridSpec(
            num_scalar_prefetch=2,
            grid=(1,),
            in_specs=[
                pl.BlockSpec(
                    (row_total, nao), lambda i, s, k: (0, 0), pipeline_mode=pl.Buffered(1)
                ),
                pl.BlockSpec(
                    (entries, LANE, LANE), lambda i, s, k: (0, 0, 0), pipeline_mode=pl.Buffered(1)
                ),
            ],
            out_specs=pl.BlockSpec((row_total, piece_chunks * LANE), lambda i, s, k: (0, 0)),
        )
        results.append(
            pl.pallas_call(
                kernel,
                grid_spec=grid_spec,
                out_shape=jax.ShapeDtypeStruct((row_total, piece_chunks * LANE), jnp.bfloat16),
                compiler_params=pltpu.CompilerParams(vmem_limit_bytes=60 * 1024 * 1024),
            )(starts, k_sorted, rows_all, padded)
        )
    return results

def per_device(tensor, tensor_pattern, green, green_pattern):
    layer_count = lax.axis_size("layer")
    row_count = lax.axis_size("row")
    if layer_count != row_count:
        return cannon_per_device(tensor, tensor_pattern, green, green_pattern)
    ri_local, mu_local, nu_local = tensor.shape
    tile_rows, tile_cols = green_pattern.shape
    tensor_mask = jnp.repeat(tensor_pattern, BLK, axis=1).astype(jnp.bfloat16)
    masked = tensor * tensor_mask[None, :, :]
    own = masked.reshape(ri_local * mu_local, nu_local)
    layer_index = lax.axis_index("layer")
    col_count = lax.axis_size("col")
    blocks, block_row, block_col = compressed_tile(green, green_pattern)
    blocks, block_row, block_col = (
        lax.all_gather(transposed(part, row_count), ("row", "col"), axis=0)
        for part in (blocks, block_row, block_col)
    )
    band_count = blocks.shape[0]
    band = jnp.arange(band_count)[:, None]
    rows_all = lax.all_gather(own, "layer", axis=1, tiled=True)
    position = band // col_count
    entry_rows = (position * col_count + band % col_count) * tile_rows + block_row
    entry_rows = entry_rows.reshape(-1)
    entry_cols = block_col.reshape(-1)
    entry_blocks = blocks.reshape(-1, BLK, BLK)
    pieces = []
    for start in range(0, ri_local * mu_local, ROW_CHUNK):
        (piece,) = block_sparse_product(
            rows_all[start : start + ROW_CHUNK], entry_blocks, entry_rows, entry_cols, tile_cols * BLK, 1
        )
        pieces.append(transposed(piece, row_count))
    product = jnp.concatenate(pieces, axis=0)
    return product.reshape(ri_local, mu_local, tile_cols * BLK)

def solution(mesh):
    in_specs = (
        P("row", "col", "layer"),
        P("col", "layer"),
        P(("layer", "col"), "row"),
        P(("layer", "col"), "row"),
    )
    out_specs = P("layer", "col", "row")
    return jax.shard_map(
        per_device, mesh=mesh, in_specs=in_specs, out_specs=out_specs, check_vma=False
    )
```

```python
import jax
import jax.numpy as jnp
from jax import lax
from jax.experimental import pallas as pl
from jax.experimental.pallas import tpu as pltpu
from jax.sharding import PartitionSpec as P

BLK = 64
CAP = 48
LANE = 128
ROW_CHUNK = 512


def passed_along(value, axis, by):
    length = lax.axis_size(axis)
    return lax.ppermute(value, axis, [(i, (i + by) % length) for i in range(length)])


def cannon_per_device(tensor, tensor_pattern, green, green_pattern):
    row_count = lax.axis_size("row")
    col_count = lax.axis_size("col")
    col_bits = col_count.bit_length() - 1
    row_index = lax.axis_index("row")
    col_index = lax.axis_index("col")
    odd_row = row_index % 2 == 1
    half_row = row_index // 2
    ri_local, mu_local, nu_local = tensor.shape
    width = nu_local // row_count
    tensor_mask = jnp.repeat(tensor_pattern, BLK, axis=1).astype(jnp.bfloat16)
    masked = tensor * tensor_mask[None, :, :]
    left_block = lax.all_to_all(masked, "row", split_axis=2, concat_axis=0, tiled=True)
    for bit_number in range(col_bits):
        arrived = passed_along(left_block, "row", -(2 << bit_number))
        left_block = jnp.where(col_index >> bit_number & 1 == 1, arrived, left_block)
    ri_total = left_block.shape[0]
    all_rows = ri_total * mu_local
    left_block = left_block.reshape(all_rows, width)
    tile_rows, tile_cols = green_pattern.shape
    green_mask = green_pattern.astype(jnp.bfloat16)[:, None, :, None]
    green_tile = (green.reshape(tile_rows, BLK, tile_cols, BLK) * green_mask).reshape(
        tile_rows * BLK, tile_cols * BLK
    )
    green_state = green_tile
    for bit_number in range(col_bits):
        arrived = passed_along(green_state, "col", -(1 << bit_number))
        green_state = jnp.where(half_row >> bit_number & 1 == 1, arrived, green_state)

    def advance(current_state):
        arrived_state = passed_along(current_state, "col", -1)
        return (arrived_state, arrived_state)

    def shift_left(block_now):
        return passed_along(block_now, "row", -1)

    def pair_turn(state_now, shift_last):
        product_sum, block_now, current_state, current = state_now
        green_half = jnp.where(odd_row, current[width:], current[:width])
        product_sum = product_sum + jnp.dot(
            block_now, green_half, preferred_element_type=jnp.float32
        )
        block_now = shift_left(block_now)
        previous = current
        current_state, current = advance(current_state)
        green_half = jnp.where(odd_row, current[:width], previous[width:])
        product_sum = product_sum + jnp.dot(
            block_now, green_half, preferred_element_type=jnp.float32
        )
        if shift_last:
            block_now = shift_left(block_now)
        return (product_sum, block_now, current_state, current)

    start = (
        jnp.zeros((all_rows, tile_cols * BLK), jnp.float32),
        left_block,
        green_state,
        green_state,
    )
    state_now = lax.fori_loop(
        0, col_count - 1, lambda turn_index, state_before: pair_turn(state_before, True), start
    )
    state_now = pair_turn(state_now, False)
    layer_terms = state_now[0].reshape(ri_total, mu_local, tile_cols * BLK)
    return lax.psum_scatter(layer_terms, "layer", scatter_dimension=0, tiled=True).astype(
        jnp.bfloat16
    )


def transposed(value, size):
    return lax.ppermute(
        value,
        ("layer", "row"),
        [(a * size + b, b * size + a) for a in range(size) for b in range(size)],
    )


def gathered_windows(green, window_rows, window_cols):
    count = window_rows.shape[0]

    def kernel(rows_ref, cols_ref, green_ref, out_ref):
        out_ref[0] = green_ref[...]

    grid_spec = pltpu.PrefetchScalarGridSpec(
        num_scalar_prefetch=2,
        grid=(count,),
        in_specs=[pl.BlockSpec((BLK, LANE), lambda e, r, c: (r[e], c[e]))],
        out_specs=pl.BlockSpec((1, BLK, LANE), lambda e, r, c: (e, 0, 0)),
    )
    return pl.pallas_call(
        kernel,
        grid_spec=grid_spec,
        out_shape=jax.ShapeDtypeStruct((count, BLK, LANE), green.dtype),
    )(window_rows.astype(jnp.int32), window_cols.astype(jnp.int32), green)


def compressed_tile(green, green_pattern):
    tile_rows, tile_cols = green_pattern.shape
    cap = min(CAP, tile_rows * tile_cols)
    flat = green_pattern.reshape(-1)
    (spots,) = jnp.nonzero(flat != 0, size=cap, fill_value=0)
    valid = jnp.arange(cap) < jnp.sum(flat != 0)
    block_row = spots // tile_cols
    block_col = spots % tile_cols
    windows = gathered_windows(green, block_row, block_col // 2)
    left = (block_col % 2 == 0)[:, None, None]
    blocks = jnp.where(left, windows[:, :, :BLK], windows[:, :, BLK:])
    scale = jnp.where(valid, flat[spots], 0).astype(jnp.bfloat16)
    blocks = blocks * scale[:, None, None]
    return blocks, block_row, block_col


def padded_blocks(blocks, block_rows, block_cols):
    empty = jnp.zeros_like(blocks)
    left = (block_cols % 2 == 0)[:, None, None]
    top = (block_rows % 2 == 0)[:, None, None]
    half = jnp.concatenate([jnp.where(left, blocks, empty), jnp.where(left, empty, blocks)], axis=2)
    empty = jnp.zeros_like(half)
    return jnp.concatenate([jnp.where(top, half, empty), jnp.where(top, empty, half)], axis=1)


def block_sparse_product(rows_all, blocks, block_rows, block_cols, width, pieces):
    row_total, nao = rows_all.shape
    entries = blocks.shape[0]
    chunks = width // LANE
    piece_chunks = chunks // pieces
    chunk_of = block_cols // 2
    order = jnp.argsort(chunk_of)
    chunk_sorted = chunk_of[order]
    starts = jnp.searchsorted(chunk_sorted, jnp.arange(chunks + 1), side="left").astype(jnp.int32)
    k_sorted = (block_rows[order] // 2).astype(jnp.int32)
    padded = padded_blocks(blocks, block_rows, block_cols)[order]
    results = []
    for piece in range(pieces):
        first = piece * piece_chunks

        def kernel(starts_ref, k_ref, t_ref, g_ref, o_ref, first=first):
            def window(entry):
                return t_ref[:, pl.ds(pl.multiple_of(k_ref[entry] * LANE, LANE), LANE)]

            def one(entry, acc):
                return acc + jnp.dot(window(entry), g_ref[entry], preferred_element_type=jnp.float32)

            for chunk in range(piece_chunks):
                begin = starts_ref[first + chunk]
                end = starts_ref[first + chunk + 1]
                pairs = (end - begin) // 2

                def two(pair, acc, begin=begin):
                    entry = begin + 2 * pair
                    lhs = jnp.concatenate([window(entry), window(entry + 1)], axis=1)
                    rhs = jnp.concatenate([g_ref[entry], g_ref[entry + 1]], axis=0)
                    return acc + jnp.dot(lhs, rhs, preferred_element_type=jnp.float32)

                acc = lax.fori_loop(0, pairs, two, jnp.zeros((row_total, LANE), jnp.float32))
                acc = lax.fori_loop(begin + 2 * pairs, end, one, acc)
                o_ref[:, chunk * LANE : (chunk + 1) * LANE] = acc.astype(o_ref.dtype)

        grid_spec = pltpu.PrefetchScalarGridSpec(
            num_scalar_prefetch=2,
            grid=(1,),
            in_specs=[
                pl.BlockSpec(
                    (row_total, nao), lambda i, s, k: (0, 0), pipeline_mode=pl.Buffered(1)
                ),
                pl.BlockSpec(
                    (entries, LANE, LANE), lambda i, s, k: (0, 0, 0), pipeline_mode=pl.Buffered(1)
                ),
            ],
            out_specs=pl.BlockSpec((row_total, piece_chunks * LANE), lambda i, s, k: (0, 0)),
        )
        results.append(
            pl.pallas_call(
                kernel,
                grid_spec=grid_spec,
                out_shape=jax.ShapeDtypeStruct((row_total, piece_chunks * LANE), jnp.bfloat16),
                compiler_params=pltpu.CompilerParams(vmem_limit_bytes=60 * 1024 * 1024),
            )(starts, k_sorted, rows_all, padded)
        )
    return results

def per_device(tensor, tensor_pattern, green, green_pattern):
    layer_count = lax.axis_size("layer")
    row_count = lax.axis_size("row")
    if layer_count != row_count:
        return cannon_per_device(tensor, tensor_pattern, green, green_pattern)
    ri_local, mu_local, nu_local = tensor.shape
    tile_rows, tile_cols = green_pattern.shape
    tensor_mask = jnp.repeat(tensor_pattern, BLK, axis=1).astype(jnp.bfloat16)
    masked = tensor * tensor_mask[None, :, :]
    own = masked.reshape(ri_local * mu_local, nu_local)
    layer_index = lax.axis_index("layer")
    col_count = lax.axis_size("col")
    blocks, block_row, block_col = compressed_tile(green, green_pattern)
    blocks, block_row, block_col = (
        lax.all_gather(transposed(part, row_count), ("row", "col"), axis=0)
        for part in (blocks, block_row, block_col)
    )
    band_count = blocks.shape[0]
    band = jnp.arange(band_count)[:, None]
    position = band // col_count
    entry_rows = (position * col_count + band % col_count) * tile_rows + block_row
    entry_rows = entry_rows.reshape(-1)
    entry_cols = block_col.reshape(-1)
    entry_blocks = blocks.reshape(-1, BLK, BLK)
    pieces = []
    for start in range(0, ri_local * mu_local, ROW_CHUNK):
        rows = lax.all_gather(own[start : start + ROW_CHUNK], "layer", axis=1, tiled=True)
        (piece,) = block_sparse_product(
            rows, entry_blocks, entry_rows, entry_cols, tile_cols * BLK, 1
        )
        pieces.append(transposed(piece, row_count))
    product = jnp.concatenate(pieces, axis=0)
    return product.reshape(ri_local, mu_local, tile_cols * BLK)

def solution(mesh):
    in_specs = (
        P("row", "col", "layer"),
        P("col", "layer"),
        P(("layer", "col"), "row"),
        P(("layer", "col"), "row"),
    )
    out_specs = P("layer", "col", "row")
    return jax.shard_map(
        per_device, mesh=mesh, in_specs=in_specs, out_specs=out_specs, check_vma=False
    )
```

```python
import jax
import jax.numpy as jnp
from jax import lax
from jax.experimental import pallas as pl
from jax.experimental.pallas import tpu as pltpu
from jax.sharding import PartitionSpec as P

BLK = 64
CAP = 48
LANE = 128
ROW_CHUNK = 512


def passed_along(value, axis, by):
    length = lax.axis_size(axis)
    return lax.ppermute(value, axis, [(i, (i + by) % length) for i in range(length)])


def cannon_per_device(tensor, tensor_pattern, green, green_pattern):
    row_count = lax.axis_size("row")
    col_count = lax.axis_size("col")
    col_bits = col_count.bit_length() - 1
    row_index = lax.axis_index("row")
    col_index = lax.axis_index("col")
    odd_row = row_index % 2 == 1
    half_row = row_index // 2
    ri_local, mu_local, nu_local = tensor.shape
    width = nu_local // row_count
    tensor_mask = jnp.repeat(tensor_pattern, BLK, axis=1).astype(jnp.bfloat16)
    masked = tensor * tensor_mask[None, :, :]
    left_block = lax.all_to_all(masked, "row", split_axis=2, concat_axis=0, tiled=True)
    for bit_number in range(col_bits):
        arrived = passed_along(left_block, "row", -(2 << bit_number))
        left_block = jnp.where(col_index >> bit_number & 1 == 1, arrived, left_block)
    ri_total = left_block.shape[0]
    all_rows = ri_total * mu_local
    left_block = left_block.reshape(all_rows, width)
    tile_rows, tile_cols = green_pattern.shape
    green_mask = green_pattern.astype(jnp.bfloat16)[:, None, :, None]
    green_tile = (green.reshape(tile_rows, BLK, tile_cols, BLK) * green_mask).reshape(
        tile_rows * BLK, tile_cols * BLK
    )
    green_state = green_tile
    for bit_number in range(col_bits):
        arrived = passed_along(green_state, "col", -(1 << bit_number))
        green_state = jnp.where(half_row >> bit_number & 1 == 1, arrived, green_state)

    def advance(current_state):
        arrived_state = passed_along(current_state, "col", -1)
        return (arrived_state, arrived_state)

    def shift_left(block_now):
        return passed_along(block_now, "row", -1)

    def pair_turn(state_now, shift_last):
        product_sum, block_now, current_state, current = state_now
        green_half = jnp.where(odd_row, current[width:], current[:width])
        product_sum = product_sum + jnp.dot(
            block_now, green_half, preferred_element_type=jnp.float32
        )
        block_now = shift_left(block_now)
        previous = current
        current_state, current = advance(current_state)
        green_half = jnp.where(odd_row, current[:width], previous[width:])
        product_sum = product_sum + jnp.dot(
            block_now, green_half, preferred_element_type=jnp.float32
        )
        if shift_last:
            block_now = shift_left(block_now)
        return (product_sum, block_now, current_state, current)

    start = (
        jnp.zeros((all_rows, tile_cols * BLK), jnp.float32),
        left_block,
        green_state,
        green_state,
    )
    state_now = lax.fori_loop(
        0, col_count - 1, lambda turn_index, state_before: pair_turn(state_before, True), start
    )
    state_now = pair_turn(state_now, False)
    layer_terms = state_now[0].reshape(ri_total, mu_local, tile_cols * BLK)
    return lax.psum_scatter(layer_terms, "layer", scatter_dimension=0, tiled=True).astype(
        jnp.bfloat16
    )


def spread(size):
    return [2, 0, 3, 1] if size == 4 else list(range(size))


def green_to_layers(value, size):
    inverse = {quarter: layer for layer, quarter in enumerate(spread(size))}
    return lax.ppermute(
        value,
        ("layer", "row"),
        [(a * size + b, inverse[b] * size + a) for a in range(size) for b in range(size)],
    )


def product_to_owners(value, size):
    quarter = spread(size)
    return lax.ppermute(
        value,
        ("layer", "row"),
        [(a * size + b, b * size + quarter[a]) for a in range(size) for b in range(size)],
    )


def gathered_windows(green, window_rows, window_cols):
    count = window_rows.shape[0]

    def kernel(rows_ref, cols_ref, green_ref, out_ref):
        out_ref[0] = green_ref[...]

    grid_spec = pltpu.PrefetchScalarGridSpec(
        num_scalar_prefetch=2,
        grid=(count,),
        in_specs=[pl.BlockSpec((BLK, LANE), lambda e, r, c: (r[e], c[e]))],
        out_specs=pl.BlockSpec((1, BLK, LANE), lambda e, r, c: (e, 0, 0)),
    )
    return pl.pallas_call(
        kernel,
        grid_spec=grid_spec,
        out_shape=jax.ShapeDtypeStruct((count, BLK, LANE), green.dtype),
    )(window_rows.astype(jnp.int32), window_cols.astype(jnp.int32), green)


def compressed_tile(green, green_pattern):
    tile_rows, tile_cols = green_pattern.shape
    cap = min(CAP, tile_rows * tile_cols)
    flat = green_pattern.reshape(-1)
    (spots,) = jnp.nonzero(flat != 0, size=cap, fill_value=0)
    valid = jnp.arange(cap) < jnp.sum(flat != 0)
    block_row = spots // tile_cols
    block_col = spots % tile_cols
    windows = gathered_windows(green, block_row, block_col // 2)
    left = (block_col % 2 == 0)[:, None, None]
    blocks = jnp.where(left, windows[:, :, :BLK], windows[:, :, BLK:])
    scale = jnp.where(valid, flat[spots], 0).astype(jnp.bfloat16)
    blocks = blocks * scale[:, None, None]
    return blocks, block_row, block_col


def padded_blocks(blocks, block_rows, block_cols):
    empty = jnp.zeros_like(blocks)
    left = (block_cols % 2 == 0)[:, None, None]
    top = (block_rows % 2 == 0)[:, None, None]
    half = jnp.concatenate([jnp.where(left, blocks, empty), jnp.where(left, empty, blocks)], axis=2)
    empty = jnp.zeros_like(half)
    return jnp.concatenate([jnp.where(top, half, empty), jnp.where(top, empty, half)], axis=1)


def block_sparse_product(rows_all, blocks, block_rows, block_cols, width, pieces):
    row_total, nao = rows_all.shape
    entries = blocks.shape[0]
    chunks = width // LANE
    piece_chunks = chunks // pieces
    chunk_of = block_cols // 2
    order = jnp.argsort(chunk_of)
    chunk_sorted = chunk_of[order]
    starts = jnp.searchsorted(chunk_sorted, jnp.arange(chunks + 1), side="left", method="compare_all").astype(jnp.int32)
    k_sorted = (block_rows[order] // 2).astype(jnp.int32)
    padded = padded_blocks(blocks, block_rows, block_cols)[order]
    results = []
    for piece in range(pieces):
        first = piece * piece_chunks

        def kernel(starts_ref, k_ref, t_ref, g_ref, o_ref, first=first):
            def window(entry):
                return t_ref[:, pl.ds(pl.multiple_of(k_ref[entry] * LANE, LANE), LANE)]

            def one(entry, acc):
                return acc + jnp.dot(window(entry), g_ref[entry], preferred_element_type=jnp.float32)

            for chunk in range(piece_chunks):
                begin = starts_ref[first + chunk]
                end = starts_ref[first + chunk + 1]
                pairs = (end - begin) // 2

                def two(pair, acc, begin=begin):
                    entry = begin + 2 * pair
                    lhs = jnp.concatenate([window(entry), window(entry + 1)], axis=1)
                    rhs = jnp.concatenate([g_ref[entry], g_ref[entry + 1]], axis=0)
                    return acc + jnp.dot(lhs, rhs, preferred_element_type=jnp.float32)

                acc = lax.fori_loop(0, pairs, two, jnp.zeros((row_total, LANE), jnp.float32))
                acc = lax.fori_loop(begin + 2 * pairs, end, one, acc)
                o_ref[:, chunk * LANE : (chunk + 1) * LANE] = acc.astype(o_ref.dtype)

        grid_spec = pltpu.PrefetchScalarGridSpec(
            num_scalar_prefetch=2,
            grid=(1,),
            in_specs=[
                pl.BlockSpec(
                    (row_total, nao), lambda i, s, k: (0, 0), pipeline_mode=pl.Buffered(1)
                ),
                pl.BlockSpec(
                    (entries, LANE, LANE), lambda i, s, k: (0, 0, 0), pipeline_mode=pl.Buffered(1)
                ),
            ],
            out_specs=pl.BlockSpec((row_total, piece_chunks * LANE), lambda i, s, k: (0, 0)),
        )
        results.append(
            pl.pallas_call(
                kernel,
                grid_spec=grid_spec,
                out_shape=jax.ShapeDtypeStruct((row_total, piece_chunks * LANE), jnp.bfloat16),
                compiler_params=pltpu.CompilerParams(vmem_limit_bytes=60 * 1024 * 1024),
            )(starts, k_sorted, rows_all, padded)
        )
    return results

def per_device(tensor, tensor_pattern, green, green_pattern):
    layer_count = lax.axis_size("layer")
    row_count = lax.axis_size("row")
    if layer_count != row_count:
        return cannon_per_device(tensor, tensor_pattern, green, green_pattern)
    ri_local, mu_local, nu_local = tensor.shape
    tile_rows, tile_cols = green_pattern.shape
    tensor_mask = jnp.repeat(tensor_pattern, BLK, axis=1).astype(jnp.bfloat16)
    masked = tensor * tensor_mask[None, :, :]
    own = masked.reshape(ri_local * mu_local, nu_local)
    layer_index = lax.axis_index("layer")
    col_count = lax.axis_size("col")
    blocks, block_row, block_col = compressed_tile(green, green_pattern)
    blocks, block_row, block_col = (
        lax.all_gather(green_to_layers(part, row_count), ("row", "col"), axis=0)
        for part in (blocks, block_row, block_col)
    )
    band_count = blocks.shape[0]
    band = jnp.arange(band_count)[:, None]
    position = band // col_count
    entry_rows = (position * col_count + band % col_count) * tile_rows + block_row
    entry_rows = entry_rows.reshape(-1)
    entry_cols = block_col.reshape(-1)
    entry_blocks = blocks.reshape(-1, BLK, BLK)
    pieces = []
    for start in range(0, ri_local * mu_local, ROW_CHUNK):
        rows = lax.all_gather(own[start : start + ROW_CHUNK], "layer", axis=1, tiled=True)
        (piece,) = block_sparse_product(
            rows, entry_blocks, entry_rows, entry_cols, tile_cols * BLK, 1
        )
        pieces.append(product_to_owners(piece, row_count))
    product = jnp.concatenate(pieces, axis=0)
    return product.reshape(ri_local, mu_local, tile_cols * BLK)

def solution(mesh):
    in_specs = (
        P("row", "col", "layer"),
        P("col", "layer"),
        P(("layer", "col"), "row"),
        P(("layer", "col"), "row"),
    )
    out_specs = P("layer", "col", "row")
    return jax.shard_map(
        per_device, mesh=mesh, in_specs=in_specs, out_specs=out_specs, check_vma=False
    )
```

```python
import jax
import jax.numpy as jnp
from jax import lax
from jax.experimental import pallas as pl
from jax.experimental.pallas import tpu as pltpu
from jax.sharding import PartitionSpec as P

BLK = 64
CAP = 48
LANE = 128
ROW_CHUNK = 512


def passed_along(value, axis, by):
    length = lax.axis_size(axis)
    return lax.ppermute(value, axis, [(i, (i + by) % length) for i in range(length)])


def cannon_per_device(tensor, tensor_pattern, green, green_pattern):
    row_count = lax.axis_size("row")
    col_count = lax.axis_size("col")
    col_bits = col_count.bit_length() - 1
    row_index = lax.axis_index("row")
    col_index = lax.axis_index("col")
    odd_row = row_index % 2 == 1
    half_row = row_index // 2
    ri_local, mu_local, nu_local = tensor.shape
    width = nu_local // row_count
    tensor_mask = jnp.repeat(tensor_pattern, BLK, axis=1).astype(jnp.bfloat16)
    masked = tensor * tensor_mask[None, :, :]
    left_block = lax.all_to_all(masked, "row", split_axis=2, concat_axis=0, tiled=True)
    for bit_number in range(col_bits):
        arrived = passed_along(left_block, "row", -(2 << bit_number))
        left_block = jnp.where(col_index >> bit_number & 1 == 1, arrived, left_block)
    ri_total = left_block.shape[0]
    all_rows = ri_total * mu_local
    left_block = left_block.reshape(all_rows, width)
    tile_rows, tile_cols = green_pattern.shape
    green_mask = green_pattern.astype(jnp.bfloat16)[:, None, :, None]
    green_tile = (green.reshape(tile_rows, BLK, tile_cols, BLK) * green_mask).reshape(
        tile_rows * BLK, tile_cols * BLK
    )
    green_state = green_tile
    for bit_number in range(col_bits):
        arrived = passed_along(green_state, "col", -(1 << bit_number))
        green_state = jnp.where(half_row >> bit_number & 1 == 1, arrived, green_state)

    def advance(current_state):
        arrived_state = passed_along(current_state, "col", -1)
        return (arrived_state, arrived_state)

    def shift_left(block_now):
        return passed_along(block_now, "row", -1)

    def pair_turn(state_now, shift_last):
        product_sum, block_now, current_state, current = state_now
        green_half = jnp.where(odd_row, current[width:], current[:width])
        product_sum = product_sum + jnp.dot(
            block_now, green_half, preferred_element_type=jnp.float32
        )
        block_now = shift_left(block_now)
        previous = current
        current_state, current = advance(current_state)
        green_half = jnp.where(odd_row, current[:width], previous[width:])
        product_sum = product_sum + jnp.dot(
            block_now, green_half, preferred_element_type=jnp.float32
        )
        if shift_last:
            block_now = shift_left(block_now)
        return (product_sum, block_now, current_state, current)

    start = (
        jnp.zeros((all_rows, tile_cols * BLK), jnp.float32),
        left_block,
        green_state,
        green_state,
    )
    state_now = lax.fori_loop(
        0, col_count - 1, lambda turn_index, state_before: pair_turn(state_before, True), start
    )
    state_now = pair_turn(state_now, False)
    layer_terms = state_now[0].reshape(ri_total, mu_local, tile_cols * BLK)
    return lax.psum_scatter(layer_terms, "layer", scatter_dimension=0, tiled=True).astype(
        jnp.bfloat16
    )


def spread(size):
    return [2, 0, 3, 1] if size == 4 else list(range(size))


def green_to_layers(value, size):
    inverse = {quarter: layer for layer, quarter in enumerate(spread(size))}
    return lax.ppermute(
        value,
        ("layer", "row"),
        [(a * size + b, inverse[b] * size + a) for a in range(size) for b in range(size)],
    )


def product_to_owners(value, size):
    quarter = spread(size)
    return lax.ppermute(
        value,
        ("layer", "row"),
        [(a * size + b, b * size + quarter[a]) for a in range(size) for b in range(size)],
    )


def gathered_windows(green, window_rows, window_cols):
    count = window_rows.shape[0]

    def kernel(rows_ref, cols_ref, green_ref, out_ref):
        out_ref[0] = green_ref[...]

    grid_spec = pltpu.PrefetchScalarGridSpec(
        num_scalar_prefetch=2,
        grid=(count,),
        in_specs=[pl.BlockSpec((BLK, LANE), lambda e, r, c: (r[e], c[e]))],
        out_specs=pl.BlockSpec((1, BLK, LANE), lambda e, r, c: (e, 0, 0)),
    )
    return pl.pallas_call(
        kernel,
        grid_spec=grid_spec,
        out_shape=jax.ShapeDtypeStruct((count, BLK, LANE), green.dtype),
    )(window_rows.astype(jnp.int32), window_cols.astype(jnp.int32), green)


def compressed_tile(green, green_pattern):
    tile_rows, tile_cols = green_pattern.shape
    cap = min(CAP, tile_rows * tile_cols)
    flat = green_pattern.reshape(-1)
    (spots,) = jnp.nonzero(flat != 0, size=cap, fill_value=0)
    valid = jnp.arange(cap) < jnp.sum(flat != 0)
    block_row = spots // tile_cols
    block_col = spots % tile_cols
    windows = gathered_windows(green, block_row, block_col // 2)
    left = (block_col % 2 == 0)[:, None, None]
    blocks = jnp.where(left, windows[:, :, :BLK], windows[:, :, BLK:])
    scale = jnp.where(valid, flat[spots], 0).astype(jnp.bfloat16)
    blocks = blocks * scale[:, None, None]
    return blocks, block_row, block_col


def padded_blocks(blocks, block_rows, block_cols):
    empty = jnp.zeros_like(blocks)
    left = (block_cols % 2 == 0)[:, None, None]
    top = (block_rows % 2 == 0)[:, None, None]
    half = jnp.concatenate([jnp.where(left, blocks, empty), jnp.where(left, empty, blocks)], axis=2)
    empty = jnp.zeros_like(half)
    return jnp.concatenate([jnp.where(top, half, empty), jnp.where(top, empty, half)], axis=1)


def block_sparse_product(rows_all, blocks, block_rows, block_cols, width, pieces):
    row_total, nao = rows_all.shape
    entries = blocks.shape[0]
    chunks = width // LANE
    piece_chunks = chunks // pieces
    chunk_of = block_cols // 2
    order = jnp.argsort(chunk_of)
    chunk_sorted = chunk_of[order]
    starts = jnp.searchsorted(chunk_sorted, jnp.arange(chunks + 1), side="left", method="compare_all").astype(jnp.int32)
    k_sorted = (block_rows[order] // 2).astype(jnp.int32)
    padded = padded_blocks(blocks, block_rows, block_cols)[order]
    results = []
    for piece in range(pieces):
        first = piece * piece_chunks

        def kernel(starts_ref, k_ref, t_ref, g_ref, o_ref, first=first):
            def window(entry):
                return t_ref[:, pl.ds(pl.multiple_of(k_ref[entry] * LANE, LANE), LANE)]

            def one(entry, acc):
                return acc + jnp.dot(window(entry), g_ref[entry], preferred_element_type=jnp.float32)

            for chunk in range(piece_chunks):
                begin = starts_ref[first + chunk]
                end = starts_ref[first + chunk + 1]
                pairs = (end - begin) // 2

                def two(pair, acc, begin=begin):
                    entry = begin + 2 * pair
                    lhs = jnp.concatenate([window(entry), window(entry + 1)], axis=1)
                    rhs = jnp.concatenate([g_ref[entry], g_ref[entry + 1]], axis=0)
                    return acc + jnp.dot(lhs, rhs, preferred_element_type=jnp.float32)

                acc = lax.fori_loop(0, pairs, two, jnp.zeros((row_total, LANE), jnp.float32))
                acc = lax.fori_loop(begin + 2 * pairs, end, one, acc)
                o_ref[:, chunk * LANE : (chunk + 1) * LANE] = acc.astype(o_ref.dtype)

        grid_spec = pltpu.PrefetchScalarGridSpec(
            num_scalar_prefetch=2,
            grid=(1,),
            in_specs=[
                pl.BlockSpec(
                    (row_total, nao), lambda i, s, k: (0, 0), pipeline_mode=pl.Buffered(1)
                ),
                pl.BlockSpec(
                    (entries, LANE, LANE), lambda i, s, k: (0, 0, 0), pipeline_mode=pl.Buffered(1)
                ),
            ],
            out_specs=pl.BlockSpec((row_total, piece_chunks * LANE), lambda i, s, k: (0, 0)),
        )
        results.append(
            pl.pallas_call(
                kernel,
                grid_spec=grid_spec,
                out_shape=jax.ShapeDtypeStruct((row_total, piece_chunks * LANE), jnp.bfloat16),
                compiler_params=pltpu.CompilerParams(vmem_limit_bytes=60 * 1024 * 1024),
            )(starts, k_sorted, rows_all, padded)
        )
    return results

def per_device(tensor, tensor_pattern, green, green_pattern):
    layer_count = lax.axis_size("layer")
    row_count = lax.axis_size("row")
    if layer_count != row_count:
        return cannon_per_device(tensor, tensor_pattern, green, green_pattern)
    ri_local, mu_local, nu_local = tensor.shape
    tile_rows, tile_cols = green_pattern.shape
    tensor_mask = jnp.repeat(tensor_pattern, BLK, axis=1).astype(jnp.bfloat16)
    masked = tensor * tensor_mask[None, :, :]
    own = masked.reshape(ri_local * mu_local, nu_local)
    layer_index = lax.axis_index("layer")
    col_count = lax.axis_size("col")
    blocks, block_row, block_col = compressed_tile(green, green_pattern)
    parts = tuple(green_to_layers(part, row_count) for part in (blocks, block_row, block_col))
    group = row_count * col_count
    me = lax.axis_index("row") * col_count + lax.axis_index("col")
    received = [parts]
    for shift in range(1, group):
        pairs = [(i, (i + shift) % group) for i in range(group)]
        received.append(tuple(lax.ppermute(part, ("row", "col"), pairs) for part in parts))
    blocks, block_row, block_col = (
        jnp.stack([got[k] for got in received]) for k in range(len(parts))
    )
    band = ((me - jnp.arange(group)) % group)[:, None]
    entry_rows = band * tile_rows + block_row
    entry_rows = entry_rows.reshape(-1)
    entry_cols = block_col.reshape(-1)
    entry_blocks = blocks.reshape(-1, BLK, BLK)
    pieces = []
    for start in range(0, ri_local * mu_local, ROW_CHUNK):
        rows = lax.all_gather(own[start : start + ROW_CHUNK], "layer", axis=1, tiled=True)
        (piece,) = block_sparse_product(
            rows, entry_blocks, entry_rows, entry_cols, tile_cols * BLK, 1
        )
        pieces.append(product_to_owners(piece, row_count))
    product = jnp.concatenate(pieces, axis=0)
    return product.reshape(ri_local, mu_local, tile_cols * BLK)

def solution(mesh):
    in_specs = (
        P("row", "col", "layer"),
        P("col", "layer"),
        P(("layer", "col"), "row"),
        P(("layer", "col"), "row"),
    )
    out_specs = P("layer", "col", "row")
    return jax.shard_map(
        per_device, mesh=mesh, in_specs=in_specs, out_specs=out_specs, check_vma=False
    )
```

```python
import jax
import jax.numpy as jnp
from jax import lax
from jax.experimental import pallas as pl
from jax.experimental.pallas import tpu as pltpu
from jax.sharding import PartitionSpec as P

BLK = 64
CAP = 48
LANE = 128
ROW_CHUNK = 512


def passed_along(value, axis, by):
    length = lax.axis_size(axis)
    return lax.ppermute(value, axis, [(i, (i + by) % length) for i in range(length)])


def cannon_per_device(tensor, tensor_pattern, green, green_pattern):
    row_count = lax.axis_size("row")
    col_count = lax.axis_size("col")
    col_bits = col_count.bit_length() - 1
    row_index = lax.axis_index("row")
    col_index = lax.axis_index("col")
    odd_row = row_index % 2 == 1
    half_row = row_index // 2
    ri_local, mu_local, nu_local = tensor.shape
    width = nu_local // row_count
    tensor_mask = jnp.repeat(tensor_pattern, BLK, axis=1).astype(jnp.bfloat16)
    masked = tensor * tensor_mask[None, :, :]
    left_block = lax.all_to_all(masked, "row", split_axis=2, concat_axis=0, tiled=True)
    for bit_number in range(col_bits):
        arrived = passed_along(left_block, "row", -(2 << bit_number))
        left_block = jnp.where(col_index >> bit_number & 1 == 1, arrived, left_block)
    ri_total = left_block.shape[0]
    all_rows = ri_total * mu_local
    left_block = left_block.reshape(all_rows, width)
    tile_rows, tile_cols = green_pattern.shape
    green_mask = green_pattern.astype(jnp.bfloat16)[:, None, :, None]
    green_tile = (green.reshape(tile_rows, BLK, tile_cols, BLK) * green_mask).reshape(
        tile_rows * BLK, tile_cols * BLK
    )
    green_state = green_tile
    for bit_number in range(col_bits):
        arrived = passed_along(green_state, "col", -(1 << bit_number))
        green_state = jnp.where(half_row >> bit_number & 1 == 1, arrived, green_state)

    def advance(current_state):
        arrived_state = passed_along(current_state, "col", -1)
        return (arrived_state, arrived_state)

    def shift_left(block_now):
        return passed_along(block_now, "row", -1)

    def pair_turn(state_now, shift_last):
        product_sum, block_now, current_state, current = state_now
        green_half = jnp.where(odd_row, current[width:], current[:width])
        product_sum = product_sum + jnp.dot(
            block_now, green_half, preferred_element_type=jnp.float32
        )
        block_now = shift_left(block_now)
        previous = current
        current_state, current = advance(current_state)
        green_half = jnp.where(odd_row, current[:width], previous[width:])
        product_sum = product_sum + jnp.dot(
            block_now, green_half, preferred_element_type=jnp.float32
        )
        if shift_last:
            block_now = shift_left(block_now)
        return (product_sum, block_now, current_state, current)

    start = (
        jnp.zeros((all_rows, tile_cols * BLK), jnp.float32),
        left_block,
        green_state,
        green_state,
    )
    state_now = lax.fori_loop(
        0, col_count - 1, lambda turn_index, state_before: pair_turn(state_before, True), start
    )
    state_now = pair_turn(state_now, False)
    layer_terms = state_now[0].reshape(ri_total, mu_local, tile_cols * BLK)
    return lax.psum_scatter(layer_terms, "layer", scatter_dimension=0, tiled=True).astype(
        jnp.bfloat16
    )


def spread(size):
    return [2, 0, 3, 1] if size == 4 else list(range(size))


def green_to_layers(value, size):
    inverse = {quarter: layer for layer, quarter in enumerate(spread(size))}
    return lax.ppermute(
        value,
        ("layer", "row"),
        [(a * size + b, inverse[b] * size + a) for a in range(size) for b in range(size)],
    )


def product_to_owners(value, size):
    quarter = spread(size)
    return lax.ppermute(
        value,
        ("layer", "row"),
        [(a * size + b, b * size + quarter[a]) for a in range(size) for b in range(size)],
    )


def gathered_windows(green, window_rows, window_cols):
    count = window_rows.shape[0]

    def kernel(rows_ref, cols_ref, green_ref, out_ref):
        out_ref[0] = green_ref[...]

    grid_spec = pltpu.PrefetchScalarGridSpec(
        num_scalar_prefetch=2,
        grid=(count,),
        in_specs=[pl.BlockSpec((BLK, LANE), lambda e, r, c: (r[e], c[e]))],
        out_specs=pl.BlockSpec((1, BLK, LANE), lambda e, r, c: (e, 0, 0)),
    )
    return pl.pallas_call(
        kernel,
        grid_spec=grid_spec,
        out_shape=jax.ShapeDtypeStruct((count, BLK, LANE), green.dtype),
    )(window_rows.astype(jnp.int32), window_cols.astype(jnp.int32), green)


def compressed_tile(green, green_pattern):
    tile_rows, tile_cols = green_pattern.shape
    cap = min(CAP, tile_rows * tile_cols)
    flat = green_pattern.reshape(-1)
    (spots,) = jnp.nonzero(flat != 0, size=cap, fill_value=0)
    valid = jnp.arange(cap) < jnp.sum(flat != 0)
    block_row = spots // tile_cols
    block_col = spots % tile_cols
    windows = gathered_windows(green, block_row, block_col // 2)
    left = (block_col % 2 == 0)[:, None, None]
    blocks = jnp.where(left, windows[:, :, :BLK], windows[:, :, BLK:])
    scale = jnp.where(valid, flat[spots], 0).astype(jnp.bfloat16)
    blocks = blocks * scale[:, None, None]
    return blocks, block_row, block_col


def padded_blocks(blocks, block_rows, block_cols):
    empty = jnp.zeros_like(blocks)
    left = (block_cols % 2 == 0)[:, None, None]
    top = (block_rows % 2 == 0)[:, None, None]
    half = jnp.concatenate([jnp.where(left, blocks, empty), jnp.where(left, empty, blocks)], axis=2)
    empty = jnp.zeros_like(half)
    return jnp.concatenate([jnp.where(top, half, empty), jnp.where(top, empty, half)], axis=1)


def block_sparse_product(rows_all, blocks, block_rows, block_cols, width, pieces):
    row_total, nao = rows_all.shape
    entries = blocks.shape[0]
    chunks = width // LANE
    piece_chunks = chunks // pieces
    chunk_of = block_cols // 2
    order = jnp.argsort(chunk_of)
    chunk_sorted = chunk_of[order]
    starts = jnp.searchsorted(chunk_sorted, jnp.arange(chunks + 1), side="left", method="compare_all").astype(jnp.int32)
    k_sorted = (block_rows[order] // 2).astype(jnp.int32)
    padded = padded_blocks(blocks, block_rows, block_cols)[order]
    results = []
    for piece in range(pieces):
        first = piece * piece_chunks

        def kernel(starts_ref, k_ref, t_ref, g_ref, o_ref, first=first):
            def window(entry):
                return t_ref[:, pl.ds(pl.multiple_of(k_ref[entry] * LANE, LANE), LANE)]

            def one(entry, acc):
                return acc + jnp.dot(window(entry), g_ref[entry], preferred_element_type=jnp.float32)

            for chunk in range(piece_chunks):
                begin = starts_ref[first + chunk]
                end = starts_ref[first + chunk + 1]
                pairs = (end - begin) // 2

                def two(pair, acc, begin=begin):
                    entry = begin + 2 * pair
                    lhs = jnp.concatenate([window(entry), window(entry + 1)], axis=1)
                    rhs = jnp.concatenate([g_ref[entry], g_ref[entry + 1]], axis=0)
                    return acc + jnp.dot(lhs, rhs, preferred_element_type=jnp.float32)

                acc = lax.fori_loop(0, pairs, two, jnp.zeros((row_total, LANE), jnp.float32))
                acc = lax.fori_loop(begin + 2 * pairs, end, one, acc)
                o_ref[:, chunk * LANE : (chunk + 1) * LANE] = acc.astype(o_ref.dtype)

        grid_spec = pltpu.PrefetchScalarGridSpec(
            num_scalar_prefetch=2,
            grid=(1,),
            in_specs=[
                pl.BlockSpec(
                    (row_total, nao), lambda i, s, k: (0, 0), pipeline_mode=pl.Buffered(1)
                ),
                pl.BlockSpec(
                    (entries, LANE, LANE), lambda i, s, k: (0, 0, 0), pipeline_mode=pl.Buffered(1)
                ),
            ],
            out_specs=pl.BlockSpec((row_total, piece_chunks * LANE), lambda i, s, k: (0, 0)),
        )
        results.append(
            pl.pallas_call(
                kernel,
                grid_spec=grid_spec,
                out_shape=jax.ShapeDtypeStruct((row_total, piece_chunks * LANE), jnp.bfloat16),
                compiler_params=pltpu.CompilerParams(vmem_limit_bytes=60 * 1024 * 1024),
            )(starts, k_sorted, rows_all, padded)
        )
    return results

def per_device(tensor, tensor_pattern, green, green_pattern):
    layer_count = lax.axis_size("layer")
    row_count = lax.axis_size("row")
    if layer_count != row_count:
        return cannon_per_device(tensor, tensor_pattern, green, green_pattern)
    ri_local, mu_local, nu_local = tensor.shape
    tile_rows, tile_cols = green_pattern.shape
    tensor_mask = jnp.repeat(tensor_pattern, BLK, axis=1).astype(jnp.bfloat16)
    masked = tensor * tensor_mask[None, :, :]
    own = masked.reshape(ri_local * mu_local, nu_local)
    layer_index = lax.axis_index("layer")
    col_count = lax.axis_size("col")
    blocks, block_row, block_col = compressed_tile(green, green_pattern)
    parts = tuple(green_to_layers(part, row_count) for part in (blocks, block_row, block_col))
    group = row_count * col_count
    me = lax.axis_index("row") * col_count + lax.axis_index("col")
    received = [parts]
    for shift in range(1, group):
        pairs = [(i, (i + shift) % group) for i in range(group)]
        received.append(tuple(lax.ppermute(part, ("row", "col"), pairs) for part in parts))
    blocks, block_row, block_col = (
        jnp.stack([got[k] for got in received]) for k in range(len(parts))
    )
    band = ((me - jnp.arange(group)) % group)[:, None]
    entry_rows = band * tile_rows + block_row
    entry_rows = entry_rows.reshape(-1)
    entry_cols = block_col.reshape(-1)
    entry_blocks = blocks.reshape(-1, BLK, BLK)
    if layer_count != 4:
        pieces = []
        for start in range(0, ri_local * mu_local, ROW_CHUNK):
            rows = lax.all_gather(own[start : start + ROW_CHUNK], "layer", axis=1, tiled=True)
            (piece,) = block_sparse_product(
                rows, entry_blocks, entry_rows, entry_cols, tile_cols * BLK, 1
            )
            pieces.append(product_to_owners(piece, row_count))
        product = jnp.concatenate(pieces, axis=0)
        return product.reshape(ri_local, mu_local, tile_cols * BLK)
    half = ri_local * mu_local // 2
    halves = own.reshape(2, half, nu_local)
    sent = jnp.stack([halves[0], halves[0], halves[1], halves[1]])
    arrived = lax.all_to_all(sent, "layer", 0, 0)
    rows = arrived.transpose(1, 0, 2).reshape(half, layer_count * nu_local)
    across = [(i, i ^ 2) for i in range(4)]
    other_blocks, other_rows, other_cols = (
        lax.ppermute(part, "layer", across) for part in (entry_blocks, entry_rows, entry_cols)
    )
    (mine,) = block_sparse_product(rows, entry_blocks, entry_rows, entry_cols, tile_cols * BLK, 1)
    mine = product_to_owners(mine, row_count)
    (theirs,) = block_sparse_product(rows, other_blocks, other_rows, other_cols, tile_cols * BLK, 1)
    quarter = spread(row_count)
    theirs = lax.ppermute(
        theirs,
        ("layer", "row"),
        [(a * 4 + b, b * 4 + quarter[a ^ 2]) for a in range(4) for b in range(4)],
    )
    inverse = [quarter.index(r) // 2 for r in range(4)]
    first_half = jnp.array(inverse, jnp.int32)[lax.axis_index("row")]
    product = jnp.where(
        first_half == 0,
        jnp.concatenate([mine, theirs], axis=0),
        jnp.concatenate([theirs, mine], axis=0),
    )
    return product.reshape(ri_local, mu_local, tile_cols * BLK)


def solution(mesh):
    in_specs = (
        P("row", "col", "layer"),
        P("col", "layer"),
        P(("layer", "col"), "row"),
        P(("layer", "col"), "row"),
    )
    out_specs = P("layer", "col", "row")
    return jax.shard_map(
        per_device, mesh=mesh, in_specs=in_specs, out_specs=out_specs, check_vma=False
    )
```

```python
import jax
import jax.numpy as jnp
from jax import lax
from jax.experimental import pallas as pl
from jax.experimental.pallas import tpu as pltpu
from jax.sharding import PartitionSpec as P

BLK = 64
CAP = 48
LANE = 128
ROW_CHUNK = 512


def passed_along(value, axis, by):
    length = lax.axis_size(axis)
    return lax.ppermute(value, axis, [(i, (i + by) % length) for i in range(length)])


def cannon_per_device(tensor, tensor_pattern, green, green_pattern):
    row_count = lax.axis_size("row")
    col_count = lax.axis_size("col")
    col_bits = col_count.bit_length() - 1
    row_index = lax.axis_index("row")
    col_index = lax.axis_index("col")
    odd_row = row_index % 2 == 1
    half_row = row_index // 2
    ri_local, mu_local, nu_local = tensor.shape
    width = nu_local // row_count
    tensor_mask = jnp.repeat(tensor_pattern, BLK, axis=1).astype(jnp.bfloat16)
    masked = tensor * tensor_mask[None, :, :]
    left_block = lax.all_to_all(masked, "row", split_axis=2, concat_axis=0, tiled=True)
    for bit_number in range(col_bits):
        arrived = passed_along(left_block, "row", -(2 << bit_number))
        left_block = jnp.where(col_index >> bit_number & 1 == 1, arrived, left_block)
    ri_total = left_block.shape[0]
    all_rows = ri_total * mu_local
    left_block = left_block.reshape(all_rows, width)
    tile_rows, tile_cols = green_pattern.shape
    green_mask = green_pattern.astype(jnp.bfloat16)[:, None, :, None]
    green_tile = (green.reshape(tile_rows, BLK, tile_cols, BLK) * green_mask).reshape(
        tile_rows * BLK, tile_cols * BLK
    )
    green_state = green_tile
    for bit_number in range(col_bits):
        arrived = passed_along(green_state, "col", -(1 << bit_number))
        green_state = jnp.where(half_row >> bit_number & 1 == 1, arrived, green_state)

    def advance(current_state):
        arrived_state = passed_along(current_state, "col", -1)
        return (arrived_state, arrived_state)

    def shift_left(block_now):
        return passed_along(block_now, "row", -1)

    def pair_turn(state_now, shift_last):
        product_sum, block_now, current_state, current = state_now
        green_half = jnp.where(odd_row, current[width:], current[:width])
        product_sum = product_sum + jnp.dot(
            block_now, green_half, preferred_element_type=jnp.float32
        )
        block_now = shift_left(block_now)
        previous = current
        current_state, current = advance(current_state)
        green_half = jnp.where(odd_row, current[:width], previous[width:])
        product_sum = product_sum + jnp.dot(
            block_now, green_half, preferred_element_type=jnp.float32
        )
        if shift_last:
            block_now = shift_left(block_now)
        return (product_sum, block_now, current_state, current)

    start = (
        jnp.zeros((all_rows, tile_cols * BLK), jnp.float32),
        left_block,
        green_state,
        green_state,
    )
    state_now = lax.fori_loop(
        0, col_count - 1, lambda turn_index, state_before: pair_turn(state_before, True), start
    )
    state_now = pair_turn(state_now, False)
    layer_terms = state_now[0].reshape(ri_total, mu_local, tile_cols * BLK)
    return lax.psum_scatter(layer_terms, "layer", scatter_dimension=0, tiled=True).astype(
        jnp.bfloat16
    )


def spread(size):
    return [2, 0, 3, 1] if size == 4 else list(range(size))


def green_to_layers(value, size):
    inverse = {quarter: layer for layer, quarter in enumerate(spread(size))}
    return lax.ppermute(
        value,
        ("layer", "row"),
        [(a * size + b, inverse[b] * size + a) for a in range(size) for b in range(size)],
    )


def product_to_owners(value, size):
    quarter = spread(size)
    return lax.ppermute(
        value,
        ("layer", "row"),
        [(a * size + b, b * size + quarter[a]) for a in range(size) for b in range(size)],
    )


def gathered_windows(green, window_rows, window_cols):
    count = window_rows.shape[0]

    def kernel(rows_ref, cols_ref, green_ref, out_ref):
        out_ref[0] = green_ref[...]

    grid_spec = pltpu.PrefetchScalarGridSpec(
        num_scalar_prefetch=2,
        grid=(count,),
        in_specs=[pl.BlockSpec((BLK, LANE), lambda e, r, c: (r[e], c[e]))],
        out_specs=pl.BlockSpec((1, BLK, LANE), lambda e, r, c: (e, 0, 0)),
    )
    return pl.pallas_call(
        kernel,
        grid_spec=grid_spec,
        out_shape=jax.ShapeDtypeStruct((count, BLK, LANE), green.dtype),
    )(window_rows.astype(jnp.int32), window_cols.astype(jnp.int32), green)


def compressed_tile(green, green_pattern):
    tile_rows, tile_cols = green_pattern.shape
    cap = min(CAP, tile_rows * tile_cols)
    flat = green_pattern.reshape(-1)
    (spots,) = jnp.nonzero(flat != 0, size=cap, fill_value=0)
    valid = jnp.arange(cap) < jnp.sum(flat != 0)
    block_row = spots // tile_cols
    block_col = spots % tile_cols
    windows = gathered_windows(green, block_row, block_col // 2)
    left = (block_col % 2 == 0)[:, None, None]
    blocks = jnp.where(left, windows[:, :, :BLK], windows[:, :, BLK:])
    scale = jnp.where(valid, flat[spots], 0).astype(jnp.bfloat16)
    blocks = blocks * scale[:, None, None]
    return blocks, block_row, block_col


def padded_blocks(blocks, block_rows, block_cols):
    empty = jnp.zeros_like(blocks)
    left = (block_cols % 2 == 0)[:, None, None]
    top = (block_rows % 2 == 0)[:, None, None]
    half = jnp.concatenate([jnp.where(left, blocks, empty), jnp.where(left, empty, blocks)], axis=2)
    empty = jnp.zeros_like(half)
    return jnp.concatenate([jnp.where(top, half, empty), jnp.where(top, empty, half)], axis=1)


def block_sparse_product(rows_all, blocks, block_rows, block_cols, width, pieces):
    row_total, nao = rows_all.shape
    entries = blocks.shape[0]
    chunks = width // LANE
    piece_chunks = chunks // pieces
    chunk_of = block_cols // 2
    order = jnp.argsort(chunk_of)
    chunk_sorted = chunk_of[order]
    starts = jnp.searchsorted(chunk_sorted, jnp.arange(chunks + 1), side="left", method="compare_all").astype(jnp.int32)
    k_sorted = (block_rows[order] // 2).astype(jnp.int32)
    padded = padded_blocks(blocks, block_rows, block_cols)[order]
    results = []
    for piece in range(pieces):
        first = piece * piece_chunks

        def kernel(starts_ref, k_ref, t_ref, g_ref, o_ref, first=first):
            def window(entry):
                return t_ref[:, pl.ds(pl.multiple_of(k_ref[entry] * LANE, LANE), LANE)]

            def one(entry, acc):
                return acc + jnp.dot(window(entry), g_ref[entry], preferred_element_type=jnp.float32)

            for chunk in range(piece_chunks):
                begin = starts_ref[first + chunk]
                end = starts_ref[first + chunk + 1]
                pairs = (end - begin) // 2

                def two(pair, acc, begin=begin):
                    entry = begin + 2 * pair
                    lhs = jnp.concatenate([window(entry), window(entry + 1)], axis=1)
                    rhs = jnp.concatenate([g_ref[entry], g_ref[entry + 1]], axis=0)
                    return acc + jnp.dot(lhs, rhs, preferred_element_type=jnp.float32)

                acc = lax.fori_loop(0, pairs, two, jnp.zeros((row_total, LANE), jnp.float32))
                acc = lax.fori_loop(begin + 2 * pairs, end, one, acc)
                o_ref[:, chunk * LANE : (chunk + 1) * LANE] = acc.astype(o_ref.dtype)

        grid_spec = pltpu.PrefetchScalarGridSpec(
            num_scalar_prefetch=2,
            grid=(1,),
            in_specs=[
                pl.BlockSpec(
                    (row_total, nao), lambda i, s, k: (0, 0), pipeline_mode=pl.Buffered(1)
                ),
                pl.BlockSpec(
                    (entries, LANE, LANE), lambda i, s, k: (0, 0, 0), pipeline_mode=pl.Buffered(1)
                ),
            ],
            out_specs=pl.BlockSpec((row_total, piece_chunks * LANE), lambda i, s, k: (0, 0)),
        )
        results.append(
            pl.pallas_call(
                kernel,
                grid_spec=grid_spec,
                out_shape=jax.ShapeDtypeStruct((row_total, piece_chunks * LANE), jnp.bfloat16),
                compiler_params=pltpu.CompilerParams(vmem_limit_bytes=60 * 1024 * 1024),
            )(starts, k_sorted, rows_all, padded)
        )
    return results

def per_device(tensor, tensor_pattern, green, green_pattern):
    layer_count = lax.axis_size("layer")
    row_count = lax.axis_size("row")
    if layer_count != row_count or max(green_pattern.shape) > 256:
        return cannon_per_device(tensor, tensor_pattern, green, green_pattern)
    ri_local, mu_local, nu_local = tensor.shape
    tile_rows, tile_cols = green_pattern.shape
    tensor_mask = jnp.repeat(tensor_pattern, BLK, axis=1).astype(jnp.bfloat16)
    masked = tensor * tensor_mask[None, :, :]
    own = masked.reshape(ri_local * mu_local, nu_local)
    layer_index = lax.axis_index("layer")
    col_count = lax.axis_size("col")
    blocks, block_row, block_col = compressed_tile(green, green_pattern)
    marks = jnp.zeros((blocks.shape[0], 16, BLK), jnp.bfloat16)
    marks = marks.at[:, 0, 0].set(block_row.astype(jnp.bfloat16))
    marks = marks.at[:, 0, 1].set(block_col.astype(jnp.bfloat16))
    packed = green_to_layers(jnp.concatenate([blocks, marks], axis=1), row_count)
    group = row_count * col_count
    me = lax.axis_index("row") * col_count + lax.axis_index("col")
    received = [packed]
    for shift in range(1, group):
        pairs = [(i, (i + shift) % group) for i in range(group)]
        received.append(lax.ppermute(packed, ("row", "col"), pairs))
    packed = jnp.stack(received)
    blocks = packed[:, :, :BLK, :]
    block_row = packed[:, :, BLK, 0].astype(jnp.int32)
    block_col = packed[:, :, BLK, 1].astype(jnp.int32)
    band = ((me - jnp.arange(group)) % group)[:, None]
    entry_rows = band * tile_rows + block_row
    entry_rows = entry_rows.reshape(-1)
    entry_cols = block_col.reshape(-1)
    entry_blocks = blocks.reshape(-1, BLK, BLK)
    pieces = []
    for start in range(0, ri_local * mu_local, ROW_CHUNK):
        rows = lax.all_gather(own[start : start + ROW_CHUNK], "layer", axis=1, tiled=True)
        (piece,) = block_sparse_product(
            rows, entry_blocks, entry_rows, entry_cols, tile_cols * BLK, 1
        )
        pieces.append(product_to_owners(piece, row_count))
    product = jnp.concatenate(pieces, axis=0)
    return product.reshape(ri_local, mu_local, tile_cols * BLK)

def solution(mesh):
    in_specs = (
        P("row", "col", "layer"),
        P("col", "layer"),
        P(("layer", "col"), "row"),
        P(("layer", "col"), "row"),
    )
    out_specs = P("layer", "col", "row")
    return jax.shard_map(
        per_device, mesh=mesh, in_specs=in_specs, out_specs=out_specs, check_vma=False
    )
```

```python
import jax
import jax.numpy as jnp
from jax import lax
from jax.experimental import pallas as pl
from jax.experimental.pallas import tpu as pltpu
from jax.sharding import PartitionSpec as P

BLK = 64
CAP = 48
LANE = 128
ROW_CHUNK = 256


def passed_along(value, axis, by):
    length = lax.axis_size(axis)
    return lax.ppermute(value, axis, [(i, (i + by) % length) for i in range(length)])


def cannon_per_device(tensor, tensor_pattern, green, green_pattern):
    row_count = lax.axis_size("row")
    col_count = lax.axis_size("col")
    col_bits = col_count.bit_length() - 1
    row_index = lax.axis_index("row")
    col_index = lax.axis_index("col")
    odd_row = row_index % 2 == 1
    half_row = row_index // 2
    ri_local, mu_local, nu_local = tensor.shape
    width = nu_local // row_count
    tensor_mask = jnp.repeat(tensor_pattern, BLK, axis=1).astype(jnp.bfloat16)
    masked = tensor * tensor_mask[None, :, :]
    left_block = lax.all_to_all(masked, "row", split_axis=2, concat_axis=0, tiled=True)
    for bit_number in range(col_bits):
        arrived = passed_along(left_block, "row", -(2 << bit_number))
        left_block = jnp.where(col_index >> bit_number & 1 == 1, arrived, left_block)
    ri_total = left_block.shape[0]
    all_rows = ri_total * mu_local
    left_block = left_block.reshape(all_rows, width)
    tile_rows, tile_cols = green_pattern.shape
    green_mask = green_pattern.astype(jnp.bfloat16)[:, None, :, None]
    green_tile = (green.reshape(tile_rows, BLK, tile_cols, BLK) * green_mask).reshape(
        tile_rows * BLK, tile_cols * BLK
    )
    green_state = green_tile
    for bit_number in range(col_bits):
        arrived = passed_along(green_state, "col", -(1 << bit_number))
        green_state = jnp.where(half_row >> bit_number & 1 == 1, arrived, green_state)

    def advance(current_state):
        arrived_state = passed_along(current_state, "col", -1)
        return (arrived_state, arrived_state)

    def shift_left(block_now):
        return passed_along(block_now, "row", -1)

    def pair_turn(state_now, shift_last):
        product_sum, block_now, current_state, current = state_now
        green_half = jnp.where(odd_row, current[width:], current[:width])
        product_sum = product_sum + jnp.dot(
            block_now, green_half, preferred_element_type=jnp.float32
        )
        block_now = shift_left(block_now)
        previous = current
        current_state, current = advance(current_state)
        green_half = jnp.where(odd_row, current[:width], previous[width:])
        product_sum = product_sum + jnp.dot(
            block_now, green_half, preferred_element_type=jnp.float32
        )
        if shift_last:
            block_now = shift_left(block_now)
        return (product_sum, block_now, current_state, current)

    start = (
        jnp.zeros((all_rows, tile_cols * BLK), jnp.float32),
        left_block,
        green_state,
        green_state,
    )
    state_now = lax.fori_loop(
        0, col_count - 1, lambda turn_index, state_before: pair_turn(state_before, True), start
    )
    state_now = pair_turn(state_now, False)
    layer_terms = state_now[0].reshape(ri_total, mu_local, tile_cols * BLK)
    return lax.psum_scatter(layer_terms, "layer", scatter_dimension=0, tiled=True).astype(
        jnp.bfloat16
    )


def spread(size):
    return [2, 0, 3, 1] if size == 4 else list(range(size))


def green_to_layers(value, size):
    inverse = {quarter: layer for layer, quarter in enumerate(spread(size))}
    return lax.ppermute(
        value,
        ("layer", "row"),
        [(a * size + b, inverse[b] * size + a) for a in range(size) for b in range(size)],
    )


def product_to_owners(value, size):
    quarter = spread(size)
    return lax.ppermute(
        value,
        ("layer", "row"),
        [(a * size + b, b * size + quarter[a]) for a in range(size) for b in range(size)],
    )


def gathered_windows(green, window_rows, window_cols):
    count = window_rows.shape[0]

    def kernel(rows_ref, cols_ref, green_ref, out_ref):
        out_ref[0] = green_ref[...]

    grid_spec = pltpu.PrefetchScalarGridSpec(
        num_scalar_prefetch=2,
        grid=(count,),
        in_specs=[pl.BlockSpec((BLK, LANE), lambda e, r, c: (r[e], c[e]))],
        out_specs=pl.BlockSpec((1, BLK, LANE), lambda e, r, c: (e, 0, 0)),
    )
    return pl.pallas_call(
        kernel,
        grid_spec=grid_spec,
        out_shape=jax.ShapeDtypeStruct((count, BLK, LANE), green.dtype),
    )(window_rows.astype(jnp.int32), window_cols.astype(jnp.int32), green)


def compressed_tile(green, green_pattern):
    tile_rows, tile_cols = green_pattern.shape
    cap = min(CAP, tile_rows * tile_cols)
    flat = green_pattern.reshape(-1)
    (spots,) = jnp.nonzero(flat != 0, size=cap, fill_value=0)
    valid = jnp.arange(cap) < jnp.sum(flat != 0)
    block_row = spots // tile_cols
    block_col = spots % tile_cols
    windows = gathered_windows(green, block_row, block_col // 2)
    left = (block_col % 2 == 0)[:, None, None]
    blocks = jnp.where(left, windows[:, :, :BLK], windows[:, :, BLK:])
    scale = jnp.where(valid, flat[spots], 0).astype(jnp.bfloat16)
    blocks = blocks * scale[:, None, None]
    return blocks, block_row, block_col


def padded_blocks(blocks, block_rows, block_cols):
    empty = jnp.zeros_like(blocks)
    left = (block_cols % 2 == 0)[:, None, None]
    top = (block_rows % 2 == 0)[:, None, None]
    half = jnp.concatenate([jnp.where(left, blocks, empty), jnp.where(left, empty, blocks)], axis=2)
    empty = jnp.zeros_like(half)
    return jnp.concatenate([jnp.where(top, half, empty), jnp.where(top, empty, half)], axis=1)


def block_sparse_product(rows_all, blocks, block_rows, block_cols, width, pieces):
    row_total, nao = rows_all.shape
    entries = blocks.shape[0]
    chunks = width // LANE
    piece_chunks = chunks // pieces
    chunk_of = block_cols // 2
    order = jnp.argsort(chunk_of)
    chunk_sorted = chunk_of[order]
    starts = jnp.searchsorted(chunk_sorted, jnp.arange(chunks + 1), side="left", method="compare_all").astype(jnp.int32)
    k_sorted = (block_rows[order] // 2).astype(jnp.int32)
    padded = padded_blocks(blocks, block_rows, block_cols)[order]
    results = []
    for piece in range(pieces):
        first = piece * piece_chunks

        def kernel(starts_ref, k_ref, t_ref, g_ref, o_ref, first=first):
            def window(entry):
                return t_ref[:, pl.ds(pl.multiple_of(k_ref[entry] * LANE, LANE), LANE)]

            def one(entry, acc):
                return acc + jnp.dot(window(entry), g_ref[entry], preferred_element_type=jnp.float32)

            for chunk in range(piece_chunks):
                begin = starts_ref[first + chunk]
                end = starts_ref[first + chunk + 1]
                pairs = (end - begin) // 2

                def two(pair, acc, begin=begin):
                    entry = begin + 2 * pair
                    lhs = jnp.concatenate([window(entry), window(entry + 1)], axis=1)
                    rhs = jnp.concatenate([g_ref[entry], g_ref[entry + 1]], axis=0)
                    return acc + jnp.dot(lhs, rhs, preferred_element_type=jnp.float32)

                acc = lax.fori_loop(0, pairs, two, jnp.zeros((row_total, LANE), jnp.float32))
                acc = lax.fori_loop(begin + 2 * pairs, end, one, acc)
                o_ref[:, chunk * LANE : (chunk + 1) * LANE] = acc.astype(o_ref.dtype)

        grid_spec = pltpu.PrefetchScalarGridSpec(
            num_scalar_prefetch=2,
            grid=(1,),
            in_specs=[
                pl.BlockSpec(
                    (row_total, nao), lambda i, s, k: (0, 0), pipeline_mode=pl.Buffered(1)
                ),
                pl.BlockSpec(
                    (entries, LANE, LANE), lambda i, s, k: (0, 0, 0), pipeline_mode=pl.Buffered(1)
                ),
            ],
            out_specs=pl.BlockSpec((row_total, piece_chunks * LANE), lambda i, s, k: (0, 0)),
        )
        results.append(
            pl.pallas_call(
                kernel,
                grid_spec=grid_spec,
                out_shape=jax.ShapeDtypeStruct((row_total, piece_chunks * LANE), jnp.bfloat16),
                compiler_params=pltpu.CompilerParams(vmem_limit_bytes=60 * 1024 * 1024),
            )(starts, k_sorted, rows_all, padded)
        )
    return results

def per_device(tensor, tensor_pattern, green, green_pattern):
    layer_count = lax.axis_size("layer")
    row_count = lax.axis_size("row")
    if layer_count != row_count:
        return cannon_per_device(tensor, tensor_pattern, green, green_pattern)
    ri_local, mu_local, nu_local = tensor.shape
    tile_rows, tile_cols = green_pattern.shape
    tensor_mask = jnp.repeat(tensor_pattern, BLK, axis=1).astype(jnp.bfloat16)
    masked = tensor * tensor_mask[None, :, :]
    own = masked.reshape(ri_local * mu_local, nu_local)
    layer_index = lax.axis_index("layer")
    col_count = lax.axis_size("col")
    blocks, block_row, block_col = compressed_tile(green, green_pattern)
    parts = tuple(green_to_layers(part, row_count) for part in (blocks, block_row, block_col))
    group = row_count * col_count
    me = lax.axis_index("row") * col_count + lax.axis_index("col")
    received = [parts]
    for shift in range(1, group):
        pairs = [(i, (i + shift) % group) for i in range(group)]
        received.append(tuple(lax.ppermute(part, ("row", "col"), pairs) for part in parts))
    blocks, block_row, block_col = (
        jnp.stack([got[k] for got in received]) for k in range(len(parts))
    )
    band = ((me - jnp.arange(group)) % group)[:, None]
    entry_rows = band * tile_rows + block_row
    entry_rows = entry_rows.reshape(-1)
    entry_cols = block_col.reshape(-1)
    entry_blocks = blocks.reshape(-1, BLK, BLK)
    pieces = []
    for start in range(0, ri_local * mu_local, ROW_CHUNK):
        rows = lax.all_gather(own[start : start + ROW_CHUNK], "layer", axis=1, tiled=True)
        (piece,) = block_sparse_product(
            rows, entry_blocks, entry_rows, entry_cols, tile_cols * BLK, 1
        )
        pieces.append(product_to_owners(piece, row_count))
    product = jnp.concatenate(pieces, axis=0)
    return product.reshape(ri_local, mu_local, tile_cols * BLK)

def solution(mesh):
    in_specs = (
        P("row", "col", "layer"),
        P("col", "layer"),
        P(("layer", "col"), "row"),
        P(("layer", "col"), "row"),
    )
    out_specs = P("layer", "col", "row")
    return jax.shard_map(
        per_device, mesh=mesh, in_specs=in_specs, out_specs=out_specs, check_vma=False
    )
```

```python
import jax
import jax.numpy as jnp
from jax import lax
from jax.experimental import pallas as pl
from jax.experimental.pallas import tpu as pltpu
from jax.sharding import PartitionSpec as P

BLK = 64
CAP = 48
LANE = 128
ROW_CHUNK = 256


def passed_along(value, axis, by):
    length = lax.axis_size(axis)
    return lax.ppermute(value, axis, [(i, (i + by) % length) for i in range(length)])


def cannon_per_device(tensor, tensor_pattern, green, green_pattern):
    row_count = lax.axis_size("row")
    col_count = lax.axis_size("col")
    col_bits = col_count.bit_length() - 1
    row_index = lax.axis_index("row")
    col_index = lax.axis_index("col")
    odd_row = row_index % 2 == 1
    half_row = row_index // 2
    ri_local, mu_local, nu_local = tensor.shape
    width = nu_local // row_count
    tensor_mask = jnp.repeat(tensor_pattern, BLK, axis=1).astype(jnp.bfloat16)
    masked = tensor * tensor_mask[None, :, :]
    left_block = lax.all_to_all(masked, "row", split_axis=2, concat_axis=0, tiled=True)
    for bit_number in range(col_bits):
        arrived = passed_along(left_block, "row", -(2 << bit_number))
        left_block = jnp.where(col_index >> bit_number & 1 == 1, arrived, left_block)
    ri_total = left_block.shape[0]
    all_rows = ri_total * mu_local
    left_block = left_block.reshape(all_rows, width)
    tile_rows, tile_cols = green_pattern.shape
    green_mask = green_pattern.astype(jnp.bfloat16)[:, None, :, None]
    green_tile = (green.reshape(tile_rows, BLK, tile_cols, BLK) * green_mask).reshape(
        tile_rows * BLK, tile_cols * BLK
    )
    green_state = green_tile
    for bit_number in range(col_bits):
        arrived = passed_along(green_state, "col", -(1 << bit_number))
        green_state = jnp.where(half_row >> bit_number & 1 == 1, arrived, green_state)

    def advance(current_state):
        arrived_state = passed_along(current_state, "col", -1)
        return (arrived_state, arrived_state)

    def shift_left(block_now):
        return passed_along(block_now, "row", -1)

    def pair_turn(state_now, shift_last):
        product_sum, block_now, current_state, current = state_now
        green_half = jnp.where(odd_row, current[width:], current[:width])
        product_sum = product_sum + jnp.dot(
            block_now, green_half, preferred_element_type=jnp.float32
        )
        block_now = shift_left(block_now)
        previous = current
        current_state, current = advance(current_state)
        green_half = jnp.where(odd_row, current[:width], previous[width:])
        product_sum = product_sum + jnp.dot(
            block_now, green_half, preferred_element_type=jnp.float32
        )
        if shift_last:
            block_now = shift_left(block_now)
        return (product_sum, block_now, current_state, current)

    start = (
        jnp.zeros((all_rows, tile_cols * BLK), jnp.float32),
        left_block,
        green_state,
        green_state,
    )
    state_now = lax.fori_loop(
        0, col_count - 1, lambda turn_index, state_before: pair_turn(state_before, True), start
    )
    state_now = pair_turn(state_now, False)
    layer_terms = state_now[0].reshape(ri_total, mu_local, tile_cols * BLK)
    return lax.psum_scatter(layer_terms, "layer", scatter_dimension=0, tiled=True).astype(
        jnp.bfloat16
    )


def spread(size):
    return [2, 0, 3, 1] if size == 4 else list(range(size))


def green_to_layers(value, size):
    inverse = {quarter: layer for layer, quarter in enumerate(spread(size))}
    return lax.ppermute(
        value,
        ("layer", "row"),
        [(a * size + b, inverse[b] * size + a) for a in range(size) for b in range(size)],
    )


def product_to_owners(value, size):
    quarter = spread(size)
    return lax.ppermute(
        value,
        ("layer", "row"),
        [(a * size + b, b * size + quarter[a]) for a in range(size) for b in range(size)],
    )


def gathered_windows(green, window_rows, window_cols):
    count = window_rows.shape[0]

    def kernel(rows_ref, cols_ref, green_ref, out_ref):
        out_ref[0] = green_ref[...]

    grid_spec = pltpu.PrefetchScalarGridSpec(
        num_scalar_prefetch=2,
        grid=(count,),
        in_specs=[pl.BlockSpec((BLK, LANE), lambda e, r, c: (r[e], c[e]))],
        out_specs=pl.BlockSpec((1, BLK, LANE), lambda e, r, c: (e, 0, 0)),
    )
    return pl.pallas_call(
        kernel,
        grid_spec=grid_spec,
        out_shape=jax.ShapeDtypeStruct((count, BLK, LANE), green.dtype),
    )(window_rows.astype(jnp.int32), window_cols.astype(jnp.int32), green)


def compressed_tile(green, green_pattern):
    tile_rows, tile_cols = green_pattern.shape
    cap = min(CAP, tile_rows * tile_cols)
    flat = green_pattern.reshape(-1)
    (spots,) = jnp.nonzero(flat != 0, size=cap, fill_value=0)
    valid = jnp.arange(cap) < jnp.sum(flat != 0)
    block_row = spots // tile_cols
    block_col = spots % tile_cols
    windows = gathered_windows(green, block_row, block_col // 2)
    left = (block_col % 2 == 0)[:, None, None]
    blocks = jnp.where(left, windows[:, :, :BLK], windows[:, :, BLK:])
    scale = jnp.where(valid, flat[spots], 0).astype(jnp.bfloat16)
    blocks = blocks * scale[:, None, None]
    return blocks, block_row, block_col


def padded_blocks(blocks, block_rows, block_cols):
    empty = jnp.zeros_like(blocks)
    left = (block_cols % 2 == 0)[:, None, None]
    top = (block_rows % 2 == 0)[:, None, None]
    half = jnp.concatenate([jnp.where(left, blocks, empty), jnp.where(left, empty, blocks)], axis=2)
    empty = jnp.zeros_like(half)
    return jnp.concatenate([jnp.where(top, half, empty), jnp.where(top, empty, half)], axis=1)


def block_sparse_product(rows_all, blocks, block_rows, block_cols, width, pieces):
    row_total, nao = rows_all.shape
    entries = blocks.shape[0]
    chunks = width // LANE
    piece_chunks = chunks // pieces
    chunk_of = block_cols // 2
    order = jnp.argsort(chunk_of)
    chunk_sorted = chunk_of[order]
    starts = jnp.searchsorted(chunk_sorted, jnp.arange(chunks + 1), side="left", method="compare_all").astype(jnp.int32)
    k_sorted = (block_rows[order] // 2).astype(jnp.int32)
    padded = padded_blocks(blocks, block_rows, block_cols)[order]
    results = []
    for piece in range(pieces):
        first = piece * piece_chunks

        def kernel(starts_ref, k_ref, t_ref, g_ref, o_ref, first=first):
            def window(entry):
                return t_ref[:, pl.ds(pl.multiple_of(k_ref[entry] * LANE, LANE), LANE)]

            def one(entry, acc):
                return acc + jnp.dot(window(entry), g_ref[entry], preferred_element_type=jnp.float32)

            for chunk in range(piece_chunks):
                begin = starts_ref[first + chunk]
                end = starts_ref[first + chunk + 1]
                pairs = (end - begin) // 2

                def two(pair, acc, begin=begin):
                    entry = begin + 2 * pair
                    lhs = jnp.concatenate([window(entry), window(entry + 1)], axis=1)
                    rhs = jnp.concatenate([g_ref[entry], g_ref[entry + 1]], axis=0)
                    return acc + jnp.dot(lhs, rhs, preferred_element_type=jnp.float32)

                acc = lax.fori_loop(0, pairs, two, jnp.zeros((row_total, LANE), jnp.float32))
                acc = lax.fori_loop(begin + 2 * pairs, end, one, acc)
                o_ref[:, chunk * LANE : (chunk + 1) * LANE] = acc.astype(o_ref.dtype)

        grid_spec = pltpu.PrefetchScalarGridSpec(
            num_scalar_prefetch=2,
            grid=(1,),
            in_specs=[
                pl.BlockSpec(
                    (row_total, nao), lambda i, s, k: (0, 0), pipeline_mode=pl.Buffered(1)
                ),
                pl.BlockSpec(
                    (entries, LANE, LANE), lambda i, s, k: (0, 0, 0), pipeline_mode=pl.Buffered(1)
                ),
            ],
            out_specs=pl.BlockSpec((row_total, piece_chunks * LANE), lambda i, s, k: (0, 0)),
        )
        results.append(
            pl.pallas_call(
                kernel,
                grid_spec=grid_spec,
                out_shape=jax.ShapeDtypeStruct((row_total, piece_chunks * LANE), jnp.bfloat16),
                compiler_params=pltpu.CompilerParams(vmem_limit_bytes=60 * 1024 * 1024),
            )(starts, k_sorted, rows_all, padded)
        )
    return results

def per_device(tensor, tensor_pattern, green, green_pattern):
    layer_count = lax.axis_size("layer")
    row_count = lax.axis_size("row")
    if layer_count != row_count:
        return cannon_per_device(tensor, tensor_pattern, green, green_pattern)
    ri_local, mu_local, nu_local = tensor.shape
    tile_rows, tile_cols = green_pattern.shape
    tensor_mask = jnp.repeat(tensor_pattern, BLK, axis=1).astype(jnp.bfloat16)
    masked = tensor * tensor_mask[None, :, :]
    own = masked.reshape(ri_local * mu_local, nu_local)
    layer_index = lax.axis_index("layer")
    col_count = lax.axis_size("col")
    blocks, block_row, block_col = compressed_tile(green, green_pattern)
    parts = tuple(green_to_layers(part, row_count) for part in (blocks, block_row, block_col))
    group = row_count * col_count
    me = lax.axis_index("row") * col_count + lax.axis_index("col")
    received = [parts]
    for shift in range(1, group):
        pairs = [(i, (i + shift) % group) for i in range(group)]
        received.append(tuple(lax.ppermute(part, ("row", "col"), pairs) for part in parts))
    blocks, block_row, block_col = (
        jnp.stack([got[k] for got in received]) for k in range(len(parts))
    )
    own, blocks = lax.optimization_barrier((own, blocks))
    band = ((me - jnp.arange(group)) % group)[:, None]
    entry_rows = band * tile_rows + block_row
    entry_rows = entry_rows.reshape(-1)
    entry_cols = block_col.reshape(-1)
    entry_blocks = blocks.reshape(-1, BLK, BLK)
    pieces = []
    for start in range(0, ri_local * mu_local, ROW_CHUNK):
        rows = lax.all_gather(own[start : start + ROW_CHUNK], "layer", axis=1, tiled=True)
        (piece,) = block_sparse_product(
            rows, entry_blocks, entry_rows, entry_cols, tile_cols * BLK, 1
        )
        pieces.append(product_to_owners(piece, row_count))
    product = jnp.concatenate(pieces, axis=0)
    return product.reshape(ri_local, mu_local, tile_cols * BLK)

def solution(mesh):
    in_specs = (
        P("row", "col", "layer"),
        P("col", "layer"),
        P(("layer", "col"), "row"),
        P(("layer", "col"), "row"),
    )
    out_specs = P("layer", "col", "row")
    return jax.shard_map(
        per_device, mesh=mesh, in_specs=in_specs, out_specs=out_specs, check_vma=False
    )
```

```python
import jax
import jax.numpy as jnp
from jax import lax
from jax.experimental import pallas as pl
from jax.experimental.pallas import tpu as pltpu
from jax.sharding import PartitionSpec as P

BLK = 64
CAP = 48
LANE = 128
ROW_CHUNK = 256


def passed_along(value, axis, by):
    length = lax.axis_size(axis)
    return lax.ppermute(value, axis, [(i, (i + by) % length) for i in range(length)])


def cannon_per_device(tensor, tensor_pattern, green, green_pattern):
    row_count = lax.axis_size("row")
    col_count = lax.axis_size("col")
    col_bits = col_count.bit_length() - 1
    row_index = lax.axis_index("row")
    col_index = lax.axis_index("col")
    odd_row = row_index % 2 == 1
    half_row = row_index // 2
    ri_local, mu_local, nu_local = tensor.shape
    width = nu_local // row_count
    tensor_mask = jnp.repeat(tensor_pattern, BLK, axis=1).astype(jnp.bfloat16)
    masked = tensor * tensor_mask[None, :, :]
    left_block = lax.all_to_all(masked, "row", split_axis=2, concat_axis=0, tiled=True)
    for bit_number in range(col_bits):
        arrived = passed_along(left_block, "row", -(2 << bit_number))
        left_block = jnp.where(col_index >> bit_number & 1 == 1, arrived, left_block)
    ri_total = left_block.shape[0]
    all_rows = ri_total * mu_local
    left_block = left_block.reshape(all_rows, width)
    tile_rows, tile_cols = green_pattern.shape
    green_mask = green_pattern.astype(jnp.bfloat16)[:, None, :, None]
    green_tile = (green.reshape(tile_rows, BLK, tile_cols, BLK) * green_mask).reshape(
        tile_rows * BLK, tile_cols * BLK
    )
    green_state = green_tile
    for bit_number in range(col_bits):
        arrived = passed_along(green_state, "col", -(1 << bit_number))
        green_state = jnp.where(half_row >> bit_number & 1 == 1, arrived, green_state)

    def advance(current_state):
        arrived_state = passed_along(current_state, "col", -1)
        return (arrived_state, arrived_state)

    def shift_left(block_now):
        return passed_along(block_now, "row", -1)

    def pair_turn(state_now, shift_last):
        product_sum, block_now, current_state, current = state_now
        green_half = jnp.where(odd_row, current[width:], current[:width])
        product_sum = product_sum + jnp.dot(
            block_now, green_half, preferred_element_type=jnp.float32
        )
        block_now = shift_left(block_now)
        previous = current
        current_state, current = advance(current_state)
        green_half = jnp.where(odd_row, current[:width], previous[width:])
        product_sum = product_sum + jnp.dot(
            block_now, green_half, preferred_element_type=jnp.float32
        )
        if shift_last:
            block_now = shift_left(block_now)
        return (product_sum, block_now, current_state, current)

    start = (
        jnp.zeros((all_rows, tile_cols * BLK), jnp.float32),
        left_block,
        green_state,
        green_state,
    )
    state_now = lax.fori_loop(
        0, col_count - 1, lambda turn_index, state_before: pair_turn(state_before, True), start
    )
    state_now = pair_turn(state_now, False)
    layer_terms = state_now[0].reshape(ri_total, mu_local, tile_cols * BLK)
    return lax.psum_scatter(layer_terms, "layer", scatter_dimension=0, tiled=True).astype(
        jnp.bfloat16
    )


def spread(size):
    return [2, 0, 3, 1] if size == 4 else list(range(size))


def green_to_layers(value, size):
    inverse = {quarter: layer for layer, quarter in enumerate(spread(size))}
    return lax.ppermute(
        value,
        ("layer", "row"),
        [(a * size + b, inverse[b] * size + a) for a in range(size) for b in range(size)],
    )


def product_to_owners(value, size):
    quarter = spread(size)
    return lax.ppermute(
        value,
        ("layer", "row"),
        [(a * size + b, b * size + quarter[a]) for a in range(size) for b in range(size)],
    )


def gathered_windows(green, window_rows, window_cols):
    count = window_rows.shape[0]

    def kernel(rows_ref, cols_ref, green_ref, out_ref):
        out_ref[0] = green_ref[...]

    grid_spec = pltpu.PrefetchScalarGridSpec(
        num_scalar_prefetch=2,
        grid=(count,),
        in_specs=[pl.BlockSpec((BLK, LANE), lambda e, r, c: (r[e], c[e]))],
        out_specs=pl.BlockSpec((1, BLK, LANE), lambda e, r, c: (e, 0, 0)),
    )
    return pl.pallas_call(
        kernel,
        grid_spec=grid_spec,
        out_shape=jax.ShapeDtypeStruct((count, BLK, LANE), green.dtype),
    )(window_rows.astype(jnp.int32), window_cols.astype(jnp.int32), green)


def compressed_tile(green, green_pattern):
    tile_rows, tile_cols = green_pattern.shape
    cap = min(CAP, tile_rows * tile_cols)
    flat = green_pattern.reshape(-1)
    (spots,) = jnp.nonzero(flat != 0, size=cap, fill_value=0)
    valid = jnp.arange(cap) < jnp.sum(flat != 0)
    block_row = spots // tile_cols
    block_col = spots % tile_cols
    windows = gathered_windows(green, block_row, block_col // 2)
    left = (block_col % 2 == 0)[:, None, None]
    blocks = jnp.where(left, windows[:, :, :BLK], windows[:, :, BLK:])
    scale = jnp.where(valid, flat[spots], 0).astype(jnp.bfloat16)
    blocks = blocks * scale[:, None, None]
    return blocks, block_row, block_col


def padded_blocks(blocks, block_rows, block_cols):
    empty = jnp.zeros_like(blocks)
    left = (block_cols % 2 == 0)[:, None, None]
    top = (block_rows % 2 == 0)[:, None, None]
    half = jnp.concatenate([jnp.where(left, blocks, empty), jnp.where(left, empty, blocks)], axis=2)
    empty = jnp.zeros_like(half)
    return jnp.concatenate([jnp.where(top, half, empty), jnp.where(top, empty, half)], axis=1)


def block_sparse_product(rows_all, blocks, block_rows, block_cols, width, pieces):
    row_total, nao = rows_all.shape
    entries = blocks.shape[0]
    chunks = width // LANE
    piece_chunks = chunks // pieces
    chunk_of = block_cols // 2
    order = jnp.argsort(chunk_of)
    chunk_sorted = chunk_of[order]
    starts = jnp.searchsorted(chunk_sorted, jnp.arange(chunks + 1), side="left", method="compare_all").astype(jnp.int32)
    k_sorted = (block_rows[order] // 2).astype(jnp.int32)
    padded = padded_blocks(blocks, block_rows, block_cols)[order]
    results = []
    for piece in range(pieces):
        first = piece * piece_chunks

        def kernel(starts_ref, k_ref, t_ref, g_ref, o_ref, first=first):
            def window(entry):
                return t_ref[:, pl.ds(pl.multiple_of(k_ref[entry] * LANE, LANE), LANE)]

            def one(entry, acc):
                return acc + jnp.dot(window(entry), g_ref[entry], preferred_element_type=jnp.float32)

            def grouped(width, base):
                def step(index, acc):
                    entry = base + width * index
                    lhs = jnp.concatenate([window(entry + j) for j in range(width)], axis=1)
                    rhs = jnp.concatenate([g_ref[entry + j] for j in range(width)], axis=0)
                    return acc + jnp.dot(lhs, rhs, preferred_element_type=jnp.float32)

                return step

            for chunk in range(piece_chunks):
                begin = starts_ref[first + chunk]
                end = starts_ref[first + chunk + 1]
                acc = jnp.zeros((row_total, LANE), jnp.float32)
                for width in (4, 2):
                    count = (end - begin) // width
                    acc = lax.fori_loop(0, count, grouped(width, begin), acc)
                    begin = begin + width * count
                acc = lax.fori_loop(begin, end, one, acc)
                o_ref[:, chunk * LANE : (chunk + 1) * LANE] = acc.astype(o_ref.dtype)

        grid_spec = pltpu.PrefetchScalarGridSpec(
            num_scalar_prefetch=2,
            grid=(1,),
            in_specs=[
                pl.BlockSpec(
                    (row_total, nao), lambda i, s, k: (0, 0), pipeline_mode=pl.Buffered(1)
                ),
                pl.BlockSpec(
                    (entries, LANE, LANE), lambda i, s, k: (0, 0, 0), pipeline_mode=pl.Buffered(1)
                ),
            ],
            out_specs=pl.BlockSpec((row_total, piece_chunks * LANE), lambda i, s, k: (0, 0)),
        )
        results.append(
            pl.pallas_call(
                kernel,
                grid_spec=grid_spec,
                out_shape=jax.ShapeDtypeStruct((row_total, piece_chunks * LANE), jnp.bfloat16),
                compiler_params=pltpu.CompilerParams(vmem_limit_bytes=60 * 1024 * 1024),
            )(starts, k_sorted, rows_all, padded)
        )
    return results

def per_device(tensor, tensor_pattern, green, green_pattern):
    layer_count = lax.axis_size("layer")
    row_count = lax.axis_size("row")
    if layer_count != row_count:
        return cannon_per_device(tensor, tensor_pattern, green, green_pattern)
    ri_local, mu_local, nu_local = tensor.shape
    tile_rows, tile_cols = green_pattern.shape
    tensor_mask = jnp.repeat(tensor_pattern, BLK, axis=1).astype(jnp.bfloat16)
    masked = tensor * tensor_mask[None, :, :]
    own = masked.reshape(ri_local * mu_local, nu_local)
    layer_index = lax.axis_index("layer")
    col_count = lax.axis_size("col")
    blocks, block_row, block_col = compressed_tile(green, green_pattern)
    parts = tuple(green_to_layers(part, row_count) for part in (blocks, block_row, block_col))
    group = row_count * col_count
    me = lax.axis_index("row") * col_count + lax.axis_index("col")
    received = [parts]
    for shift in range(1, group):
        pairs = [(i, (i + shift) % group) for i in range(group)]
        received.append(tuple(lax.ppermute(part, ("row", "col"), pairs) for part in parts))
    blocks, block_row, block_col = (
        jnp.stack([got[k] for got in received]) for k in range(len(parts))
    )
    band = ((me - jnp.arange(group)) % group)[:, None]
    entry_rows = band * tile_rows + block_row
    entry_rows = entry_rows.reshape(-1)
    entry_cols = block_col.reshape(-1)
    entry_blocks = blocks.reshape(-1, BLK, BLK)
    pieces = []
    for start in range(0, ri_local * mu_local, ROW_CHUNK):
        rows = lax.all_gather(own[start : start + ROW_CHUNK], "layer", axis=1, tiled=True)
        (piece,) = block_sparse_product(
            rows, entry_blocks, entry_rows, entry_cols, tile_cols * BLK, 1
        )
        pieces.append(product_to_owners(piece, row_count))
    product = jnp.concatenate(pieces, axis=0)
    return product.reshape(ri_local, mu_local, tile_cols * BLK)

def solution(mesh):
    in_specs = (
        P("row", "col", "layer"),
        P("col", "layer"),
        P(("layer", "col"), "row"),
        P(("layer", "col"), "row"),
    )
    out_specs = P("layer", "col", "row")
    return jax.shard_map(
        per_device, mesh=mesh, in_specs=in_specs, out_specs=out_specs, check_vma=False
    )
```

```python
import jax
import jax.numpy as jnp
from jax import lax
from jax.experimental import pallas as pl
from jax.experimental.pallas import tpu as pltpu
from jax.sharding import PartitionSpec as P

BLK = 64
CAP = 48
LANE = 128
ROW_CHUNK = 512


def passed_along(value, axis, by):
    length = lax.axis_size(axis)
    return lax.ppermute(value, axis, [(i, (i + by) % length) for i in range(length)])


def cannon_per_device(tensor, tensor_pattern, green, green_pattern):
    row_count = lax.axis_size("row")
    col_count = lax.axis_size("col")
    col_bits = col_count.bit_length() - 1
    row_index = lax.axis_index("row")
    col_index = lax.axis_index("col")
    odd_row = row_index % 2 == 1
    half_row = row_index // 2
    ri_local, mu_local, nu_local = tensor.shape
    width = nu_local // row_count
    tensor_mask = jnp.repeat(tensor_pattern, BLK, axis=1).astype(jnp.bfloat16)
    masked = tensor * tensor_mask[None, :, :]
    left_block = lax.all_to_all(masked, "row", split_axis=2, concat_axis=0, tiled=True)
    for bit_number in range(col_bits):
        arrived = passed_along(left_block, "row", -(2 << bit_number))
        left_block = jnp.where(col_index >> bit_number & 1 == 1, arrived, left_block)
    ri_total = left_block.shape[0]
    all_rows = ri_total * mu_local
    left_block = left_block.reshape(all_rows, width)
    tile_rows, tile_cols = green_pattern.shape
    green_mask = green_pattern.astype(jnp.bfloat16)[:, None, :, None]
    green_tile = (green.reshape(tile_rows, BLK, tile_cols, BLK) * green_mask).reshape(
        tile_rows * BLK, tile_cols * BLK
    )
    green_state = green_tile
    for bit_number in range(col_bits):
        arrived = passed_along(green_state, "col", -(1 << bit_number))
        green_state = jnp.where(half_row >> bit_number & 1 == 1, arrived, green_state)

    def advance(current_state):
        arrived_state = passed_along(current_state, "col", -1)
        return (arrived_state, arrived_state)

    def shift_left(block_now):
        return passed_along(block_now, "row", -1)

    def pair_turn(state_now, shift_last):
        product_sum, block_now, current_state, current = state_now
        green_half = jnp.where(odd_row, current[width:], current[:width])
        product_sum = product_sum + jnp.dot(
            block_now, green_half, preferred_element_type=jnp.float32
        )
        block_now = shift_left(block_now)
        previous = current
        current_state, current = advance(current_state)
        green_half = jnp.where(odd_row, current[:width], previous[width:])
        product_sum = product_sum + jnp.dot(
            block_now, green_half, preferred_element_type=jnp.float32
        )
        if shift_last:
            block_now = shift_left(block_now)
        return (product_sum, block_now, current_state, current)

    start = (
        jnp.zeros((all_rows, tile_cols * BLK), jnp.float32),
        left_block,
        green_state,
        green_state,
    )
    state_now = lax.fori_loop(
        0, col_count - 1, lambda turn_index, state_before: pair_turn(state_before, True), start
    )
    state_now = pair_turn(state_now, False)
    layer_terms = state_now[0].reshape(ri_total, mu_local, tile_cols * BLK)
    return lax.psum_scatter(layer_terms, "layer", scatter_dimension=0, tiled=True).astype(
        jnp.bfloat16
    )


def spread(size):
    return [2, 0, 3, 1] if size == 4 else list(range(size))


def green_to_layers(value, size):
    inverse = {quarter: layer for layer, quarter in enumerate(spread(size))}
    return lax.ppermute(
        value,
        ("layer", "row"),
        [(a * size + b, inverse[b] * size + a) for a in range(size) for b in range(size)],
    )


def product_to_owners(value, size):
    quarter = spread(size)
    return lax.ppermute(
        value,
        ("layer", "row"),
        [(a * size + b, b * size + quarter[a]) for a in range(size) for b in range(size)],
    )


def gathered_windows(green, window_rows, window_cols):
    count = window_rows.shape[0]

    def kernel(rows_ref, cols_ref, green_ref, out_ref):
        out_ref[0] = green_ref[...]

    grid_spec = pltpu.PrefetchScalarGridSpec(
        num_scalar_prefetch=2,
        grid=(count,),
        in_specs=[pl.BlockSpec((BLK, LANE), lambda e, r, c: (r[e], c[e]))],
        out_specs=pl.BlockSpec((1, BLK, LANE), lambda e, r, c: (e, 0, 0)),
    )
    return pl.pallas_call(
        kernel,
        grid_spec=grid_spec,
        out_shape=jax.ShapeDtypeStruct((count, BLK, LANE), green.dtype),
    )(window_rows.astype(jnp.int32), window_cols.astype(jnp.int32), green)


def compressed_tile(green, green_pattern):
    tile_rows, tile_cols = green_pattern.shape
    cap = min(CAP, tile_rows * tile_cols)
    flat = green_pattern.reshape(-1)
    (spots,) = jnp.nonzero(flat != 0, size=cap, fill_value=0)
    valid = jnp.arange(cap) < jnp.sum(flat != 0)
    block_row = spots // tile_cols
    block_col = spots % tile_cols
    windows = gathered_windows(green, block_row, block_col // 2)
    left = (block_col % 2 == 0)[:, None, None]
    blocks = jnp.where(left, windows[:, :, :BLK], windows[:, :, BLK:])
    scale = jnp.where(valid, flat[spots], 0).astype(jnp.bfloat16)
    blocks = blocks * scale[:, None, None]
    return blocks, block_row, block_col


def padded_blocks(blocks, block_rows, block_cols):
    empty = jnp.zeros_like(blocks)
    left = (block_cols % 2 == 0)[:, None, None]
    top = (block_rows % 2 == 0)[:, None, None]
    half = jnp.concatenate([jnp.where(left, blocks, empty), jnp.where(left, empty, blocks)], axis=2)
    empty = jnp.zeros_like(half)
    return jnp.concatenate([jnp.where(top, half, empty), jnp.where(top, empty, half)], axis=1)


def block_sparse_product(rows_all, blocks, block_rows, block_cols, width, pieces):
    row_total, nao = rows_all.shape
    entries = blocks.shape[0]
    chunks = width // LANE
    piece_chunks = chunks // pieces
    chunk_of = block_cols // 2
    order = jnp.argsort(chunk_of)
    chunk_sorted = chunk_of[order]
    starts = jnp.searchsorted(chunk_sorted, jnp.arange(chunks + 1), side="left", method="compare_all").astype(jnp.int32)
    k_sorted = (block_rows[order] // 2).astype(jnp.int32)
    padded = padded_blocks(blocks, block_rows, block_cols)[order]
    results = []
    for piece in range(pieces):
        first = piece * piece_chunks

        def kernel(starts_ref, k_ref, t_ref, g_ref, o_ref, first=first):
            def window(entry):
                return t_ref[:, pl.ds(pl.multiple_of(k_ref[entry] * LANE, LANE), LANE)]

            def one(entry, acc):
                return acc + jnp.dot(window(entry), g_ref[entry], preferred_element_type=jnp.float32)

            def grouped(width, base):
                def step(index, acc):
                    entry = base + width * index
                    lhs = jnp.concatenate([window(entry + j) for j in range(width)], axis=1)
                    rhs = jnp.concatenate([g_ref[entry + j] for j in range(width)], axis=0)
                    return acc + jnp.dot(lhs, rhs, preferred_element_type=jnp.float32)

                return step

            for chunk in range(piece_chunks):
                begin = starts_ref[first + chunk]
                end = starts_ref[first + chunk + 1]
                acc = jnp.zeros((row_total, LANE), jnp.float32)
                for width in (4, 2):
                    count = (end - begin) // width
                    acc = lax.fori_loop(0, count, grouped(width, begin), acc)
                    begin = begin + width * count
                acc = lax.fori_loop(begin, end, one, acc)
                o_ref[:, chunk * LANE : (chunk + 1) * LANE] = acc.astype(o_ref.dtype)

        grid_spec = pltpu.PrefetchScalarGridSpec(
            num_scalar_prefetch=2,
            grid=(1,),
            in_specs=[
                pl.BlockSpec(
                    (row_total, nao), lambda i, s, k: (0, 0), pipeline_mode=pl.Buffered(1)
                ),
                pl.BlockSpec(
                    (entries, LANE, LANE), lambda i, s, k: (0, 0, 0), pipeline_mode=pl.Buffered(1)
                ),
            ],
            out_specs=pl.BlockSpec((row_total, piece_chunks * LANE), lambda i, s, k: (0, 0)),
        )
        results.append(
            pl.pallas_call(
                kernel,
                grid_spec=grid_spec,
                out_shape=jax.ShapeDtypeStruct((row_total, piece_chunks * LANE), jnp.bfloat16),
                compiler_params=pltpu.CompilerParams(vmem_limit_bytes=60 * 1024 * 1024),
            )(starts, k_sorted, rows_all, padded)
        )
    return results

def per_device(tensor, tensor_pattern, green, green_pattern):
    layer_count = lax.axis_size("layer")
    row_count = lax.axis_size("row")
    if layer_count != row_count:
        return cannon_per_device(tensor, tensor_pattern, green, green_pattern)
    ri_local, mu_local, nu_local = tensor.shape
    tile_rows, tile_cols = green_pattern.shape
    tensor_mask = jnp.repeat(tensor_pattern, BLK, axis=1).astype(jnp.bfloat16)
    masked = tensor * tensor_mask[None, :, :]
    own = masked.reshape(ri_local * mu_local, nu_local)
    layer_index = lax.axis_index("layer")
    col_count = lax.axis_size("col")
    blocks, block_row, block_col = compressed_tile(green, green_pattern)
    parts = tuple(green_to_layers(part, row_count) for part in (blocks, block_row, block_col))
    group = row_count * col_count
    me = lax.axis_index("row") * col_count + lax.axis_index("col")
    received = [parts]
    for shift in range(1, group):
        pairs = [(i, (i + shift) % group) for i in range(group)]
        received.append(tuple(lax.ppermute(part, ("row", "col"), pairs) for part in parts))
    blocks, block_row, block_col = (
        jnp.stack([got[k] for got in received]) for k in range(len(parts))
    )
    band = ((me - jnp.arange(group)) % group)[:, None]
    entry_rows = band * tile_rows + block_row
    entry_rows = entry_rows.reshape(-1)
    entry_cols = block_col.reshape(-1)
    entry_blocks = blocks.reshape(-1, BLK, BLK)
    pieces = []
    for start in range(0, ri_local * mu_local, ROW_CHUNK):
        rows = lax.all_gather(own[start : start + ROW_CHUNK], "layer", axis=1, tiled=True)
        (piece,) = block_sparse_product(
            rows, entry_blocks, entry_rows, entry_cols, tile_cols * BLK, 1
        )
        pieces.append(product_to_owners(piece, row_count))
    product = jnp.concatenate(pieces, axis=0)
    return product.reshape(ri_local, mu_local, tile_cols * BLK)

def solution(mesh):
    in_specs = (
        P("row", "col", "layer"),
        P("col", "layer"),
        P(("layer", "col"), "row"),
        P(("layer", "col"), "row"),
    )
    out_specs = P("layer", "col", "row")
    return jax.shard_map(
        per_device, mesh=mesh, in_specs=in_specs, out_specs=out_specs, check_vma=False
    )
```

```python
import jax
import jax.numpy as jnp
from jax import lax
from jax.experimental import pallas as pl
from jax.experimental.pallas import tpu as pltpu
from jax.sharding import PartitionSpec as P

BLK = 64
CAP = 48
LANE = 128
ROW_CHUNK = 128


def passed_along(value, axis, by):
    length = lax.axis_size(axis)
    return lax.ppermute(value, axis, [(i, (i + by) % length) for i in range(length)])


def cannon_per_device(tensor, tensor_pattern, green, green_pattern):
    row_count = lax.axis_size("row")
    col_count = lax.axis_size("col")
    col_bits = col_count.bit_length() - 1
    row_index = lax.axis_index("row")
    col_index = lax.axis_index("col")
    odd_row = row_index % 2 == 1
    half_row = row_index // 2
    ri_local, mu_local, nu_local = tensor.shape
    width = nu_local // row_count
    tensor_mask = jnp.repeat(tensor_pattern, BLK, axis=1).astype(jnp.bfloat16)
    masked = tensor * tensor_mask[None, :, :]
    left_block = lax.all_to_all(masked, "row", split_axis=2, concat_axis=0, tiled=True)
    for bit_number in range(col_bits):
        arrived = passed_along(left_block, "row", -(2 << bit_number))
        left_block = jnp.where(col_index >> bit_number & 1 == 1, arrived, left_block)
    ri_total = left_block.shape[0]
    all_rows = ri_total * mu_local
    left_block = left_block.reshape(all_rows, width)
    tile_rows, tile_cols = green_pattern.shape
    green_mask = green_pattern.astype(jnp.bfloat16)[:, None, :, None]
    green_tile = (green.reshape(tile_rows, BLK, tile_cols, BLK) * green_mask).reshape(
        tile_rows * BLK, tile_cols * BLK
    )
    green_state = green_tile
    for bit_number in range(col_bits):
        arrived = passed_along(green_state, "col", -(1 << bit_number))
        green_state = jnp.where(half_row >> bit_number & 1 == 1, arrived, green_state)

    def advance(current_state):
        arrived_state = passed_along(current_state, "col", -1)
        return (arrived_state, arrived_state)

    def shift_left(block_now):
        return passed_along(block_now, "row", -1)

    def pair_turn(state_now, shift_last):
        product_sum, block_now, current_state, current = state_now
        green_half = jnp.where(odd_row, current[width:], current[:width])
        product_sum = product_sum + jnp.dot(
            block_now, green_half, preferred_element_type=jnp.float32
        )
        block_now = shift_left(block_now)
        previous = current
        current_state, current = advance(current_state)
        green_half = jnp.where(odd_row, current[:width], previous[width:])
        product_sum = product_sum + jnp.dot(
            block_now, green_half, preferred_element_type=jnp.float32
        )
        if shift_last:
            block_now = shift_left(block_now)
        return (product_sum, block_now, current_state, current)

    start = (
        jnp.zeros((all_rows, tile_cols * BLK), jnp.float32),
        left_block,
        green_state,
        green_state,
    )
    state_now = lax.fori_loop(
        0, col_count - 1, lambda turn_index, state_before: pair_turn(state_before, True), start
    )
    state_now = pair_turn(state_now, False)
    layer_terms = state_now[0].reshape(ri_total, mu_local, tile_cols * BLK)
    return lax.psum_scatter(layer_terms, "layer", scatter_dimension=0, tiled=True).astype(
        jnp.bfloat16
    )


def spread(size):
    return [2, 0, 3, 1] if size == 4 else list(range(size))


def green_to_layers(value, size):
    inverse = {quarter: layer for layer, quarter in enumerate(spread(size))}
    return lax.ppermute(
        value,
        ("layer", "row"),
        [(a * size + b, inverse[b] * size + a) for a in range(size) for b in range(size)],
    )


def product_to_owners(value, size):
    quarter = spread(size)
    return lax.ppermute(
        value,
        ("layer", "row"),
        [(a * size + b, b * size + quarter[a]) for a in range(size) for b in range(size)],
    )


def gathered_windows(green, window_rows, window_cols):
    count = window_rows.shape[0]

    def kernel(rows_ref, cols_ref, green_ref, out_ref):
        out_ref[0] = green_ref[...]

    grid_spec = pltpu.PrefetchScalarGridSpec(
        num_scalar_prefetch=2,
        grid=(count,),
        in_specs=[pl.BlockSpec((BLK, LANE), lambda e, r, c: (r[e], c[e]))],
        out_specs=pl.BlockSpec((1, BLK, LANE), lambda e, r, c: (e, 0, 0)),
    )
    return pl.pallas_call(
        kernel,
        grid_spec=grid_spec,
        out_shape=jax.ShapeDtypeStruct((count, BLK, LANE), green.dtype),
    )(window_rows.astype(jnp.int32), window_cols.astype(jnp.int32), green)


def compressed_tile(green, green_pattern):
    tile_rows, tile_cols = green_pattern.shape
    cap = min(CAP, tile_rows * tile_cols)
    flat = green_pattern.reshape(-1)
    (spots,) = jnp.nonzero(flat != 0, size=cap, fill_value=0)
    valid = jnp.arange(cap) < jnp.sum(flat != 0)
    block_row = spots // tile_cols
    block_col = spots % tile_cols
    windows = gathered_windows(green, block_row, block_col // 2)
    left = (block_col % 2 == 0)[:, None, None]
    blocks = jnp.where(left, windows[:, :, :BLK], windows[:, :, BLK:])
    scale = jnp.where(valid, flat[spots], 0).astype(jnp.bfloat16)
    blocks = blocks * scale[:, None, None]
    return blocks, block_row, block_col


def padded_blocks(blocks, block_rows, block_cols):
    empty = jnp.zeros_like(blocks)
    left = (block_cols % 2 == 0)[:, None, None]
    top = (block_rows % 2 == 0)[:, None, None]
    half = jnp.concatenate([jnp.where(left, blocks, empty), jnp.where(left, empty, blocks)], axis=2)
    empty = jnp.zeros_like(half)
    return jnp.concatenate([jnp.where(top, half, empty), jnp.where(top, empty, half)], axis=1)


def block_sparse_product(rows_all, blocks, block_rows, block_cols, width, pieces):
    row_total, nao = rows_all.shape
    entries = blocks.shape[0]
    chunks = width // LANE
    piece_chunks = chunks // pieces
    chunk_of = block_cols // 2
    order = jnp.argsort(chunk_of)
    chunk_sorted = chunk_of[order]
    starts = jnp.searchsorted(chunk_sorted, jnp.arange(chunks + 1), side="left", method="compare_all").astype(jnp.int32)
    k_sorted = (block_rows[order] // 2).astype(jnp.int32)
    padded = padded_blocks(blocks, block_rows, block_cols)[order]
    results = []
    for piece in range(pieces):
        first = piece * piece_chunks

        def kernel(starts_ref, k_ref, t_ref, g_ref, o_ref, first=first):
            def window(entry):
                return t_ref[:, pl.ds(pl.multiple_of(k_ref[entry] * LANE, LANE), LANE)]

            def one(entry, acc):
                return acc + jnp.dot(window(entry), g_ref[entry], preferred_element_type=jnp.float32)

            def grouped(width, base):
                def step(index, acc):
                    entry = base + width * index
                    lhs = jnp.concatenate([window(entry + j) for j in range(width)], axis=1)
                    rhs = jnp.concatenate([g_ref[entry + j] for j in range(width)], axis=0)
                    return acc + jnp.dot(lhs, rhs, preferred_element_type=jnp.float32)

                return step

            for chunk in range(piece_chunks):
                begin = starts_ref[first + chunk]
                end = starts_ref[first + chunk + 1]
                acc = jnp.zeros((row_total, LANE), jnp.float32)
                for width in (4, 2):
                    count = (end - begin) // width
                    acc = lax.fori_loop(0, count, grouped(width, begin), acc)
                    begin = begin + width * count
                acc = lax.fori_loop(begin, end, one, acc)
                o_ref[:, chunk * LANE : (chunk + 1) * LANE] = acc.astype(o_ref.dtype)

        grid_spec = pltpu.PrefetchScalarGridSpec(
            num_scalar_prefetch=2,
            grid=(1,),
            in_specs=[
                pl.BlockSpec(
                    (row_total, nao), lambda i, s, k: (0, 0), pipeline_mode=pl.Buffered(1)
                ),
                pl.BlockSpec(
                    (entries, LANE, LANE), lambda i, s, k: (0, 0, 0), pipeline_mode=pl.Buffered(1)
                ),
            ],
            out_specs=pl.BlockSpec((row_total, piece_chunks * LANE), lambda i, s, k: (0, 0)),
        )
        results.append(
            pl.pallas_call(
                kernel,
                grid_spec=grid_spec,
                out_shape=jax.ShapeDtypeStruct((row_total, piece_chunks * LANE), jnp.bfloat16),
                compiler_params=pltpu.CompilerParams(vmem_limit_bytes=60 * 1024 * 1024),
            )(starts, k_sorted, rows_all, padded)
        )
    return results

def per_device(tensor, tensor_pattern, green, green_pattern):
    layer_count = lax.axis_size("layer")
    row_count = lax.axis_size("row")
    if layer_count != row_count:
        return cannon_per_device(tensor, tensor_pattern, green, green_pattern)
    ri_local, mu_local, nu_local = tensor.shape
    tile_rows, tile_cols = green_pattern.shape
    tensor_mask = jnp.repeat(tensor_pattern, BLK, axis=1).astype(jnp.bfloat16)
    masked = tensor * tensor_mask[None, :, :]
    own = masked.reshape(ri_local * mu_local, nu_local)
    layer_index = lax.axis_index("layer")
    col_count = lax.axis_size("col")
    blocks, block_row, block_col = compressed_tile(green, green_pattern)
    parts = tuple(green_to_layers(part, row_count) for part in (blocks, block_row, block_col))
    group = row_count * col_count
    me = lax.axis_index("row") * col_count + lax.axis_index("col")
    received = [parts]
    for shift in range(1, group):
        pairs = [(i, (i + shift) % group) for i in range(group)]
        received.append(tuple(lax.ppermute(part, ("row", "col"), pairs) for part in parts))
    blocks, block_row, block_col = (
        jnp.stack([got[k] for got in received]) for k in range(len(parts))
    )
    band = ((me - jnp.arange(group)) % group)[:, None]
    entry_rows = band * tile_rows + block_row
    entry_rows = entry_rows.reshape(-1)
    entry_cols = block_col.reshape(-1)
    entry_blocks = blocks.reshape(-1, BLK, BLK)
    pieces = []
    for start in range(0, ri_local * mu_local, ROW_CHUNK):
        rows = lax.all_gather(own[start : start + ROW_CHUNK], "layer", axis=1, tiled=True)
        (piece,) = block_sparse_product(
            rows, entry_blocks, entry_rows, entry_cols, tile_cols * BLK, 1
        )
        pieces.append(product_to_owners(piece, row_count))
    product = jnp.concatenate(pieces, axis=0)
    return product.reshape(ri_local, mu_local, tile_cols * BLK)

def solution(mesh):
    in_specs = (
        P("row", "col", "layer"),
        P("col", "layer"),
        P(("layer", "col"), "row"),
        P(("layer", "col"), "row"),
    )
    out_specs = P("layer", "col", "row")
    return jax.shard_map(
        per_device, mesh=mesh, in_specs=in_specs, out_specs=out_specs, check_vma=False
    )
```

```python
import jax
import jax.numpy as jnp
from jax import lax
from jax.experimental import pallas as pl
from jax.experimental.pallas import tpu as pltpu
from jax.sharding import PartitionSpec as P

BLK = 64
CAP = 48
LANE = 128
ROW_CHUNK = 256


def passed_along(value, axis, by):
    length = lax.axis_size(axis)
    return lax.ppermute(value, axis, [(i, (i + by) % length) for i in range(length)])


def cannon_per_device(tensor, tensor_pattern, green, green_pattern):
    row_count = lax.axis_size("row")
    col_count = lax.axis_size("col")
    col_bits = col_count.bit_length() - 1
    row_index = lax.axis_index("row")
    col_index = lax.axis_index("col")
    odd_row = row_index % 2 == 1
    half_row = row_index // 2
    ri_local, mu_local, nu_local = tensor.shape
    width = nu_local // row_count
    tensor_mask = jnp.repeat(tensor_pattern, BLK, axis=1).astype(jnp.bfloat16)
    masked = tensor * tensor_mask[None, :, :]
    left_block = lax.all_to_all(masked, "row", split_axis=2, concat_axis=0, tiled=True)
    for bit_number in range(col_bits):
        arrived = passed_along(left_block, "row", -(2 << bit_number))
        left_block = jnp.where(col_index >> bit_number & 1 == 1, arrived, left_block)
    ri_total = left_block.shape[0]
    all_rows = ri_total * mu_local
    left_block = left_block.reshape(all_rows, width)
    tile_rows, tile_cols = green_pattern.shape
    green_mask = green_pattern.astype(jnp.bfloat16)[:, None, :, None]
    green_tile = (green.reshape(tile_rows, BLK, tile_cols, BLK) * green_mask).reshape(
        tile_rows * BLK, tile_cols * BLK
    )
    green_state = green_tile
    for bit_number in range(col_bits):
        arrived = passed_along(green_state, "col", -(1 << bit_number))
        green_state = jnp.where(half_row >> bit_number & 1 == 1, arrived, green_state)

    def advance(current_state):
        arrived_state = passed_along(current_state, "col", -1)
        return (arrived_state, arrived_state)

    def shift_left(block_now):
        return passed_along(block_now, "row", -1)

    def pair_turn(state_now, shift_last):
        product_sum, block_now, current_state, current = state_now
        green_half = jnp.where(odd_row, current[width:], current[:width])
        product_sum = product_sum + jnp.dot(
            block_now, green_half, preferred_element_type=jnp.float32
        )
        block_now = shift_left(block_now)
        previous = current
        current_state, current = advance(current_state)
        green_half = jnp.where(odd_row, current[:width], previous[width:])
        product_sum = product_sum + jnp.dot(
            block_now, green_half, preferred_element_type=jnp.float32
        )
        if shift_last:
            block_now = shift_left(block_now)
        return (product_sum, block_now, current_state, current)

    start = (
        jnp.zeros((all_rows, tile_cols * BLK), jnp.float32),
        left_block,
        green_state,
        green_state,
    )
    state_now = lax.fori_loop(
        0, col_count - 1, lambda turn_index, state_before: pair_turn(state_before, True), start
    )
    state_now = pair_turn(state_now, False)
    layer_terms = state_now[0].reshape(ri_total, mu_local, tile_cols * BLK)
    return lax.psum_scatter(layer_terms, "layer", scatter_dimension=0, tiled=True).astype(
        jnp.bfloat16
    )


def spread(size):
    return [2, 0, 3, 1] if size == 4 else list(range(size))


def green_to_layers(value, size):
    inverse = {quarter: layer for layer, quarter in enumerate(spread(size))}
    return lax.ppermute(
        value,
        ("layer", "row"),
        [(a * size + b, inverse[b] * size + a) for a in range(size) for b in range(size)],
    )


def product_to_owners(value, size):
    quarter = spread(size)
    return lax.ppermute(
        value,
        ("layer", "row"),
        [(a * size + b, b * size + quarter[a]) for a in range(size) for b in range(size)],
    )


def gathered_windows(green, window_rows, window_cols):
    count = window_rows.shape[0]

    def kernel(rows_ref, cols_ref, green_ref, out_ref):
        out_ref[0] = green_ref[...]

    grid_spec = pltpu.PrefetchScalarGridSpec(
        num_scalar_prefetch=2,
        grid=(count,),
        in_specs=[pl.BlockSpec((BLK, LANE), lambda e, r, c: (r[e], c[e]))],
        out_specs=pl.BlockSpec((1, BLK, LANE), lambda e, r, c: (e, 0, 0)),
    )
    return pl.pallas_call(
        kernel,
        grid_spec=grid_spec,
        out_shape=jax.ShapeDtypeStruct((count, BLK, LANE), green.dtype),
    )(window_rows.astype(jnp.int32), window_cols.astype(jnp.int32), green)


def compressed_tile(green, green_pattern):
    tile_rows, tile_cols = green_pattern.shape
    cap = min(CAP, tile_rows * tile_cols)
    flat = green_pattern.reshape(-1)
    (spots,) = jnp.nonzero(flat != 0, size=cap, fill_value=0)
    valid = jnp.arange(cap) < jnp.sum(flat != 0)
    block_row = spots // tile_cols
    block_col = spots % tile_cols
    windows = gathered_windows(green, block_row, block_col // 2)
    left = (block_col % 2 == 0)[:, None, None]
    blocks = jnp.where(left, windows[:, :, :BLK], windows[:, :, BLK:])
    scale = jnp.where(valid, flat[spots], 0).astype(jnp.bfloat16)
    blocks = blocks * scale[:, None, None]
    return blocks, block_row, block_col


def padded_blocks(blocks, block_rows, block_cols):
    empty = jnp.zeros_like(blocks)
    left = (block_cols % 2 == 0)[:, None, None]
    top = (block_rows % 2 == 0)[:, None, None]
    half = jnp.concatenate([jnp.where(left, blocks, empty), jnp.where(left, empty, blocks)], axis=2)
    empty = jnp.zeros_like(half)
    return jnp.concatenate([jnp.where(top, half, empty), jnp.where(top, empty, half)], axis=1)


def block_sparse_product(rows_all, blocks, block_rows, block_cols, width, pieces):
    row_total, nao = rows_all.shape
    entries = blocks.shape[0]
    chunks = width // LANE
    piece_chunks = chunks // pieces
    chunk_of = block_cols // 2
    order = jnp.argsort(chunk_of)
    chunk_sorted = chunk_of[order]
    starts = jnp.searchsorted(chunk_sorted, jnp.arange(chunks + 1), side="left", method="compare_all").astype(jnp.int32)
    k_sorted = (block_rows[order] // 2).astype(jnp.int32)
    padded = padded_blocks(blocks, block_rows, block_cols)[order]
    results = []
    for piece in range(pieces):
        first = piece * piece_chunks

        def kernel(starts_ref, k_ref, t_ref, g_ref, o_ref, first=first):
            def window(entry):
                return t_ref[:, pl.ds(pl.multiple_of(k_ref[entry] * LANE, LANE), LANE)]

            def one(entry, acc):
                return acc + jnp.dot(window(entry), g_ref[entry], preferred_element_type=jnp.float32)

            def grouped(width, base):
                def step(index, acc):
                    entry = base + width * index
                    lhs = jnp.concatenate([window(entry + j) for j in range(width)], axis=1)
                    rhs = jnp.concatenate([g_ref[entry + j] for j in range(width)], axis=0)
                    return acc + jnp.dot(lhs, rhs, preferred_element_type=jnp.float32)

                return step

            for chunk in range(piece_chunks):
                begin = starts_ref[first + chunk]
                end = starts_ref[first + chunk + 1]
                acc = jnp.zeros((row_total, LANE), jnp.float32)
                for width in (4, 2):
                    count = (end - begin) // width
                    acc = lax.fori_loop(0, count, grouped(width, begin), acc)
                    begin = begin + width * count
                acc = lax.fori_loop(begin, end, one, acc)
                o_ref[:, chunk * LANE : (chunk + 1) * LANE] = acc.astype(o_ref.dtype)

        grid_spec = pltpu.PrefetchScalarGridSpec(
            num_scalar_prefetch=2,
            grid=(1,),
            in_specs=[
                pl.BlockSpec(
                    (row_total, nao), lambda i, s, k: (0, 0), pipeline_mode=pl.Buffered(1)
                ),
                pl.BlockSpec(
                    (entries, LANE, LANE), lambda i, s, k: (0, 0, 0), pipeline_mode=pl.Buffered(1)
                ),
            ],
            out_specs=pl.BlockSpec((row_total, piece_chunks * LANE), lambda i, s, k: (0, 0)),
        )
        results.append(
            pl.pallas_call(
                kernel,
                grid_spec=grid_spec,
                out_shape=jax.ShapeDtypeStruct((row_total, piece_chunks * LANE), jnp.bfloat16),
                compiler_params=pltpu.CompilerParams(vmem_limit_bytes=60 * 1024 * 1024),
            )(starts, k_sorted, rows_all, padded)
        )
    return results

def per_device(tensor, tensor_pattern, green, green_pattern):
    layer_count = lax.axis_size("layer")
    row_count = lax.axis_size("row")
    if layer_count != row_count:
        return cannon_per_device(tensor, tensor_pattern, green, green_pattern)
    ri_local, mu_local, nu_local = tensor.shape
    tile_rows, tile_cols = green_pattern.shape
    tensor_mask = jnp.repeat(tensor_pattern, BLK, axis=1).astype(jnp.bfloat16)
    masked = tensor * tensor_mask[None, :, :]
    own = masked.reshape(ri_local * mu_local, nu_local)
    layer_index = lax.axis_index("layer")
    col_count = lax.axis_size("col")
    blocks, block_row, block_col = compressed_tile(green, green_pattern)
    parts = tuple(green_to_layers(part, row_count) for part in (blocks, block_row, block_col))
    group = row_count * col_count
    me = lax.axis_index("row") * col_count + lax.axis_index("col")
    received = [parts]
    for shift in range(1, group):
        pairs = [(i, (i + shift) % group) for i in range(group)]
        received.append(tuple(lax.ppermute(part, ("row", "col"), pairs) for part in parts))
    blocks, block_row, block_col = (
        jnp.stack([got[k] for got in received]) for k in range(len(parts))
    )
    band = ((me - jnp.arange(group)) % group)[:, None]
    entry_rows = band * tile_rows + block_row
    entry_rows = entry_rows.reshape(-1)
    entry_cols = block_col.reshape(-1)
    entry_blocks = blocks.reshape(-1, BLK, BLK)
    pieces = []
    total_rows = ri_local * mu_local
    bounds = [0]
    while bounds[-1] < total_rows:
        size = ROW_CHUNK if bounds[-1] < total_rows // 2 else 2 * ROW_CHUNK
        bounds.append(min(total_rows, bounds[-1] + size))
    for start, stop in zip(bounds[:-1], bounds[1:]):
        rows = lax.all_gather(own[start:stop], "layer", axis=1, tiled=True)
        (piece,) = block_sparse_product(
            rows, entry_blocks, entry_rows, entry_cols, tile_cols * BLK, 1
        )
        pieces.append(product_to_owners(piece, row_count))
    product = jnp.concatenate(pieces, axis=0)
    return product.reshape(ri_local, mu_local, tile_cols * BLK)

def solution(mesh):
    in_specs = (
        P("row", "col", "layer"),
        P("col", "layer"),
        P(("layer", "col"), "row"),
        P(("layer", "col"), "row"),
    )
    out_specs = P("layer", "col", "row")
    return jax.shard_map(
        per_device, mesh=mesh, in_specs=in_specs, out_specs=out_specs, check_vma=False
    )
```

```python
import jax
import jax.numpy as jnp
from jax import lax
from jax.experimental import pallas as pl
from jax.experimental.pallas import tpu as pltpu
from jax.sharding import PartitionSpec as P

BLK = 64
CAP = 48
LANE = 128
ROW_CHUNK = 256


def passed_along(value, axis, by):
    length = lax.axis_size(axis)
    return lax.ppermute(value, axis, [(i, (i + by) % length) for i in range(length)])


def cannon_per_device(tensor, tensor_pattern, green, green_pattern):
    row_count = lax.axis_size("row")
    col_count = lax.axis_size("col")
    col_bits = col_count.bit_length() - 1
    row_index = lax.axis_index("row")
    col_index = lax.axis_index("col")
    odd_row = row_index % 2 == 1
    half_row = row_index // 2
    ri_local, mu_local, nu_local = tensor.shape
    width = nu_local // row_count
    tensor_mask = jnp.repeat(tensor_pattern, BLK, axis=1).astype(jnp.bfloat16)
    masked = tensor * tensor_mask[None, :, :]
    left_block = lax.all_to_all(masked, "row", split_axis=2, concat_axis=0, tiled=True)
    for bit_number in range(col_bits):
        arrived = passed_along(left_block, "row", -(2 << bit_number))
        left_block = jnp.where(col_index >> bit_number & 1 == 1, arrived, left_block)
    ri_total = left_block.shape[0]
    all_rows = ri_total * mu_local
    left_block = left_block.reshape(all_rows, width)
    tile_rows, tile_cols = green_pattern.shape
    green_mask = green_pattern.astype(jnp.bfloat16)[:, None, :, None]
    green_tile = (green.reshape(tile_rows, BLK, tile_cols, BLK) * green_mask).reshape(
        tile_rows * BLK, tile_cols * BLK
    )
    green_state = green_tile
    for bit_number in range(col_bits):
        arrived = passed_along(green_state, "col", -(1 << bit_number))
        green_state = jnp.where(half_row >> bit_number & 1 == 1, arrived, green_state)

    def advance(current_state):
        arrived_state = passed_along(current_state, "col", -1)
        return (arrived_state, arrived_state)

    def shift_left(block_now):
        return passed_along(block_now, "row", -1)

    def pair_turn(state_now, shift_last):
        product_sum, block_now, current_state, current = state_now
        green_half = jnp.where(odd_row, current[width:], current[:width])
        product_sum = product_sum + jnp.dot(
            block_now, green_half, preferred_element_type=jnp.float32
        )
        block_now = shift_left(block_now)
        previous = current
        current_state, current = advance(current_state)
        green_half = jnp.where(odd_row, current[:width], previous[width:])
        product_sum = product_sum + jnp.dot(
            block_now, green_half, preferred_element_type=jnp.float32
        )
        if shift_last:
            block_now = shift_left(block_now)
        return (product_sum, block_now, current_state, current)

    start = (
        jnp.zeros((all_rows, tile_cols * BLK), jnp.float32),
        left_block,
        green_state,
        green_state,
    )
    state_now = lax.fori_loop(
        0, col_count - 1, lambda turn_index, state_before: pair_turn(state_before, True), start
    )
    state_now = pair_turn(state_now, False)
    layer_terms = state_now[0].reshape(ri_total, mu_local, tile_cols * BLK)
    return lax.psum_scatter(layer_terms, "layer", scatter_dimension=0, tiled=True).astype(
        jnp.bfloat16
    )


def spread(size):
    return [2, 0, 3, 1] if size == 4 else list(range(size))


def green_to_layers(value, size):
    inverse = {quarter: layer for layer, quarter in enumerate(spread(size))}
    return lax.ppermute(
        value,
        ("layer", "row"),
        [(a * size + b, inverse[b] * size + a) for a in range(size) for b in range(size)],
    )


def product_to_owners(value, size):
    quarter = spread(size)
    return lax.ppermute(
        value,
        ("layer", "row"),
        [(a * size + b, b * size + quarter[a]) for a in range(size) for b in range(size)],
    )


def gathered_windows(green, window_rows, window_cols):
    count = window_rows.shape[0]

    def kernel(rows_ref, cols_ref, green_ref, out_ref):
        out_ref[0] = green_ref[...]

    grid_spec = pltpu.PrefetchScalarGridSpec(
        num_scalar_prefetch=2,
        grid=(count,),
        in_specs=[pl.BlockSpec((BLK, LANE), lambda e, r, c: (r[e], c[e]))],
        out_specs=pl.BlockSpec((1, BLK, LANE), lambda e, r, c: (e, 0, 0)),
    )
    return pl.pallas_call(
        kernel,
        grid_spec=grid_spec,
        out_shape=jax.ShapeDtypeStruct((count, BLK, LANE), green.dtype),
    )(window_rows.astype(jnp.int32), window_cols.astype(jnp.int32), green)


def compressed_tile(green, green_pattern):
    tile_rows, tile_cols = green_pattern.shape
    cap = min(CAP, tile_rows * tile_cols)
    flat = green_pattern.reshape(-1)
    (spots,) = jnp.nonzero(flat != 0, size=cap, fill_value=0)
    valid = jnp.arange(cap) < jnp.sum(flat != 0)
    block_row = spots // tile_cols
    block_col = spots % tile_cols
    windows = gathered_windows(green, block_row, block_col // 2)
    left = (block_col % 2 == 0)[:, None, None]
    blocks = jnp.where(left, windows[:, :, :BLK], windows[:, :, BLK:])
    scale = jnp.where(valid, flat[spots], 0).astype(jnp.bfloat16)
    blocks = blocks * scale[:, None, None]
    return blocks, block_row, block_col


def padded_blocks(blocks, block_rows, block_cols):
    empty = jnp.zeros_like(blocks)
    left = (block_cols % 2 == 0)[:, None, None]
    top = (block_rows % 2 == 0)[:, None, None]
    half = jnp.concatenate([jnp.where(left, blocks, empty), jnp.where(left, empty, blocks)], axis=2)
    empty = jnp.zeros_like(half)
    return jnp.concatenate([jnp.where(top, half, empty), jnp.where(top, empty, half)], axis=1)


def block_sparse_product(rows_all, blocks, block_rows, block_cols, width, pieces):
    row_total, nao = rows_all.shape
    entries = blocks.shape[0]
    chunks = width // LANE
    piece_chunks = chunks // pieces
    chunk_of = block_cols // 2
    order = jnp.argsort(chunk_of)
    chunk_sorted = chunk_of[order]
    starts = jnp.searchsorted(chunk_sorted, jnp.arange(chunks + 1), side="left", method="compare_all").astype(jnp.int32)
    k_sorted = (block_rows[order] // 2).astype(jnp.int32)
    padded = padded_blocks(blocks, block_rows, block_cols)[order]
    results = []
    for piece in range(pieces):
        first = piece * piece_chunks

        def kernel(starts_ref, k_ref, t_ref, g_ref, o_ref, first=first):
            def window(entry):
                return t_ref[:, pl.ds(pl.multiple_of(k_ref[entry] * LANE, LANE), LANE)]

            def one(entry, acc):
                return acc + jnp.dot(window(entry), g_ref[entry], preferred_element_type=jnp.float32)

            def grouped(width, base):
                def step(index, acc):
                    entry = base + width * index
                    lhs = jnp.concatenate([window(entry + j) for j in range(width)], axis=1)
                    rhs = jnp.concatenate([g_ref[entry + j] for j in range(width)], axis=0)
                    return acc + jnp.dot(lhs, rhs, preferred_element_type=jnp.float32)

                return step

            for chunk in range(piece_chunks):
                begin = starts_ref[first + chunk]
                end = starts_ref[first + chunk + 1]
                acc = jnp.zeros((row_total, LANE), jnp.float32)
                for width in (8, 4, 2):
                    count = (end - begin) // width
                    acc = lax.fori_loop(0, count, grouped(width, begin), acc)
                    begin = begin + width * count
                acc = lax.fori_loop(begin, end, one, acc)
                o_ref[:, chunk * LANE : (chunk + 1) * LANE] = acc.astype(o_ref.dtype)

        grid_spec = pltpu.PrefetchScalarGridSpec(
            num_scalar_prefetch=2,
            grid=(1,),
            in_specs=[
                pl.BlockSpec(
                    (row_total, nao), lambda i, s, k: (0, 0), pipeline_mode=pl.Buffered(1)
                ),
                pl.BlockSpec(
                    (entries, LANE, LANE), lambda i, s, k: (0, 0, 0), pipeline_mode=pl.Buffered(1)
                ),
            ],
            out_specs=pl.BlockSpec((row_total, piece_chunks * LANE), lambda i, s, k: (0, 0)),
        )
        results.append(
            pl.pallas_call(
                kernel,
                grid_spec=grid_spec,
                out_shape=jax.ShapeDtypeStruct((row_total, piece_chunks * LANE), jnp.bfloat16),
                compiler_params=pltpu.CompilerParams(vmem_limit_bytes=60 * 1024 * 1024),
            )(starts, k_sorted, rows_all, padded)
        )
    return results

def per_device(tensor, tensor_pattern, green, green_pattern):
    layer_count = lax.axis_size("layer")
    row_count = lax.axis_size("row")
    if layer_count != row_count:
        return cannon_per_device(tensor, tensor_pattern, green, green_pattern)
    ri_local, mu_local, nu_local = tensor.shape
    tile_rows, tile_cols = green_pattern.shape
    tensor_mask = jnp.repeat(tensor_pattern, BLK, axis=1).astype(jnp.bfloat16)
    masked = tensor * tensor_mask[None, :, :]
    own = masked.reshape(ri_local * mu_local, nu_local)
    layer_index = lax.axis_index("layer")
    col_count = lax.axis_size("col")
    blocks, block_row, block_col = compressed_tile(green, green_pattern)
    parts = tuple(green_to_layers(part, row_count) for part in (blocks, block_row, block_col))
    group = row_count * col_count
    me = lax.axis_index("row") * col_count + lax.axis_index("col")
    received = [parts]
    for shift in range(1, group):
        pairs = [(i, (i + shift) % group) for i in range(group)]
        received.append(tuple(lax.ppermute(part, ("row", "col"), pairs) for part in parts))
    blocks, block_row, block_col = (
        jnp.stack([got[k] for got in received]) for k in range(len(parts))
    )
    band = ((me - jnp.arange(group)) % group)[:, None]
    entry_rows = band * tile_rows + block_row
    entry_rows = entry_rows.reshape(-1)
    entry_cols = block_col.reshape(-1)
    entry_blocks = blocks.reshape(-1, BLK, BLK)
    pieces = []
    for start in range(0, ri_local * mu_local, ROW_CHUNK):
        rows = lax.all_gather(own[start : start + ROW_CHUNK], "layer", axis=1, tiled=True)
        (piece,) = block_sparse_product(
            rows, entry_blocks, entry_rows, entry_cols, tile_cols * BLK, 1
        )
        pieces.append(product_to_owners(piece, row_count))
    product = jnp.concatenate(pieces, axis=0)
    return product.reshape(ri_local, mu_local, tile_cols * BLK)

def solution(mesh):
    in_specs = (
        P("row", "col", "layer"),
        P("col", "layer"),
        P(("layer", "col"), "row"),
        P(("layer", "col"), "row"),
    )
    out_specs = P("layer", "col", "row")
    return jax.shard_map(
        per_device, mesh=mesh, in_specs=in_specs, out_specs=out_specs, check_vma=False
    )
```
